32 devices in a mesh: seq: 8 (over z, x), tp: 4 (over y, core).
Axes of the slice: x: 2, y: 2, z: 4, core: 2. Of those that a mesh axis runs over, the one named last changes fastest.
Arguments:
- hidden: bfloat16 [2048, 2048], P('seq', 'tp'), may hold values from -40 to 40
- new_queries: bfloat16 [2048, 2048], P('seq', 'tp'), may hold values from -9 to 9
- new_keys: bfloat16 [2048, 2048], P('seq', 'tp'), may hold values from -6 to 6
- new_values: bfloat16 [2048, 2048], P('seq', 'tp'), may hold values from -6 to 6
- cache_keys: bfloat16 [8, 4096, 2048], P('seq', None, 'tp'), may hold values from -6 to 6
- cache_values: bfloat16 [8, 4096, 2048], P('seq', None, 'tp'), may hold values from -6 to 6
- cache_lengths: int32 [8], replicated, may hold values from 1 to 4096, as said below
- out_proj: bfloat16 [2048, 2048], P('tp'), may hold values from -0.5 to 0.5
- moe_gain: float32 [2048], P('tp'), may hold values from 0.1 to 1.9
- expert_ids: int32 [2048, 8], P('seq'), may hold values from 0 to 15, all different within a row; in each aligned block of 256 rows (0 to 255, 256 to 511, ...) at most 192 rows name the same one
- route_weights: float32 [2048, 8], P('seq'), may hold values from 0.25 to 0.5
- expert_gate_up: bfloat16 [16, 2048, 2, 1024], P('seq', None, None, 'tp'), may hold values from -0.125 to 0.125
- expert_down: bfloat16 [16, 1024, 2048], P('seq', 'tp'), may hold values from -0.375 to 0.375
- next_gain: float32 [2048], P('tp'), may hold values from 0.1 to 1.9
- qkv_proj: bfloat16 [2048, 3, 2048], P(None, None, 'tp'), may hold values from -0.125 to 0.125
- query_gain: float32 [2048], P('tp'), may hold values from 0.1 to 1.9
- key_gain: float32 [2048], P('tp'), may hold values from 0.1 to 1.9
Outputs:
- layer_out: bfloat16 [2048, 2048], P('seq', 'tp')
- next_query: bfloat16 [2048, 2048], P('seq', 'tp')
- next_key: bfloat16 [2048, 2048], P('seq', 'tp')
- next_value: bfloat16 [2048, 2048], P('seq', 'tp')
The draws below stay inside these ranges and needn't reach their ends.
Inputs may be any that keep to these rules, and one draw needn't show every extreme that they name: Request r has cached positions 0 to cache_lengths[r] - 1; one request has 4096 of them and one has 1. `expert_ids`: each row names 8 different experts; among the 256 rows of one request no expert is named more than 192 times, and in some request one expert is named exactly 192 times.
All inputs are finite; a program needn't handle non-finite values.
Results may differ from the reference program's by a relative error of at most 0.017.
Values may be sent and summed in bfloat16 or wider, within the bound.
No kernel may reach another device: no remote copies, remote signals or barrier semaphores. Data moves between devices by JAX's collectives and lax.ppermute only.
A program may use at most 128 MiB of HBM per device.

```python
import math
import jax
import jax.numpy as jnp
import numpy as np
from jax import lax

D = 2048
HEADS = 16
HEAD_DIM = 128
FF = 1024
TOP = 8
NEW = 256
MAXC = 4096
REQS = 8
TOKENS = 2048
EXPERTS = 16
CAP = 192
N_SEQ = 8
N_TP = 4


def draw_hidden(key, part):
    base_key = jax.random.fold_in(key, 11)
    row_key = jax.random.fold_in(key, 12)
    columns = jnp.arange(D, dtype=jnp.float32) / D
    base = jax.random.truncated_normal(base_key, -6.0, 6.0, (TOKENS, D), jnp.float32)
    column_scale = 0.3 * jnp.exp(math.log(10.0) * columns)
    row_scale = jnp.exp(jax.random.uniform(row_key, (TOKENS, 1), jnp.float32, math.log(0.5), math.log(2.0)))
    return (base * column_scale[None, :] * row_scale).astype(jnp.bfloat16)


def draw_new_queries(key, part):
    values = 1.5 * jax.random.truncated_normal(jax.random.fold_in(key, 21), -6.0, 6.0, (TOKENS, D), jnp.float32)
    return values.astype(jnp.bfloat16)


def draw_new_keys(key, part):
    values = jax.random.truncated_normal(jax.random.fold_in(key, 23), -6.0, 6.0, (TOKENS, D), jnp.float32)
    return values.astype(jnp.bfloat16)


def draw_cache_keys(key, part):
    values = jax.random.truncated_normal(jax.random.fold_in(key, 24), -6.0, 6.0, (REQS, MAXC, D), jnp.float32)
    return values.astype(jnp.bfloat16)


def draw_cache_lengths(key, part):
    lengths = jax.random.randint(jax.random.fold_in(key, 31), (REQS,), 1, MAXC + 1)
    order = jax.random.permutation(jax.random.fold_in(key, 32), REQS)
    lengths = lengths.at[order[0]].set(MAXC)
    lengths = lengths.at[order[1]].set(1)
    return lengths.astype(jnp.int32)


def steps_of(rng, shape, shards, low, top_value):
    gain = 1.0
    for axis_at, blocks in shards:
        heights = jax.random.uniform(jax.random.fold_in(jax.random.fold_in(rng, 6), axis_at), (blocks,), jnp.float32, low / len(shards), top_value / len(shards))
        gain = gain * jnp.repeat(jnp.exp(heights), shape[axis_at] // blocks).reshape((-1,) + (1,) * (len(shape) - 1 - axis_at))
    return gain


def routed_block(own_key, own, number, rows, count, top, most, skew):
    ranking = jax.random.permutation(own_key, count)
    heavy_load, ordinary = load_shares(count, rows * top, most, skew, True), load_shares(count, rows * top, most, skew, False)
    places = jnp.arange(count)

    def named(sizes, offset_by):
        used = int((sizes > 0).sum())
        fixed = max(1, used // 4)
        shifted = fixed + (places - fixed + offset_by * (used - fixed)) % max(1, count - fixed)
        return jnp.zeros((count,), jnp.int32).at[ranking[jnp.where(places < fixed, places, shifted)]].set(jnp.asarray(sizes, jnp.int32))

    sizes = jnp.where(number % 4 == 0, named(heavy_load, number // 4), named(ordinary, number - number // 4 - 1))
    mixed = jax.random.permutation(jax.random.fold_in(own, 3), count)
    giver, taker = mixed[0:count // 2 * 2:2], mixed[1:count // 2 * 2:2]
    room = jnp.minimum(sizes[giver] - 1, most - sizes[taker]) // 2
    room = jnp.where((giver == ranking[0]) | (taker == ranking[0]) | (sizes[taker] == 0), 0, jnp.maximum(room, 0))
    shifted = jax.random.randint(jax.random.fold_in(own, 4), (count // 2,), 0, 1 << 20) % (room + 1)
    sizes = sizes.at[giver].add(-shifted).at[taker].add(shifted)
    items = jnp.searchsorted(jnp.cumsum(sizes), jnp.arange(rows * top), side="right").astype(jnp.int32)
    grid = items.reshape(top, rows).T
    grid = grid[jax.random.permutation(jax.random.fold_in(own, 1), rows)]
    offset_by = jax.random.randint(jax.random.fold_in(own, 2), (rows, 1), 0, top)
    return jnp.take_along_axis(grid, (jnp.arange(top)[None, :] + offset_by) % top, axis=1)


def load_shares(amount, total, limit, lean, full):
    weights = [(1 << 20) // math.isqrt(rank ** lean) + 1 for rank in range(1, amount + 1)]
    largest = limit if full else min(limit, max(-(-total // amount), total * weights[0] // sum(weights)))
    least = 1 if total - largest >= amount - 1 else 0
    counts, surplus = [largest] + [least] * (amount - 1), total - largest - least * (amount - 1)
    while surplus > 0:
        candidates = [i for i in range(1, amount) if counts[i] < largest] or [i for i in range(1, amount) if counts[i] < limit]
        whole, remaining = sum([weights[i] for i in candidates]), surplus
        for i in candidates:
            extra = min(limit - counts[i], max(1, remaining * weights[i] // whole), surplus)
            counts[i] = counts[i] + extra
            surplus = surplus - extra
    return np.array(counts)


def centred(rng, dims, width, reach, cuts=(), kind=jnp.bfloat16):
    gain = steps_of(rng, dims, cuts, -0.22, 0.18) if cuts else 1.0
    values = jax.random.normal(rng, dims, jnp.float32) * width * gain
    return jnp.minimum(jnp.maximum(values, -reach), reach).astype(kind)


def setup_inputs(seed: int = 0) -> dict:
    key_of = jax.random.split(jax.random.key(seed), 18)
    hidden = draw_hidden(jax.random.fold_in(key_of[17], 71), 0)
    new_queries = draw_new_queries(jax.random.fold_in(key_of[17], 71), 0)
    new_keys = draw_new_keys(jax.random.fold_in(key_of[17], 71), 0)
    new_values = centred(key_of[3], (TOKENS, D), 1.0, 6.0, ((0, 8), (1, 4)))
    cache_keys = draw_cache_keys(jax.random.fold_in(key_of[17], 71), 0)
    cache_values = centred(key_of[5], (REQS, MAXC, D), 1.0, 6.0, ((0, 8), (2, 4)))
    cache_lengths = draw_cache_lengths(jax.random.fold_in(key_of[17], 71), 0)
    out_proj = centred(key_of[7], (D, D), (D // 16) ** -0.5, 0.5, ((0, 4),))
    moe_gain = jnp.clip(1.0 + 0.18 * jax.random.normal(key_of[8], (D,), jnp.float32), 0.1, 1.9)
    expert_ids_keys = jax.random.split(jax.random.fold_in(key_of[9], 1), TOKENS // NEW)
    expert_ids_turns = jax.random.permutation(jax.random.fold_in(key_of[9], 3), TOKENS // NEW)
    expert_ids = jax.vmap(lambda own, number: routed_block(jax.random.fold_in(key_of[9], 2), own, number, NEW, EXPERTS, TOP, CAP, 2))(expert_ids_keys, expert_ids_turns).reshape((TOKENS, TOP))
    route_weights = jnp.clip(0.25 + 0.25 * jax.random.uniform(key_of[10], (TOKENS, TOP), jnp.float32) ** steps_of(key_of[10], (TOKENS, TOP), ((0, 8),), -0.2, 0.2), 0.25, 0.5)
    expert_gate_up = centred(key_of[11], (EXPERTS, D, 2, FF), D ** -0.5, 0.125, ((0, 8), (3, 4)))
    expert_down = centred(key_of[12], (EXPERTS, FF, D), (FF // 4) ** -0.5, 0.375, ((0, 8), (1, 4)))
    next_gain = jnp.clip(1.0 + 0.18 * jax.random.normal(key_of[13], (D,), jnp.float32), 0.1, 1.9)
    qkv_proj = centred(key_of[14], (D, 3, D), D ** -0.5, 0.125, ((2, 4),))
    query_gain = jnp.clip(1.0 + 0.18 * jax.random.normal(key_of[15], (D,), jnp.float32), 0.1, 1.9)
    key_gain = jnp.clip(1.0 + 0.18 * jax.random.normal(key_of[16], (D,), jnp.float32), 0.1, 1.9)
    return dict(hidden=hidden, new_queries=new_queries, new_keys=new_keys, new_values=new_values, cache_keys=cache_keys, cache_values=cache_values, cache_lengths=cache_lengths, out_proj=out_proj, moe_gain=moe_gain, expert_ids=expert_ids, route_weights=route_weights, expert_gate_up=expert_gate_up, expert_down=expert_down, next_gain=next_gain, qkv_proj=qkv_proj, query_gain=query_gain, key_gain=key_gain)


epsilon = 1e-05

def attend_request(inputs):
    queries, cache_key_rows, cache_value_rows, fresh_keys, fresh_values, length = inputs
    key_rows = jnp.concatenate([cache_key_rows, fresh_keys], 0).astype(jnp.float32).reshape(MAXC + NEW, HEADS, HEAD_DIM)
    value_rows = jnp.concatenate([cache_value_rows, fresh_values], 0).astype(jnp.float32).reshape(MAXC + NEW, HEADS, HEAD_DIM)
    query_rows = queries.astype(jnp.float32).reshape(NEW, HEADS, HEAD_DIM)
    scores = jnp.einsum('the,che->htc', query_rows, key_rows) / math.sqrt(HEAD_DIM)
    cached = jnp.arange(MAXC, dtype=jnp.int32) < length
    offsets = jnp.arange(NEW, dtype=jnp.int32)
    allowed = jnp.concatenate([jnp.broadcast_to(cached[None, :], (NEW, MAXC)), offsets[None, :] <= offsets[:, None]], 1)
    scores = jnp.where(allowed[None], scores, -1e+30)
    row_max = lax.optimization_barrier(jnp.max(scores, axis=2, keepdims=True))
    weights = jnp.where(allowed[None], jnp.exp(scores - row_max), 0.0)
    row_total = lax.optimization_barrier(jnp.sum(weights, axis=2))
    rounded = lax.optimization_barrier(weights.astype(jnp.bfloat16)).astype(jnp.float32)
    mixed = jnp.einsum('htc,che->the', rounded, value_rows)
    mixed = mixed / jnp.transpose(row_total)[:, :, None]
    return mixed.reshape(NEW, D).astype(jnp.bfloat16)

def run_expert(inputs):
    rows_in, gate_up, down_rows = inputs
    projected = jnp.dot(rows_in, gate_up.reshape(D, 2 * FF), preferred_element_type=jnp.float32)
    activated = (jax.nn.silu(projected[:, :FF]) * projected[:, FF:]).astype(jnp.bfloat16)
    quarter = FF // N_TP
    pieces = jnp.einsum('rqf,qfd->qrd', activated.astype(jnp.float32).reshape(-1, N_TP, quarter), down_rows.astype(jnp.float32).reshape(N_TP, quarter, D))
    pieces = lax.optimization_barrier(pieces.astype(jnp.bfloat16)).astype(jnp.float32)
    return lax.optimization_barrier(jnp.sum(pieces, axis=0)).astype(jnp.bfloat16)

def reference(hidden, new_queries, new_keys, new_values, cache_keys, cache_values, cache_lengths, out_proj, moe_gain, expert_ids, route_weights, expert_gate_up, expert_down, next_gain, qkv_proj, query_gain, key_gain):
    attended = lax.map(attend_request, (new_queries.reshape(REQS, NEW, D), cache_keys, cache_values, new_keys.reshape(REQS, NEW, D), new_values.reshape(REQS, NEW, D), cache_lengths))
    attended = attended.reshape(TOKENS, D)
    residual = hidden.astype(jnp.float32) + jnp.dot(attended, out_proj, preferred_element_type=jnp.float32)
    moe_in = (residual * lax.rsqrt(lax.optimization_barrier(jnp.mean(residual * residual, axis=1, keepdims=True)) + epsilon) * moe_gain).astype(jnp.bfloat16)
    flat_ids = expert_ids.reshape(REQS, NEW * TOP)
    onehot = (flat_ids[:, :, None] == jnp.arange(EXPERTS, dtype=jnp.int32)[None, None, :]).astype(jnp.int32)
    ranks = lax.optimization_barrier(jnp.sum((jnp.cumsum(onehot, axis=1) - onehot) * onehot, axis=2))
    source = jnp.arange(REQS, dtype=jnp.int32)[:, None]
    target = ((flat_ids * N_SEQ + source) * CAP + ranks).reshape(TOKENS, TOP).astype(jnp.int32)
    buffer = jnp.zeros((EXPERTS * N_SEQ * CAP, D), jnp.bfloat16).at[target.reshape(-1)].set(jnp.repeat(moe_in, TOP, axis=0))
    expert_rows = lax.map(run_expert, (buffer.reshape(EXPERTS, N_SEQ * CAP, D), expert_gate_up, expert_down))
    picked = jnp.take(expert_rows.reshape(EXPERTS * N_SEQ * CAP, D), target, axis=0)
    routed = residual + lax.optimization_barrier(jnp.sum(route_weights[:, :, None] * picked.astype(jnp.float32), axis=1))
    scaled = (routed * next_gain).astype(jnp.bfloat16)
    mixed = jnp.dot(scaled, qkv_proj.reshape(D, 3 * D), preferred_element_type=jnp.float32).reshape(TOKENS, 3, D)
    x_scale = lax.rsqrt(lax.optimization_barrier(jnp.mean(routed * routed, axis=1, keepdims=True)) + epsilon)
    query_pre = mixed[:, 0] * x_scale
    key_pre = mixed[:, 1] * x_scale
    next_query = (query_pre * lax.rsqrt(lax.optimization_barrier(jnp.mean(query_pre * query_pre, axis=1, keepdims=True)) + epsilon) * query_gain).astype(jnp.bfloat16)
    next_key = (key_pre * lax.rsqrt(lax.optimization_barrier(jnp.mean(key_pre * key_pre, axis=1, keepdims=True)) + epsilon) * key_gain).astype(jnp.bfloat16)
    next_value = (mixed[:, 2] * x_scale).astype(jnp.bfloat16)
    return (routed.astype(jnp.bfloat16), next_query, next_key, next_value)
```

```python
import math

import jax
import jax.numpy as jnp
from jax import lax
from jax.sharding import PartitionSpec as P

D = 2048
HEAD_DIM = 128
TOP = 8
NEW = 256


epsilon = 1e-05


def softmax_parts(queries, key_rows, values, allowed):
    scores = jnp.einsum(
        "bthe,bche->bhtc", queries, key_rows, preferred_element_type=jnp.float32
    ) / math.sqrt(HEAD_DIM)
    scores = jnp.where(allowed[:, None], scores, -1e30)
    row_max = jnp.max(scores, axis=3)
    weights = jnp.where(allowed[:, None], jnp.exp(scores - row_max[..., None]), 0.0)
    row_total = jnp.sum(weights, axis=3)
    partial_out = jnp.einsum(
        "bhtc,bche->bthe", weights.astype(jnp.bfloat16), values, preferred_element_type=jnp.float32
    )
    return (partial_out, jnp.swapaxes(row_max, 1, 2), jnp.swapaxes(row_total, 1, 2))


def combine_parts(first, second):
    out_a, max_a, total_a = first
    out_b, max_b, total_b = second
    joint = jnp.maximum(max_a, max_b)
    factor_a = jnp.exp(max_a - joint)
    factor_b = jnp.exp(max_b - joint)
    return (
        out_a * factor_a[..., None] + out_b * factor_b[..., None],
        joint,
        total_a * factor_a + total_b * factor_b,
    )


def merge_parts(pieces, maxima, totals):
    overall = jnp.max(maxima, axis=0)
    factor = jnp.exp(maxima - overall[None])
    denominator = jnp.sum(totals * factor, axis=0)
    merged = jnp.sum(pieces * factor[..., None], axis=0)
    return merged / denominator[..., None]


def dense_experts(moe_in, expert_ids, route_weights, expert_gate_up, expert_down, here, experts_all):
    local_experts = expert_gate_up.shape[0]
    hidden_quarter = expert_gate_up.shape[3]
    gate_w = jnp.sum(
        route_weights[:, :, None]
        * (expert_ids[:, :, None] == jnp.arange(experts_all, dtype=jnp.int32)[None, None, :]),
        axis=1,
    )
    gate_all = lax.all_gather(gate_w, "seq", axis=0, tiled=True)
    gate_local = lax.dynamic_slice_in_dim(gate_all, here * local_experts, local_experts, axis=1)
    rows = lax.all_gather(lax.all_gather(moe_in, "seq", axis=0, tiled=True), "tp", axis=1, tiled=True)
    gate_up = expert_gate_up.reshape(local_experts, D, 2 * hidden_quarter)
    projected = jnp.einsum("td,edf->etf", rows, gate_up, preferred_element_type=jnp.float32)
    activated = jax.nn.silu(projected[..., :hidden_quarter]) * projected[..., hidden_quarter:]
    activated = activated.astype(jnp.bfloat16).astype(jnp.float32)
    weighted = (activated * jnp.transpose(gate_local)[:, :, None]).astype(jnp.bfloat16)
    weighted = jnp.transpose(weighted, (1, 0, 2)).reshape(rows.shape[0], local_experts * hidden_quarter)
    down_rows = expert_down.reshape(local_experts * hidden_quarter, D)
    partial = jnp.dot(weighted, down_rows, preferred_element_type=jnp.float32).astype(jnp.bfloat16)
    partial = lax.psum_scatter(partial, "tp", scatter_dimension=1, tiled=True)
    partial = lax.psum_scatter(partial, "seq", scatter_dimension=0, tiled=True)
    return partial.astype(jnp.float32)


def dispatch_experts(moe_in, expert_ids, route_weights, expert_gate_up, expert_down, experts_all, capacity):
    quarter = moe_in.shape[1]
    local_experts = expert_gate_up.shape[0]
    flat_ids = expert_ids.reshape(NEW * TOP)
    onehot = (flat_ids[:, None] == jnp.arange(experts_all, dtype=jnp.int32)[None, :]).astype(
        jnp.int32
    )
    ranks = jnp.sum((jnp.cumsum(onehot, axis=0) - onehot) * onehot, axis=1)
    target = (flat_ids * capacity + ranks).reshape(NEW, TOP)
    slot_ids = jnp.arange(experts_all * capacity, dtype=jnp.int32)
    selector = jnp.sum(
        (target[None, :, :] == slot_ids[:, None, None]).astype(jnp.int32), axis=2
    ).astype(jnp.bfloat16)
    send_rows = jnp.dot(selector, moe_in, preferred_element_type=jnp.float32).astype(jnp.bfloat16)
    send_rows = send_rows.reshape(experts_all, capacity, quarter)
    received = lax.all_to_all(send_rows, "seq", split_axis=0, concat_axis=1, tiled=True)
    hidden_quarter = expert_gate_up.shape[3]
    gate_up_local = expert_gate_up.reshape(local_experts, D, 2 * hidden_quarter)
    weight_rows = gate_up_local
    projected = jnp.einsum(
        "erd,edf->erf",
        lax.all_gather(received, "tp", axis=2, tiled=True),
        weight_rows,
        preferred_element_type=jnp.float32,
    )
    activated = (
        jax.nn.silu(projected[..., :hidden_quarter]) * projected[..., hidden_quarter:]
    ).astype(jnp.bfloat16)
    down_terms = jnp.einsum(
        "erf,efd->erd", activated, expert_down, preferred_element_type=jnp.float32
    )
    expert_result = lax.psum_scatter(
        down_terms.astype(jnp.bfloat16), "tp", scatter_dimension=2, tiled=True
    )
    returned = lax.all_to_all(
        expert_result, "seq", split_axis=1, concat_axis=0, tiled=True
    ).reshape(experts_all * capacity, quarter)
    picked = jnp.take(returned, target, axis=0)
    return jnp.sum(route_weights[:, :, None] * picked.astype(jnp.float32), axis=1)


def body(
    hidden,
    new_queries,
    new_keys,
    new_values,
    cache_keys,
    cache_values,
    cache_lengths,
    out_proj,
    moe_gain,
    expert_ids,
    route_weights,
    expert_gate_up,
    expert_down,
    next_gain,
    qkv_proj,
    query_gain,
    key_gain,
):
    seq_count = lax.axis_size("seq")
    here = lax.axis_index("seq")
    local_width = new_queries.shape[1]
    local_heads = local_width // HEAD_DIM
    quarter = hidden.shape[1]
    own_queries = new_queries.reshape(1, NEW, local_heads, HEAD_DIM)
    own_keys = new_keys.reshape(1, NEW, local_heads, HEAD_DIM)
    own_values = new_values.reshape(1, NEW, local_heads, HEAD_DIM)
    offsets = jnp.arange(NEW, dtype=jnp.int32)
    causal = (offsets[None, :] <= offsets[:, None])[None]
    own_out, own_max, own_total = softmax_parts(own_queries, own_keys, own_values, causal)
    span = cache_keys.shape[1]
    block = min(512, span)
    my_length = lax.dynamic_index_in_dim(cache_lengths, here, 0, keepdims=False)
    block_count = (my_length + block - 1) // block
    key_blocks = cache_keys.reshape(span, local_heads, HEAD_DIM)
    value_blocks = cache_values.reshape(span, local_heads, HEAD_DIM)

    def cache_block(index, carry):
        begin = index * block
        keys_here = lax.dynamic_slice_in_dim(key_blocks, begin, block, 0)[None]
        values_here = lax.dynamic_slice_in_dim(value_blocks, begin, block, 0)[None]
        positions = begin + jnp.arange(block, dtype=jnp.int32)
        allowed = jnp.broadcast_to((positions < my_length)[None, None, :], (1, NEW, block))
        return combine_parts(carry, softmax_parts(own_queries, keys_here, values_here, allowed))

    start_parts = (
        jnp.zeros((1, NEW, local_heads, HEAD_DIM), jnp.float32),
        jnp.full((1, NEW, local_heads), -1e30, jnp.float32),
        jnp.zeros((1, NEW, local_heads), jnp.float32),
    )
    pieces, maxima, totals = lax.fori_loop(0, block_count, cache_block, start_parts)
    attended = merge_parts(
        jnp.concatenate([own_out, pieces], 0),
        jnp.concatenate([own_max, maxima], 0),
        jnp.concatenate([own_total, totals], 0),
    )
    attended = attended.reshape(NEW, local_width).astype(jnp.bfloat16)
    attn_term = jnp.dot(attended, out_proj, preferred_element_type=jnp.float32)
    residual = hidden.astype(jnp.float32) + lax.psum_scatter(
        attn_term.astype(jnp.bfloat16), "tp", scatter_dimension=1, tiled=True
    ).astype(jnp.float32)
    square_total = lax.psum(jnp.sum(residual * residual, axis=1), "tp")
    moe_in = (residual * lax.rsqrt(square_total / D + epsilon)[:, None] * moe_gain[None, :]).astype(
        jnp.bfloat16
    )
    local_experts = expert_gate_up.shape[0]
    experts_all = local_experts * seq_count
    capacity = max(2, 3 * NEW * TOP // (2 * experts_all))
    if NEW <= 2 * capacity:
        moe_term = dense_experts(
            moe_in, expert_ids, route_weights, expert_gate_up, expert_down, here, experts_all
        )
    else:
        moe_term = dispatch_experts(
            moe_in, expert_ids, route_weights, expert_gate_up, expert_down, experts_all, capacity
        )
    routed = residual + moe_term
    layer_out = routed.astype(jnp.bfloat16)
    scaled = (routed * next_gain[None, :]).astype(jnp.bfloat16)
    qkv_local = qkv_proj.reshape(D, 3 * local_width)
    weight_rows = qkv_local
    mixed = jnp.dot(
        lax.all_gather(scaled, "tp", axis=1, tiled=True),
        weight_rows,
        preferred_element_type=jnp.float32,
    )
    mixed = mixed.reshape(NEW, 3, local_width)
    squares_routed = jnp.sum(routed * routed, axis=1)
    routed_total, query_raw, key_raw = lax.psum(
        (
            squares_routed,
            jnp.sum(mixed[:, 0] * mixed[:, 0], axis=1),
            jnp.sum(mixed[:, 1] * mixed[:, 1], axis=1),
        ),
        "tp",
    )
    x_scale = lax.rsqrt(routed_total / D + epsilon)
    query_pre = mixed[:, 0] * x_scale[:, None]
    key_pre = mixed[:, 1] * x_scale[:, None]
    query_total = query_raw * x_scale * x_scale
    key_total = key_raw * x_scale * x_scale
    next_query = (
        query_pre * lax.rsqrt(query_total / D + epsilon)[:, None] * query_gain[None, :]
    ).astype(jnp.bfloat16)
    next_key = (key_pre * lax.rsqrt(key_total / D + epsilon)[:, None] * key_gain[None, :]).astype(
        jnp.bfloat16
    )
    next_value = (mixed[:, 2] * x_scale[:, None]).astype(jnp.bfloat16)
    return (layer_out, next_query, next_key, next_value)


def solution(mesh):
    return jax.shard_map(
        body,
        mesh=mesh,
        in_specs=(
            P("seq", "tp"),
            P("seq", "tp"),
            P("seq", "tp"),
            P("seq", "tp"),
            P("seq", None, "tp"),
            P("seq", None, "tp"),
            P(),
            P("tp", None),
            P("tp"),
            P("seq", None),
            P("seq", None),
            P("seq", None, None, "tp"),
            P("seq", "tp", None),
            P("tp"),
            P(None, None, "tp"),
            P("tp"),
            P("tp"),
        ),
        out_specs=(P("seq", "tp"), P("seq", "tp"), P("seq", "tp"), P("seq", "tp")),
        check_vma=False,
    )
```

```python
import math

import jax
import jax.numpy as jnp
from jax import lax
from jax.sharding import PartitionSpec as P

D = 2048
HEAD_DIM = 128
TOP = 8
NEW = 256


epsilon = 1e-05


def softmax_parts(queries, key_rows, values, allowed):
    scores = jnp.einsum(
        "bthe,bche->bhtc", queries, key_rows, preferred_element_type=jnp.float32
    ) / math.sqrt(HEAD_DIM)
    scores = jnp.where(allowed[:, None], scores, -1e30)
    row_max = jnp.max(scores, axis=3)
    weights = jnp.where(allowed[:, None], jnp.exp(scores - row_max[..., None]), 0.0)
    row_total = jnp.sum(weights, axis=3)
    partial_out = jnp.einsum(
        "bhtc,bche->bthe", weights.astype(jnp.bfloat16), values, preferred_element_type=jnp.float32
    )
    return (partial_out, jnp.swapaxes(row_max, 1, 2), jnp.swapaxes(row_total, 1, 2))


def combine_parts(first, second):
    out_a, max_a, total_a = first
    out_b, max_b, total_b = second
    joint = jnp.maximum(max_a, max_b)
    factor_a = jnp.exp(max_a - joint)
    factor_b = jnp.exp(max_b - joint)
    return (
        out_a * factor_a[..., None] + out_b * factor_b[..., None],
        joint,
        total_a * factor_a + total_b * factor_b,
    )


def merge_parts(pieces, maxima, totals):
    overall = jnp.max(maxima, axis=0)
    factor = jnp.exp(maxima - overall[None])
    denominator = jnp.sum(totals * factor, axis=0)
    merged = jnp.sum(pieces * factor[..., None], axis=0)
    return merged / denominator[..., None]


def dense_experts(moe_in, expert_ids, route_weights, expert_gate_up, down_full, here, experts_all):
    local_experts = expert_gate_up.shape[0]
    hidden_quarter = expert_gate_up.shape[3]
    tokens, quarter = moe_in.shape
    seq_count = experts_all // local_experts
    gate_w = jnp.sum(
        route_weights[:, :, None]
        * (expert_ids[:, :, None] == jnp.arange(experts_all, dtype=jnp.int32)[None, None, :]),
        axis=1,
    )
    gate_hi = gate_w.astype(jnp.bfloat16)
    gate_lo = (gate_w - gate_hi.astype(jnp.float32)).astype(jnp.bfloat16)
    info = jnp.concatenate([gate_hi, gate_lo], axis=1).reshape(-1, quarter)
    info_rows = info.shape[0]
    packed = jnp.concatenate([moe_in, info], axis=0)
    gathered = lax.all_gather(packed, "seq", axis=0, tiled=False)
    rows_q = gathered[:, :tokens].reshape(seq_count * tokens, quarter)
    info_all = gathered[:, tokens:].reshape(seq_count * tokens, 2, experts_all).astype(jnp.float32)
    gate_all = info_all[:, 0] + info_all[:, 1]
    gate_local = lax.dynamic_slice_in_dim(gate_all, here * local_experts, local_experts, axis=1)
    rows = lax.all_gather(rows_q, "tp", axis=1, tiled=True)
    gate_up = expert_gate_up.reshape(local_experts, D, 2 * hidden_quarter)
    projected = jnp.einsum("td,edf->etf", rows, gate_up, preferred_element_type=jnp.float32)
    activated = jax.nn.silu(projected[..., :hidden_quarter]) * projected[..., hidden_quarter:]
    activated = activated.astype(jnp.bfloat16).astype(jnp.float32)
    weighted = (activated * jnp.transpose(gate_local)[:, :, None]).astype(jnp.bfloat16)
    weighted = lax.all_gather(weighted, "tp", axis=2, tiled=True)
    weighted = jnp.transpose(weighted, (1, 0, 2)).reshape(rows.shape[0], -1)
    partial = jnp.dot(weighted, down_full, preferred_element_type=jnp.float32).astype(jnp.bfloat16)
    partial = lax.psum_scatter(partial, "seq", scatter_dimension=0, tiled=True)
    return partial.astype(jnp.float32)


def dispatch_experts(moe_in, expert_ids, route_weights, expert_gate_up, expert_down, experts_all, capacity):
    quarter = moe_in.shape[1]
    local_experts = expert_gate_up.shape[0]
    flat_ids = expert_ids.reshape(NEW * TOP)
    onehot = (flat_ids[:, None] == jnp.arange(experts_all, dtype=jnp.int32)[None, :]).astype(
        jnp.int32
    )
    ranks = jnp.sum((jnp.cumsum(onehot, axis=0) - onehot) * onehot, axis=1)
    target = (flat_ids * capacity + ranks).reshape(NEW, TOP)
    slot_ids = jnp.arange(experts_all * capacity, dtype=jnp.int32)
    selector = jnp.sum(
        (target[None, :, :] == slot_ids[:, None, None]).astype(jnp.int32), axis=2
    ).astype(jnp.bfloat16)
    send_rows = jnp.dot(selector, moe_in, preferred_element_type=jnp.float32).astype(jnp.bfloat16)
    send_rows = send_rows.reshape(experts_all, capacity, quarter)
    received = lax.all_to_all(send_rows, "seq", split_axis=0, concat_axis=1, tiled=True)
    hidden_quarter = expert_gate_up.shape[3]
    gate_up_local = expert_gate_up.reshape(local_experts, D, 2 * hidden_quarter)
    weight_rows = gate_up_local
    projected = jnp.einsum(
        "erd,edf->erf",
        lax.all_gather(received, "tp", axis=2, tiled=True),
        weight_rows,
        preferred_element_type=jnp.float32,
    )
    activated = (
        jax.nn.silu(projected[..., :hidden_quarter]) * projected[..., hidden_quarter:]
    ).astype(jnp.bfloat16)
    down_terms = jnp.einsum(
        "erf,efd->erd", activated, expert_down, preferred_element_type=jnp.float32
    )
    expert_result = lax.psum_scatter(
        down_terms.astype(jnp.bfloat16), "tp", scatter_dimension=2, tiled=True
    )
    returned = lax.all_to_all(
        expert_result, "seq", split_axis=1, concat_axis=0, tiled=True
    ).reshape(experts_all * capacity, quarter)
    picked = jnp.take(returned, target, axis=0)
    return jnp.sum(route_weights[:, :, None] * picked.astype(jnp.float32), axis=1)


def body(
    hidden,
    new_queries,
    new_keys,
    new_values,
    cache_keys,
    cache_values,
    cache_lengths,
    out_proj,
    moe_gain,
    expert_ids,
    route_weights,
    expert_gate_up,
    expert_down,
    next_gain,
    qkv_proj,
    query_gain,
    key_gain,
):
    seq_count = lax.axis_size("seq")
    here = lax.axis_index("seq")
    local_experts = expert_gate_up.shape[0]
    experts_all = local_experts * seq_count
    capacity = max(2, 3 * NEW * TOP // (2 * experts_all))
    dense = NEW <= 2 * capacity
    if dense:
        tp_here = lax.axis_index("tp")
        quarter_width = hidden.shape[1]
        down_full = lax.all_gather(expert_down, "tp", axis=1, tiled=True)
        down_full = lax.dynamic_slice_in_dim(down_full, tp_here * quarter_width, quarter_width, axis=2)
        down_full = down_full.reshape(-1, quarter_width)
    local_width = new_queries.shape[1]
    local_heads = local_width // HEAD_DIM
    quarter = hidden.shape[1]
    own_queries = new_queries.reshape(1, NEW, local_heads, HEAD_DIM)
    own_keys = new_keys.reshape(1, NEW, local_heads, HEAD_DIM)
    own_values = new_values.reshape(1, NEW, local_heads, HEAD_DIM)
    offsets = jnp.arange(NEW, dtype=jnp.int32)
    causal = (offsets[None, :] <= offsets[:, None])[None]
    own_out, own_max, own_total = softmax_parts(own_queries, own_keys, own_values, causal)
    span = cache_keys.shape[1]
    block = min(512, span)
    my_length = lax.dynamic_index_in_dim(cache_lengths, here, 0, keepdims=False)
    block_count = (my_length + block - 1) // block
    key_blocks = cache_keys.reshape(span, local_heads, HEAD_DIM)
    value_blocks = cache_values.reshape(span, local_heads, HEAD_DIM)

    def cache_block(index, carry):
        begin = index * block
        keys_here = lax.dynamic_slice_in_dim(key_blocks, begin, block, 0)[None]
        values_here = lax.dynamic_slice_in_dim(value_blocks, begin, block, 0)[None]
        positions = begin + jnp.arange(block, dtype=jnp.int32)
        allowed = jnp.broadcast_to((positions < my_length)[None, None, :], (1, NEW, block))
        return combine_parts(carry, softmax_parts(own_queries, keys_here, values_here, allowed))

    start_parts = (
        jnp.zeros((1, NEW, local_heads, HEAD_DIM), jnp.float32),
        jnp.full((1, NEW, local_heads), -1e30, jnp.float32),
        jnp.zeros((1, NEW, local_heads), jnp.float32),
    )
    pieces, maxima, totals = lax.fori_loop(0, block_count, cache_block, start_parts)
    attended = merge_parts(
        jnp.concatenate([own_out, pieces], 0),
        jnp.concatenate([own_max, maxima], 0),
        jnp.concatenate([own_total, totals], 0),
    )
    attended = attended.reshape(NEW, local_width).astype(jnp.bfloat16)
    attn_term = jnp.dot(attended, out_proj, preferred_element_type=jnp.float32)
    residual = hidden.astype(jnp.float32) + lax.psum_scatter(
        attn_term.astype(jnp.bfloat16), "tp", scatter_dimension=1, tiled=True
    ).astype(jnp.float32)
    square_total = lax.psum(jnp.sum(residual * residual, axis=1), "tp")
    moe_in = (residual * lax.rsqrt(square_total / D + epsilon)[:, None] * moe_gain[None, :]).astype(
        jnp.bfloat16
    )
    if dense:
        moe_term = dense_experts(
            moe_in, expert_ids, route_weights, expert_gate_up, down_full, here, experts_all
        )
    else:
        moe_term = dispatch_experts(
            moe_in, expert_ids, route_weights, expert_gate_up, expert_down, experts_all, capacity
        )
    routed = residual + moe_term
    layer_out = routed.astype(jnp.bfloat16)
    scaled = (routed * next_gain[None, :]).astype(jnp.bfloat16)
    qkv_local = qkv_proj.reshape(D, 3 * local_width)
    weight_rows = qkv_local
    mixed = jnp.dot(
        lax.all_gather(scaled, "tp", axis=1, tiled=True),
        weight_rows,
        preferred_element_type=jnp.float32,
    )
    mixed = mixed.reshape(NEW, 3, local_width)
    squares_routed = jnp.sum(routed * routed, axis=1)
    routed_total, query_raw, key_raw = lax.psum(
        (
            squares_routed,
            jnp.sum(mixed[:, 0] * mixed[:, 0], axis=1),
            jnp.sum(mixed[:, 1] * mixed[:, 1], axis=1),
        ),
        "tp",
    )
    x_scale = lax.rsqrt(routed_total / D + epsilon)
    query_pre = mixed[:, 0] * x_scale[:, None]
    key_pre = mixed[:, 1] * x_scale[:, None]
    query_total = query_raw * x_scale * x_scale
    key_total = key_raw * x_scale * x_scale
    next_query = (
        query_pre * lax.rsqrt(query_total / D + epsilon)[:, None] * query_gain[None, :]
    ).astype(jnp.bfloat16)
    next_key = (key_pre * lax.rsqrt(key_total / D + epsilon)[:, None] * key_gain[None, :]).astype(
        jnp.bfloat16
    )
    next_value = (mixed[:, 2] * x_scale[:, None]).astype(jnp.bfloat16)
    return (layer_out, next_query, next_key, next_value)


def solution(mesh):
    return jax.shard_map(
        body,
        mesh=mesh,
        in_specs=(
            P("seq", "tp"),
            P("seq", "tp"),
            P("seq", "tp"),
            P("seq", "tp"),
            P("seq", None, "tp"),
            P("seq", None, "tp"),
            P(),
            P("tp", None),
            P("tp"),
            P("seq", None),
            P("seq", None),
            P("seq", None, None, "tp"),
            P("seq", "tp", None),
            P("tp"),
            P(None, None, "tp"),
            P("tp"),
            P("tp"),
        ),
        out_specs=(P("seq", "tp"), P("seq", "tp"), P("seq", "tp"), P("seq", "tp")),
        check_vma=False,
    )
```

```python
import math

import jax
import jax.numpy as jnp
from jax import lax
from jax.sharding import PartitionSpec as P

D = 2048
HEAD_DIM = 128
TOP = 8
NEW = 256


epsilon = 1e-05


def softmax_parts(queries, key_rows, values, allowed):
    scores = jnp.einsum(
        "bthe,bche->bhtc", queries, key_rows, preferred_element_type=jnp.float32
    ) / math.sqrt(HEAD_DIM)
    scores = jnp.where(allowed[:, None], scores, -1e30)
    row_max = jnp.max(scores, axis=3)
    weights = jnp.where(allowed[:, None], jnp.exp(scores - row_max[..., None]), 0.0)
    row_total = jnp.sum(weights, axis=3)
    partial_out = jnp.einsum(
        "bhtc,bche->bthe", weights.astype(jnp.bfloat16), values, preferred_element_type=jnp.float32
    )
    return (partial_out, jnp.swapaxes(row_max, 1, 2), jnp.swapaxes(row_total, 1, 2))


def combine_parts(first, second):
    out_a, max_a, total_a = first
    out_b, max_b, total_b = second
    joint = jnp.maximum(max_a, max_b)
    factor_a = jnp.exp(max_a - joint)
    factor_b = jnp.exp(max_b - joint)
    return (
        out_a * factor_a[..., None] + out_b * factor_b[..., None],
        joint,
        total_a * factor_a + total_b * factor_b,
    )


def merge_parts(pieces, maxima, totals):
    overall = jnp.max(maxima, axis=0)
    factor = jnp.exp(maxima - overall[None])
    denominator = jnp.sum(totals * factor, axis=0)
    merged = jnp.sum(pieces * factor[..., None], axis=0)
    return merged / denominator[..., None]


def dense_experts(moe_in, expert_ids, route_weights, expert_gate_up, down_full, here, experts_all):
    local_experts = expert_gate_up.shape[0]
    hidden_quarter = expert_gate_up.shape[3]
    tokens, quarter = moe_in.shape
    seq_count = experts_all // local_experts
    gate_w = jnp.sum(
        route_weights[:, :, None]
        * (expert_ids[:, :, None] == jnp.arange(experts_all, dtype=jnp.int32)[None, None, :]),
        axis=1,
    )
    gate_hi = gate_w.astype(jnp.bfloat16)
    gate_lo = (gate_w - gate_hi.astype(jnp.float32)).astype(jnp.bfloat16)
    info = jnp.concatenate([gate_hi, gate_lo], axis=1).reshape(-1, quarter)
    info_rows = info.shape[0]
    packed = jnp.concatenate([moe_in, info], axis=0)
    gathered = lax.all_gather(packed, "seq", axis=0, tiled=False)
    rows_q = gathered[:, :tokens].reshape(seq_count * tokens, quarter)
    info_all = gathered[:, tokens:].reshape(seq_count * tokens, 2, experts_all).astype(jnp.float32)
    gate_all = info_all[:, 0] + info_all[:, 1]
    gate_local = lax.dynamic_slice_in_dim(gate_all, here * local_experts, local_experts, axis=1)
    rows = lax.all_gather(rows_q, "tp", axis=1, tiled=True)
    gate_up = expert_gate_up.reshape(local_experts, D, 2 * hidden_quarter)
    projected = jnp.einsum("td,edf->etf", rows, gate_up, preferred_element_type=jnp.float32)
    activated = jax.nn.silu(projected[..., :hidden_quarter]) * projected[..., hidden_quarter:]
    activated = activated.astype(jnp.bfloat16).astype(jnp.float32)
    weighted = (activated * jnp.transpose(gate_local)[:, :, None]).astype(jnp.bfloat16)
    weighted = lax.all_gather(weighted, "tp", axis=2, tiled=True)
    weighted = jnp.transpose(weighted, (1, 0, 2)).reshape(rows.shape[0], -1)
    partial = jnp.dot(weighted, down_full, preferred_element_type=jnp.float32).astype(jnp.bfloat16)
    partial = lax.psum_scatter(partial, "seq", scatter_dimension=0, tiled=True)
    return partial.astype(jnp.float32)


def dispatch_experts(moe_in, expert_ids, route_weights, expert_gate_up, expert_down, experts_all, capacity):
    quarter = moe_in.shape[1]
    local_experts = expert_gate_up.shape[0]
    flat_ids = expert_ids.reshape(NEW * TOP)
    onehot = (flat_ids[:, None] == jnp.arange(experts_all, dtype=jnp.int32)[None, :]).astype(
        jnp.int32
    )
    ranks = jnp.sum((jnp.cumsum(onehot, axis=0) - onehot) * onehot, axis=1)
    target = (flat_ids * capacity + ranks).reshape(NEW, TOP)
    slot_ids = jnp.arange(experts_all * capacity, dtype=jnp.int32)
    selector = jnp.sum(
        (target[None, :, :] == slot_ids[:, None, None]).astype(jnp.int32), axis=2
    ).astype(jnp.bfloat16)
    send_rows = jnp.dot(selector, moe_in, preferred_element_type=jnp.float32).astype(jnp.bfloat16)
    send_rows = send_rows.reshape(experts_all, capacity, quarter)
    received = lax.all_to_all(send_rows, "seq", split_axis=0, concat_axis=1, tiled=True)
    hidden_quarter = expert_gate_up.shape[3]
    gate_up_local = expert_gate_up.reshape(local_experts, D, 2 * hidden_quarter)
    weight_rows = gate_up_local
    projected = jnp.einsum(
        "erd,edf->erf",
        lax.all_gather(received, "tp", axis=2, tiled=True),
        weight_rows,
        preferred_element_type=jnp.float32,
    )
    activated = (
        jax.nn.silu(projected[..., :hidden_quarter]) * projected[..., hidden_quarter:]
    ).astype(jnp.bfloat16)
    down_terms = jnp.einsum(
        "erf,efd->erd", activated, expert_down, preferred_element_type=jnp.float32
    )
    expert_result = lax.psum_scatter(
        down_terms.astype(jnp.bfloat16), "tp", scatter_dimension=2, tiled=True
    )
    returned = lax.all_to_all(
        expert_result, "seq", split_axis=1, concat_axis=0, tiled=True
    ).reshape(experts_all * capacity, quarter)
    picked = jnp.take(returned, target, axis=0)
    return jnp.sum(route_weights[:, :, None] * picked.astype(jnp.float32), axis=1)


def body(
    hidden,
    new_queries,
    new_keys,
    new_values,
    cache_keys,
    cache_values,
    cache_lengths,
    out_proj,
    moe_gain,
    expert_ids,
    route_weights,
    expert_gate_up,
    expert_down,
    next_gain,
    qkv_proj,
    query_gain,
    key_gain,
):
    seq_count = lax.axis_size("seq")
    here = lax.axis_index("seq")
    local_experts = expert_gate_up.shape[0]
    experts_all = local_experts * seq_count
    capacity = max(2, 3 * NEW * TOP // (2 * experts_all))
    dense = NEW <= 2 * capacity
    if dense:
        tp_here = lax.axis_index("tp")
        quarter_width = hidden.shape[1]
        down_full = lax.all_gather(expert_down, "tp", axis=1, tiled=True)
        down_full = lax.dynamic_slice_in_dim(down_full, tp_here * quarter_width, quarter_width, axis=2)
        down_full = down_full.reshape(-1, quarter_width)
    local_width = new_queries.shape[1]
    local_heads = local_width // HEAD_DIM
    quarter = hidden.shape[1]
    own_queries = new_queries.reshape(1, NEW, local_heads, HEAD_DIM)
    own_keys = new_keys.reshape(1, NEW, local_heads, HEAD_DIM)
    own_values = new_values.reshape(1, NEW, local_heads, HEAD_DIM)
    offsets = jnp.arange(NEW, dtype=jnp.int32)
    causal = (offsets[None, :] <= offsets[:, None])[None]
    own_out, own_max, own_total = softmax_parts(own_queries, own_keys, own_values, causal)
    span = cache_keys.shape[1]
    block = min(512, span)
    my_length = lax.dynamic_index_in_dim(cache_lengths, here, 0, keepdims=False)
    block_count = (my_length + block - 1) // block
    key_blocks = cache_keys.reshape(span, local_heads, HEAD_DIM)
    value_blocks = cache_values.reshape(span, local_heads, HEAD_DIM)

    def cache_block(index, carry):
        begin = index * block
        keys_here = lax.dynamic_slice_in_dim(key_blocks, begin, block, 0)[None]
        values_here = lax.dynamic_slice_in_dim(value_blocks, begin, block, 0)[None]
        positions = begin + jnp.arange(block, dtype=jnp.int32)
        allowed = jnp.broadcast_to((positions < my_length)[None, None, :], (1, NEW, block))
        return combine_parts(carry, softmax_parts(own_queries, keys_here, values_here, allowed))

    start_parts = (
        jnp.zeros((1, NEW, local_heads, HEAD_DIM), jnp.float32),
        jnp.full((1, NEW, local_heads), -1e30, jnp.float32),
        jnp.zeros((1, NEW, local_heads), jnp.float32),
    )
    pieces, maxima, totals = lax.fori_loop(0, block_count, cache_block, start_parts)
    attended = merge_parts(
        jnp.concatenate([own_out, pieces], 0),
        jnp.concatenate([own_max, maxima], 0),
        jnp.concatenate([own_total, totals], 0),
    )
    attended = attended.reshape(NEW, local_width).astype(jnp.bfloat16)
    if dense:
        attended, down_full = lax.optimization_barrier((attended, down_full))
    attn_term = jnp.dot(attended, out_proj, preferred_element_type=jnp.float32)
    residual = hidden.astype(jnp.float32) + lax.psum_scatter(
        attn_term.astype(jnp.bfloat16), "tp", scatter_dimension=1, tiled=True
    ).astype(jnp.float32)
    square_total = lax.psum(jnp.sum(residual * residual, axis=1), "tp")
    moe_in = (residual * lax.rsqrt(square_total / D + epsilon)[:, None] * moe_gain[None, :]).astype(
        jnp.bfloat16
    )
    if dense:
        moe_term = dense_experts(
            moe_in, expert_ids, route_weights, expert_gate_up, down_full, here, experts_all
        )
    else:
        moe_term = dispatch_experts(
            moe_in, expert_ids, route_weights, expert_gate_up, expert_down, experts_all, capacity
        )
    routed = residual + moe_term
    layer_out = routed.astype(jnp.bfloat16)
    scaled = (routed * next_gain[None, :]).astype(jnp.bfloat16)
    qkv_local = qkv_proj.reshape(D, 3 * local_width)
    weight_rows = qkv_local
    mixed = jnp.dot(
        lax.all_gather(scaled, "tp", axis=1, tiled=True),
        weight_rows,
        preferred_element_type=jnp.float32,
    )
    mixed = mixed.reshape(NEW, 3, local_width)
    squares_routed = jnp.sum(routed * routed, axis=1)
    routed_total, query_raw, key_raw = lax.psum(
        (
            squares_routed,
            jnp.sum(mixed[:, 0] * mixed[:, 0], axis=1),
            jnp.sum(mixed[:, 1] * mixed[:, 1], axis=1),
        ),
        "tp",
    )
    x_scale = lax.rsqrt(routed_total / D + epsilon)
    query_pre = mixed[:, 0] * x_scale[:, None]
    key_pre = mixed[:, 1] * x_scale[:, None]
    query_total = query_raw * x_scale * x_scale
    key_total = key_raw * x_scale * x_scale
    next_query = (
        query_pre * lax.rsqrt(query_total / D + epsilon)[:, None] * query_gain[None, :]
    ).astype(jnp.bfloat16)
    next_key = (key_pre * lax.rsqrt(key_total / D + epsilon)[:, None] * key_gain[None, :]).astype(
        jnp.bfloat16
    )
    next_value = (mixed[:, 2] * x_scale[:, None]).astype(jnp.bfloat16)
    return (layer_out, next_query, next_key, next_value)


def solution(mesh):
    return jax.shard_map(
        body,
        mesh=mesh,
        in_specs=(
            P("seq", "tp"),
            P("seq", "tp"),
            P("seq", "tp"),
            P("seq", "tp"),
            P("seq", None, "tp"),
            P("seq", None, "tp"),
            P(),
            P("tp", None),
            P("tp"),
            P("seq", None),
            P("seq", None),
            P("seq", None, None, "tp"),
            P("seq", "tp", None),
            P("tp"),
            P(None, None, "tp"),
            P("tp"),
            P("tp"),
        ),
        out_specs=(P("seq", "tp"), P("seq", "tp"), P("seq", "tp"), P("seq", "tp")),
        check_vma=False,
    )
```

```python
import math

import jax
import jax.numpy as jnp
from jax import lax
from jax.sharding import PartitionSpec as P

D = 2048
HEAD_DIM = 128
TOP = 8
NEW = 256


epsilon = 1e-05


def softmax_parts(queries, key_rows, values, allowed):
    scores = jnp.einsum(
        "bthe,bche->bhtc", queries, key_rows, preferred_element_type=jnp.float32
    ) / math.sqrt(HEAD_DIM)
    scores = jnp.where(allowed[:, None], scores, -1e30)
    row_max = jnp.max(scores, axis=3)
    weights = jnp.where(allowed[:, None], jnp.exp(scores - row_max[..., None]), 0.0)
    row_total = jnp.sum(weights, axis=3)
    partial_out = jnp.einsum(
        "bhtc,bche->bthe", weights.astype(jnp.bfloat16), values, preferred_element_type=jnp.float32
    )
    return (partial_out, jnp.swapaxes(row_max, 1, 2), jnp.swapaxes(row_total, 1, 2))


def combine_parts(first, second):
    out_a, max_a, total_a = first
    out_b, max_b, total_b = second
    joint = jnp.maximum(max_a, max_b)
    factor_a = jnp.exp(max_a - joint)
    factor_b = jnp.exp(max_b - joint)
    return (
        out_a * factor_a[..., None] + out_b * factor_b[..., None],
        joint,
        total_a * factor_a + total_b * factor_b,
    )


def merge_parts(pieces, maxima, totals):
    overall = jnp.max(maxima, axis=0)
    factor = jnp.exp(maxima - overall[None])
    denominator = jnp.sum(totals * factor, axis=0)
    merged = jnp.sum(pieces * factor[..., None], axis=0)
    return merged / denominator[..., None]


def dense_experts(moe_in, expert_ids, route_weights, expert_gate_up, down_full, here, experts_all):
    local_experts = expert_gate_up.shape[0]
    hidden_quarter = expert_gate_up.shape[3]
    tokens, quarter = moe_in.shape
    seq_count = experts_all // local_experts
    gate_w = jnp.sum(
        route_weights[:, :, None]
        * (expert_ids[:, :, None] == jnp.arange(experts_all, dtype=jnp.int32)[None, None, :]),
        axis=1,
    )
    gate_t = jnp.transpose(gate_w)
    gate_hi = gate_t.astype(jnp.bfloat16)
    gate_lo = (gate_t - gate_hi.astype(jnp.float32)).astype(jnp.bfloat16)
    info = jnp.concatenate([gate_hi, gate_lo], axis=0).reshape(-1, quarter)
    packed = jnp.concatenate([moe_in, info], axis=0)
    gathered = lax.all_gather(packed, "seq", axis=0, tiled=False)
    rows_q = gathered[:, :tokens].reshape(seq_count * tokens, quarter)
    info_all = gathered[:, tokens:].reshape(seq_count, 2, experts_all, tokens).astype(jnp.float32)
    gate_all = info_all[:, 0] + info_all[:, 1]
    gate_local = lax.dynamic_slice_in_dim(gate_all, here * local_experts, local_experts, axis=1)
    gate_local = jnp.transpose(gate_local, (1, 0, 2)).reshape(local_experts, seq_count * tokens)
    rows = lax.all_gather(rows_q, "tp", axis=1, tiled=True)
    gate_up = expert_gate_up.reshape(local_experts, D, 2 * hidden_quarter)
    projected = jnp.einsum("td,edf->etf", rows, gate_up, preferred_element_type=jnp.float32)
    activated = jax.nn.silu(projected[..., :hidden_quarter]) * projected[..., hidden_quarter:]
    activated = activated.astype(jnp.bfloat16).astype(jnp.float32)
    weighted = (activated * gate_local[:, :, None]).astype(jnp.bfloat16)
    weighted = lax.all_gather(weighted, "tp", axis=2, tiled=True)
    partial = jnp.einsum(
        "etf,efd->td", weighted, down_full, preferred_element_type=jnp.float32
    ).astype(jnp.bfloat16)
    partial = lax.psum_scatter(partial, "seq", scatter_dimension=0, tiled=True)
    return partial.astype(jnp.float32)


def dispatch_experts(moe_in, expert_ids, route_weights, expert_gate_up, expert_down, experts_all, capacity):
    quarter = moe_in.shape[1]
    local_experts = expert_gate_up.shape[0]
    flat_ids = expert_ids.reshape(NEW * TOP)
    onehot = (flat_ids[:, None] == jnp.arange(experts_all, dtype=jnp.int32)[None, :]).astype(
        jnp.int32
    )
    ranks = jnp.sum((jnp.cumsum(onehot, axis=0) - onehot) * onehot, axis=1)
    target = (flat_ids * capacity + ranks).reshape(NEW, TOP)
    slot_ids = jnp.arange(experts_all * capacity, dtype=jnp.int32)
    selector = jnp.sum(
        (target[None, :, :] == slot_ids[:, None, None]).astype(jnp.int32), axis=2
    ).astype(jnp.bfloat16)
    send_rows = jnp.dot(selector, moe_in, preferred_element_type=jnp.float32).astype(jnp.bfloat16)
    send_rows = send_rows.reshape(experts_all, capacity, quarter)
    received = lax.all_to_all(send_rows, "seq", split_axis=0, concat_axis=1, tiled=True)
    hidden_quarter = expert_gate_up.shape[3]
    gate_up_local = expert_gate_up.reshape(local_experts, D, 2 * hidden_quarter)
    weight_rows = gate_up_local
    projected = jnp.einsum(
        "erd,edf->erf",
        lax.all_gather(received, "tp", axis=2, tiled=True),
        weight_rows,
        preferred_element_type=jnp.float32,
    )
    activated = (
        jax.nn.silu(projected[..., :hidden_quarter]) * projected[..., hidden_quarter:]
    ).astype(jnp.bfloat16)
    down_terms = jnp.einsum(
        "erf,efd->erd", activated, expert_down, preferred_element_type=jnp.float32
    )
    expert_result = lax.psum_scatter(
        down_terms.astype(jnp.bfloat16), "tp", scatter_dimension=2, tiled=True
    )
    returned = lax.all_to_all(
        expert_result, "seq", split_axis=1, concat_axis=0, tiled=True
    ).reshape(experts_all * capacity, quarter)
    picked = jnp.take(returned, target, axis=0)
    return jnp.sum(route_weights[:, :, None] * picked.astype(jnp.float32), axis=1)


def body(
    hidden,
    new_queries,
    new_keys,
    new_values,
    cache_keys,
    cache_values,
    cache_lengths,
    out_proj,
    moe_gain,
    expert_ids,
    route_weights,
    expert_gate_up,
    expert_down,
    next_gain,
    qkv_proj,
    query_gain,
    key_gain,
):
    seq_count = lax.axis_size("seq")
    here = lax.axis_index("seq")
    local_experts = expert_gate_up.shape[0]
    experts_all = local_experts * seq_count
    capacity = max(2, 3 * NEW * TOP // (2 * experts_all))
    dense = NEW <= 2 * capacity
    if dense:
        tp_here = lax.axis_index("tp")
        quarter_width = hidden.shape[1]
        down_full = lax.all_gather(expert_down, "tp", axis=1, tiled=True)
        down_full = lax.dynamic_slice_in_dim(down_full, tp_here * quarter_width, quarter_width, axis=2)
    local_width = new_queries.shape[1]
    local_heads = local_width // HEAD_DIM
    quarter = hidden.shape[1]
    own_queries = new_queries.reshape(1, NEW, local_heads, HEAD_DIM)
    own_keys = new_keys.reshape(1, NEW, local_heads, HEAD_DIM)
    own_values = new_values.reshape(1, NEW, local_heads, HEAD_DIM)
    offsets = jnp.arange(NEW, dtype=jnp.int32)
    causal = (offsets[None, :] <= offsets[:, None])[None]
    own_out, own_max, own_total = softmax_parts(own_queries, own_keys, own_values, causal)
    span = cache_keys.shape[1]
    block = min(512, span)
    my_length = lax.dynamic_index_in_dim(cache_lengths, here, 0, keepdims=False)
    block_count = (my_length + block - 1) // block
    key_blocks = cache_keys.reshape(span, local_heads, HEAD_DIM)
    value_blocks = cache_values.reshape(span, local_heads, HEAD_DIM)

    def cache_block(index, carry):
        begin = index * block
        keys_here = lax.dynamic_slice_in_dim(key_blocks, begin, block, 0)[None]
        values_here = lax.dynamic_slice_in_dim(value_blocks, begin, block, 0)[None]
        positions = begin + jnp.arange(block, dtype=jnp.int32)
        allowed = jnp.broadcast_to((positions < my_length)[None, None, :], (1, NEW, block))
        return combine_parts(carry, softmax_parts(own_queries, keys_here, values_here, allowed))

    start_parts = (
        jnp.zeros((1, NEW, local_heads, HEAD_DIM), jnp.float32),
        jnp.full((1, NEW, local_heads), -1e30, jnp.float32),
        jnp.zeros((1, NEW, local_heads), jnp.float32),
    )
    pieces, maxima, totals = lax.fori_loop(0, block_count, cache_block, start_parts)
    attended = merge_parts(
        jnp.concatenate([own_out, pieces], 0),
        jnp.concatenate([own_max, maxima], 0),
        jnp.concatenate([own_total, totals], 0),
    )
    attended = attended.reshape(NEW, local_width).astype(jnp.bfloat16)
    if dense:
        attended, down_full = lax.optimization_barrier((attended, down_full))
    attn_term = jnp.dot(attended, out_proj, preferred_element_type=jnp.float32)
    residual = hidden.astype(jnp.float32) + lax.psum_scatter(
        attn_term.astype(jnp.bfloat16), "tp", scatter_dimension=1, tiled=True
    ).astype(jnp.float32)
    square_total = lax.psum(jnp.sum(residual * residual, axis=1), "tp")
    moe_in = (residual * lax.rsqrt(square_total / D + epsilon)[:, None] * moe_gain[None, :]).astype(
        jnp.bfloat16
    )
    if dense:
        moe_term = dense_experts(
            moe_in, expert_ids, route_weights, expert_gate_up, down_full, here, experts_all
        )
    else:
        moe_term = dispatch_experts(
            moe_in, expert_ids, route_weights, expert_gate_up, expert_down, experts_all, capacity
        )
    routed = residual + moe_term
    layer_out = routed.astype(jnp.bfloat16)
    scaled = (routed * next_gain[None, :]).astype(jnp.bfloat16)
    qkv_local = qkv_proj.reshape(D, 3 * local_width)
    weight_rows = qkv_local
    mixed = jnp.dot(
        lax.all_gather(scaled, "tp", axis=1, tiled=True),
        weight_rows,
        preferred_element_type=jnp.float32,
    )
    mixed = mixed.reshape(NEW, 3, local_width)
    squares_routed = jnp.sum(routed * routed, axis=1)
    routed_total, query_raw, key_raw = lax.psum(
        (
            squares_routed,
            jnp.sum(mixed[:, 0] * mixed[:, 0], axis=1),
            jnp.sum(mixed[:, 1] * mixed[:, 1], axis=1),
        ),
        "tp",
    )
    x_scale = lax.rsqrt(routed_total / D + epsilon)
    query_pre = mixed[:, 0] * x_scale[:, None]
    key_pre = mixed[:, 1] * x_scale[:, None]
    query_total = query_raw * x_scale * x_scale
    key_total = key_raw * x_scale * x_scale
    next_query = (
        query_pre * lax.rsqrt(query_total / D + epsilon)[:, None] * query_gain[None, :]
    ).astype(jnp.bfloat16)
    next_key = (key_pre * lax.rsqrt(key_total / D + epsilon)[:, None] * key_gain[None, :]).astype(
        jnp.bfloat16
    )
    next_value = (mixed[:, 2] * x_scale[:, None]).astype(jnp.bfloat16)
    return (layer_out, next_query, next_key, next_value)


def solution(mesh):
    return jax.shard_map(
        body,
        mesh=mesh,
        in_specs=(
            P("seq", "tp"),
            P("seq", "tp"),
            P("seq", "tp"),
            P("seq", "tp"),
            P("seq", None, "tp"),
            P("seq", None, "tp"),
            P(),
            P("tp", None),
            P("tp"),
            P("seq", None),
            P("seq", None),
            P("seq", None, None, "tp"),
            P("seq", "tp", None),
            P("tp"),
            P(None, None, "tp"),
            P("tp"),
            P("tp"),
        ),
        out_specs=(P("seq", "tp"), P("seq", "tp"), P("seq", "tp"), P("seq", "tp")),
        check_vma=False,
    )
```

```python
import functools
import math

import jax
import jax.numpy as jnp
from jax import lax
from jax.experimental import pallas as pl
from jax.experimental.pallas import tpu as pltpu
from jax.sharding import PartitionSpec as P

D = 2048
HEAD_DIM = 128
TOP = 8
NEW = 256


epsilon = 1e-05


def flash_kernel(len_ref, q_ref, k_ref, v_ref, nk_ref, nv_ref, o_ref, m_sc, l_sc, acc_sc, *, block, heads, steps):
    j = pl.program_id(0)
    length = len_ref[0]
    valid = (length + block - 1) // block
    tokens = q_ref.shape[0]
    scale = 1.0 / math.sqrt(HEAD_DIM)

    @pl.when(j == 0)
    def _():
        m_sc[...] = jnp.full(m_sc.shape, -1e30, jnp.float32)
        l_sc[...] = jnp.zeros(l_sc.shape, jnp.float32)
        acc_sc[...] = jnp.zeros(acc_sc.shape, jnp.float32)

    def update(keys_ref, values_ref, allowed):
        for h in range(heads):
            cols = slice(h * HEAD_DIM, (h + 1) * HEAD_DIM)
            q = q_ref[:, cols]
            k = keys_ref[:, cols]
            s = lax.dot_general(q, k, (((1,), (1,)), ((), ())), preferred_element_type=jnp.float32) * scale
            s = jnp.where(allowed, s, -1e30)
            m_old = m_sc[h]
            m_new = jnp.maximum(m_old, jnp.max(s, axis=1, keepdims=True))
            alpha = jnp.exp(m_old - m_new)
            p = jnp.where(allowed, jnp.exp(s - m_new), 0.0)
            l_sc[h] = alpha * l_sc[h] + jnp.sum(p, axis=1, keepdims=True)
            pv = jnp.dot(p.astype(jnp.bfloat16), values_ref[:, cols], preferred_element_type=jnp.float32)
            acc_sc[:, cols] = alpha * acc_sc[:, cols] + pv
            m_sc[h] = m_new

    @pl.when(j < valid)
    def _():
        pos = j * block + lax.broadcasted_iota(jnp.int32, (tokens, block), 1)
        update(k_ref, v_ref, pos < length)

    @pl.when(j == steps - 1)
    def _():
        row = lax.broadcasted_iota(jnp.int32, (tokens, tokens), 0)
        col = lax.broadcasted_iota(jnp.int32, (tokens, tokens), 1)
        update(nk_ref, nv_ref, col <= row)
        for h in range(heads):
            cols = slice(h * HEAD_DIM, (h + 1) * HEAD_DIM)
            o_ref[:, cols] = (acc_sc[:, cols] / l_sc[h]).astype(o_ref.dtype)


def flash_attention(length, queries, cache_k, cache_v, new_k, new_v, block=1024):
    tokens, width = queries.shape
    span = cache_k.shape[0]
    block = min(block, span)
    heads = width // HEAD_DIM
    steps = span // block + 1
    last = span // block - 1

    def cache_map(j, len_ref):
        valid = (len_ref[0] + block - 1) // block
        return (jnp.minimum(j, jnp.maximum(valid - 1, 0)), 0)

    grid_spec = pltpu.PrefetchScalarGridSpec(
        num_scalar_prefetch=1,
        grid=(steps,),
        in_specs=[
            pl.BlockSpec((tokens, width), lambda j, l: (0, 0)),
            pl.BlockSpec((block, width), cache_map),
            pl.BlockSpec((block, width), cache_map),
            pl.BlockSpec((tokens, width), lambda j, l: (0, 0)),
            pl.BlockSpec((tokens, width), lambda j, l: (0, 0)),
        ],
        out_specs=pl.BlockSpec((tokens, width), lambda j, l: (0, 0)),
        scratch_shapes=[
            pltpu.VMEM((heads, tokens, 1), jnp.float32),
            pltpu.VMEM((heads, tokens, 1), jnp.float32),
            pltpu.VMEM((tokens, width), jnp.float32),
        ],
    )
    kernel = functools.partial(flash_kernel, block=block, heads=heads, steps=steps)
    return pl.pallas_call(
        kernel,
        grid_spec=grid_spec,
        out_shape=jax.ShapeDtypeStruct((tokens, width), jnp.bfloat16),
        compiler_params=pltpu.CompilerParams(dimension_semantics=("arbitrary",)),
    )(length.reshape(1), queries, cache_k, cache_v, new_k, new_v)


def dense_experts(moe_in, expert_ids, route_weights, expert_gate_up, down_full, here, experts_all):
    local_experts = expert_gate_up.shape[0]
    hidden_quarter = expert_gate_up.shape[3]
    tokens, quarter = moe_in.shape
    seq_count = experts_all // local_experts
    gate_w = jnp.sum(
        route_weights[:, :, None]
        * (expert_ids[:, :, None] == jnp.arange(experts_all, dtype=jnp.int32)[None, None, :]),
        axis=1,
    )
    gate_t = jnp.transpose(gate_w)
    gate_hi = gate_t.astype(jnp.bfloat16)
    gate_lo = (gate_t - gate_hi.astype(jnp.float32)).astype(jnp.bfloat16)
    info = jnp.concatenate([gate_hi, gate_lo], axis=0).reshape(-1, quarter)
    packed = jnp.concatenate([moe_in, info], axis=0)
    gathered = lax.all_gather(packed, "seq", axis=0, tiled=False)
    rows_q = gathered[:, :tokens].reshape(seq_count * tokens, quarter)
    info_all = gathered[:, tokens:].reshape(seq_count, 2, experts_all, tokens).astype(jnp.float32)
    gate_all = info_all[:, 0] + info_all[:, 1]
    gate_local = lax.dynamic_slice_in_dim(gate_all, here * local_experts, local_experts, axis=1)
    gate_local = jnp.transpose(gate_local, (1, 0, 2)).reshape(local_experts, seq_count * tokens)
    rows = lax.all_gather(rows_q, "tp", axis=1, tiled=True)
    gate_up = expert_gate_up.reshape(local_experts, D, 2 * hidden_quarter)
    projected = jnp.einsum("td,edf->etf", rows, gate_up, preferred_element_type=jnp.float32)
    activated = jax.nn.silu(projected[..., :hidden_quarter]) * projected[..., hidden_quarter:]
    activated = activated.astype(jnp.bfloat16).astype(jnp.float32)
    weighted = (activated * gate_local[:, :, None]).astype(jnp.bfloat16)
    weighted = lax.all_gather(weighted, "tp", axis=2, tiled=True)
    partial = jnp.einsum(
        "etf,efd->td", weighted, down_full, preferred_element_type=jnp.float32
    ).astype(jnp.bfloat16)
    partial = lax.psum_scatter(partial, "seq", scatter_dimension=0, tiled=True)
    return partial.astype(jnp.float32)


def dispatch_experts(moe_in, expert_ids, route_weights, expert_gate_up, expert_down, experts_all, capacity):
    quarter = moe_in.shape[1]
    local_experts = expert_gate_up.shape[0]
    flat_ids = expert_ids.reshape(NEW * TOP)
    onehot = (flat_ids[:, None] == jnp.arange(experts_all, dtype=jnp.int32)[None, :]).astype(
        jnp.int32
    )
    ranks = jnp.sum((jnp.cumsum(onehot, axis=0) - onehot) * onehot, axis=1)
    target = (flat_ids * capacity + ranks).reshape(NEW, TOP)
    slot_ids = jnp.arange(experts_all * capacity, dtype=jnp.int32)
    selector = jnp.sum(
        (target[None, :, :] == slot_ids[:, None, None]).astype(jnp.int32), axis=2
    ).astype(jnp.bfloat16)
    send_rows = jnp.dot(selector, moe_in, preferred_element_type=jnp.float32).astype(jnp.bfloat16)
    send_rows = send_rows.reshape(experts_all, capacity, quarter)
    received = lax.all_to_all(send_rows, "seq", split_axis=0, concat_axis=1, tiled=True)
    hidden_quarter = expert_gate_up.shape[3]
    gate_up_local = expert_gate_up.reshape(local_experts, D, 2 * hidden_quarter)
    weight_rows = gate_up_local
    projected = jnp.einsum(
        "erd,edf->erf",
        lax.all_gather(received, "tp", axis=2, tiled=True),
        weight_rows,
        preferred_element_type=jnp.float32,
    )
    activated = (
        jax.nn.silu(projected[..., :hidden_quarter]) * projected[..., hidden_quarter:]
    ).astype(jnp.bfloat16)
    down_terms = jnp.einsum(
        "erf,efd->erd", activated, expert_down, preferred_element_type=jnp.float32
    )
    expert_result = lax.psum_scatter(
        down_terms.astype(jnp.bfloat16), "tp", scatter_dimension=2, tiled=True
    )
    returned = lax.all_to_all(
        expert_result, "seq", split_axis=1, concat_axis=0, tiled=True
    ).reshape(experts_all * capacity, quarter)
    picked = jnp.take(returned, target, axis=0)
    return jnp.sum(route_weights[:, :, None] * picked.astype(jnp.float32), axis=1)


def body(
    hidden,
    new_queries,
    new_keys,
    new_values,
    cache_keys,
    cache_values,
    cache_lengths,
    out_proj,
    moe_gain,
    expert_ids,
    route_weights,
    expert_gate_up,
    expert_down,
    next_gain,
    qkv_proj,
    query_gain,
    key_gain,
):
    seq_count = lax.axis_size("seq")
    here = lax.axis_index("seq")
    local_experts = expert_gate_up.shape[0]
    experts_all = local_experts * seq_count
    capacity = max(2, 3 * NEW * TOP // (2 * experts_all))
    dense = NEW <= 2 * capacity
    if dense:
        tp_here = lax.axis_index("tp")
        quarter_width = hidden.shape[1]
        down_full = lax.all_gather(expert_down, "tp", axis=1, tiled=True)
        down_full = lax.dynamic_slice_in_dim(down_full, tp_here * quarter_width, quarter_width, axis=2)
    local_width = new_queries.shape[1]
    local_heads = local_width // HEAD_DIM
    quarter = hidden.shape[1]
    span = cache_keys.shape[1]
    my_length = lax.dynamic_index_in_dim(cache_lengths, here, 0, keepdims=False)
    attended = flash_attention(
        my_length,
        new_queries,
        cache_keys.reshape(span, local_width),
        cache_values.reshape(span, local_width),
        new_keys,
        new_values,
    )
    if dense:
        attended, down_full = lax.optimization_barrier((attended, down_full))
    attn_term = jnp.dot(attended, out_proj, preferred_element_type=jnp.float32)
    residual = hidden.astype(jnp.float32) + lax.psum_scatter(
        attn_term.astype(jnp.bfloat16), "tp", scatter_dimension=1, tiled=True
    ).astype(jnp.float32)
    square_total = lax.psum(jnp.sum(residual * residual, axis=1), "tp")
    moe_in = (residual * lax.rsqrt(square_total / D + epsilon)[:, None] * moe_gain[None, :]).astype(
        jnp.bfloat16
    )
    if dense:
        moe_term = dense_experts(
            moe_in, expert_ids, route_weights, expert_gate_up, down_full, here, experts_all
        )
    else:
        moe_term = dispatch_experts(
            moe_in, expert_ids, route_weights, expert_gate_up, expert_down, experts_all, capacity
        )
    routed = residual + moe_term
    layer_out = routed.astype(jnp.bfloat16)
    scaled = (routed * next_gain[None, :]).astype(jnp.bfloat16)
    qkv_local = qkv_proj.reshape(D, 3 * local_width)
    weight_rows = qkv_local
    mixed = jnp.dot(
        lax.all_gather(scaled, "tp", axis=1, tiled=True),
        weight_rows,
        preferred_element_type=jnp.float32,
    )
    mixed = mixed.reshape(NEW, 3, local_width)
    squares_routed = jnp.sum(routed * routed, axis=1)
    routed_total, query_raw, key_raw = lax.psum(
        (
            squares_routed,
            jnp.sum(mixed[:, 0] * mixed[:, 0], axis=1),
            jnp.sum(mixed[:, 1] * mixed[:, 1], axis=1),
        ),
        "tp",
    )
    x_scale = lax.rsqrt(routed_total / D + epsilon)
    query_pre = mixed[:, 0] * x_scale[:, None]
    key_pre = mixed[:, 1] * x_scale[:, None]
    query_total = query_raw * x_scale * x_scale
    key_total = key_raw * x_scale * x_scale
    next_query = (
        query_pre * lax.rsqrt(query_total / D + epsilon)[:, None] * query_gain[None, :]
    ).astype(jnp.bfloat16)
    next_key = (key_pre * lax.rsqrt(key_total / D + epsilon)[:, None] * key_gain[None, :]).astype(
        jnp.bfloat16
    )
    next_value = (mixed[:, 2] * x_scale[:, None]).astype(jnp.bfloat16)
    return (layer_out, next_query, next_key, next_value)


def solution(mesh):
    return jax.shard_map(
        body,
        mesh=mesh,
        in_specs=(
            P("seq", "tp"),
            P("seq", "tp"),
            P("seq", "tp"),
            P("seq", "tp"),
            P("seq", None, "tp"),
            P("seq", None, "tp"),
            P(),
            P("tp", None),
            P("tp"),
            P("seq", None),
            P("seq", None),
            P("seq", None, None, "tp"),
            P("seq", "tp", None),
            P("tp"),
            P(None, None, "tp"),
            P("tp"),
            P("tp"),
        ),
        out_specs=(P("seq", "tp"), P("seq", "tp"), P("seq", "tp"), P("seq", "tp")),
        check_vma=False,
    )
```

```python
import functools
import math

import jax
import jax.numpy as jnp
from jax import lax
from jax.experimental import pallas as pl
from jax.experimental.pallas import tpu as pltpu
from jax.sharding import PartitionSpec as P

D = 2048
HEAD_DIM = 128
TOP = 8
NEW = 256


epsilon = 1e-05


def flash_kernel(len_ref, q_ref, k_ref, v_ref, nk_ref, nv_ref, o_ref, m_sc, l_sc, acc_sc, *, block, heads, steps):
    j = pl.program_id(0)
    length = len_ref[0]
    valid = (length + block - 1) // block
    tokens = q_ref.shape[0]
    scale = 1.0 / math.sqrt(HEAD_DIM)

    @pl.when(j == 0)
    def _():
        m_sc[...] = jnp.full(m_sc.shape, -1e30, jnp.float32)
        l_sc[...] = jnp.zeros(l_sc.shape, jnp.float32)
        acc_sc[...] = jnp.zeros(acc_sc.shape, jnp.float32)

    def update(keys_ref, values_ref, allowed):
        for h in range(heads):
            cols = slice(h * HEAD_DIM, (h + 1) * HEAD_DIM)
            q = q_ref[:, cols]
            k = keys_ref[:, cols]
            s = lax.dot_general(q, k, (((1,), (1,)), ((), ())), preferred_element_type=jnp.float32) * scale
            s = jnp.where(allowed, s, -1e30)
            m_old = m_sc[h]
            m_new = jnp.maximum(m_old, jnp.max(s, axis=1, keepdims=True))
            alpha = jnp.exp(m_old - m_new)
            p = jnp.where(allowed, jnp.exp(s - m_new), 0.0)
            l_sc[h] = alpha * l_sc[h] + jnp.sum(p, axis=1, keepdims=True)
            pv = jnp.dot(p.astype(jnp.bfloat16), values_ref[:, cols], preferred_element_type=jnp.float32)
            acc_sc[:, cols] = alpha * acc_sc[:, cols] + pv
            m_sc[h] = m_new

    @pl.when(j < valid)
    def _():
        pos = j * block + lax.broadcasted_iota(jnp.int32, (tokens, block), 1)
        update(k_ref, v_ref, pos < length)

    @pl.when(j == steps - 1)
    def _():
        row = lax.broadcasted_iota(jnp.int32, (tokens, tokens), 0)
        col = lax.broadcasted_iota(jnp.int32, (tokens, tokens), 1)
        update(nk_ref, nv_ref, col <= row)
        for h in range(heads):
            cols = slice(h * HEAD_DIM, (h + 1) * HEAD_DIM)
            o_ref[:, cols] = (acc_sc[:, cols] / l_sc[h]).astype(o_ref.dtype)


def flash_attention(length, queries, cache_k, cache_v, new_k, new_v, block=1024):
    tokens, width = queries.shape
    span = cache_k.shape[0]
    block = min(block, span)
    heads = width // HEAD_DIM
    steps = span // block + 1
    last = span // block - 1

    def cache_map(j, len_ref):
        valid = (len_ref[0] + block - 1) // block
        return (jnp.minimum(j, jnp.maximum(valid - 1, 0)), 0)

    grid_spec = pltpu.PrefetchScalarGridSpec(
        num_scalar_prefetch=1,
        grid=(steps,),
        in_specs=[
            pl.BlockSpec((tokens, width), lambda j, l: (0, 0)),
            pl.BlockSpec((block, width), cache_map),
            pl.BlockSpec((block, width), cache_map),
            pl.BlockSpec((tokens, width), lambda j, l: (0, 0)),
            pl.BlockSpec((tokens, width), lambda j, l: (0, 0)),
        ],
        out_specs=pl.BlockSpec((tokens, width), lambda j, l: (0, 0)),
        scratch_shapes=[
            pltpu.VMEM((heads, tokens, 1), jnp.float32),
            pltpu.VMEM((heads, tokens, 1), jnp.float32),
            pltpu.VMEM((tokens, width), jnp.float32),
        ],
    )
    kernel = functools.partial(flash_kernel, block=block, heads=heads, steps=steps)
    return pl.pallas_call(
        kernel,
        grid_spec=grid_spec,
        out_shape=jax.ShapeDtypeStruct((tokens, width), jnp.bfloat16),
        compiler_params=pltpu.CompilerParams(dimension_semantics=("arbitrary",)),
    )(length.reshape(1), queries, cache_k, cache_v, new_k, new_v)


def dense_experts(moe_in, expert_ids, route_weights, expert_gate_up, down_full, here, experts_all):
    local_experts = expert_gate_up.shape[0]
    hidden_quarter = expert_gate_up.shape[2] // 2
    tokens, quarter = moe_in.shape
    seq_count = experts_all // local_experts
    gate_w = jnp.sum(
        route_weights[:, :, None]
        * (expert_ids[:, :, None] == jnp.arange(experts_all, dtype=jnp.int32)[None, None, :]),
        axis=1,
    )
    gate_t = jnp.transpose(gate_w)
    gate_hi = gate_t.astype(jnp.bfloat16)
    gate_lo = (gate_t - gate_hi.astype(jnp.float32)).astype(jnp.bfloat16)
    info = jnp.concatenate([gate_hi, gate_lo], axis=0).reshape(-1, quarter)
    packed = jnp.concatenate([moe_in, info], axis=0)
    gathered = lax.all_gather(packed, "seq", axis=0, tiled=False)
    rows_q = gathered[:, :tokens].reshape(seq_count * tokens, quarter)
    info_all = gathered[:, tokens:].reshape(seq_count, 2, experts_all, tokens).astype(jnp.float32)
    gate_all = info_all[:, 0] + info_all[:, 1]
    gate_local = lax.dynamic_slice_in_dim(gate_all, here * local_experts, local_experts, axis=1)
    gate_local = jnp.transpose(gate_local, (1, 0, 2)).reshape(local_experts, seq_count * tokens)
    rows = lax.all_gather(rows_q, "tp", axis=1, tiled=True)
    projected = jnp.einsum("td,edf->etf", rows, expert_gate_up, preferred_element_type=jnp.float32)
    activated = jax.nn.silu(projected[..., :hidden_quarter]) * projected[..., hidden_quarter:]
    activated = activated.astype(jnp.bfloat16).astype(jnp.float32)
    weighted = (activated * gate_local[:, :, None]).astype(jnp.bfloat16)
    weighted = lax.all_gather(weighted, "tp", axis=2, tiled=True)
    partial = jnp.einsum(
        "etf,efd->td", weighted, down_full, preferred_element_type=jnp.float32
    ).astype(jnp.bfloat16)
    partial = lax.psum_scatter(partial, "seq", scatter_dimension=0, tiled=True)
    return partial.astype(jnp.float32)


def dispatch_experts(moe_in, expert_ids, route_weights, expert_gate_up, expert_down, experts_all, capacity):
    quarter = moe_in.shape[1]
    local_experts = expert_gate_up.shape[0]
    flat_ids = expert_ids.reshape(NEW * TOP)
    onehot = (flat_ids[:, None] == jnp.arange(experts_all, dtype=jnp.int32)[None, :]).astype(
        jnp.int32
    )
    ranks = jnp.sum((jnp.cumsum(onehot, axis=0) - onehot) * onehot, axis=1)
    target = (flat_ids * capacity + ranks).reshape(NEW, TOP)
    slot_ids = jnp.arange(experts_all * capacity, dtype=jnp.int32)
    selector = jnp.sum(
        (target[None, :, :] == slot_ids[:, None, None]).astype(jnp.int32), axis=2
    ).astype(jnp.bfloat16)
    send_rows = jnp.dot(selector, moe_in, preferred_element_type=jnp.float32).astype(jnp.bfloat16)
    send_rows = send_rows.reshape(experts_all, capacity, quarter)
    received = lax.all_to_all(send_rows, "seq", split_axis=0, concat_axis=1, tiled=True)
    hidden_quarter = expert_gate_up.shape[3]
    gate_up_local = expert_gate_up.reshape(local_experts, D, 2 * hidden_quarter)
    weight_rows = gate_up_local
    projected = jnp.einsum(
        "erd,edf->erf",
        lax.all_gather(received, "tp", axis=2, tiled=True),
        weight_rows,
        preferred_element_type=jnp.float32,
    )
    activated = (
        jax.nn.silu(projected[..., :hidden_quarter]) * projected[..., hidden_quarter:]
    ).astype(jnp.bfloat16)
    down_terms = jnp.einsum(
        "erf,efd->erd", activated, expert_down, preferred_element_type=jnp.float32
    )
    expert_result = lax.psum_scatter(
        down_terms.astype(jnp.bfloat16), "tp", scatter_dimension=2, tiled=True
    )
    returned = lax.all_to_all(
        expert_result, "seq", split_axis=1, concat_axis=0, tiled=True
    ).reshape(experts_all * capacity, quarter)
    picked = jnp.take(returned, target, axis=0)
    return jnp.sum(route_weights[:, :, None] * picked.astype(jnp.float32), axis=1)


def body(
    hidden,
    new_queries,
    new_keys,
    new_values,
    cache_keys,
    cache_values,
    cache_lengths,
    out_proj,
    moe_gain,
    expert_ids,
    route_weights,
    expert_gate_up,
    expert_down,
    next_gain,
    qkv_proj,
    query_gain,
    key_gain,
):
    seq_count = lax.axis_size("seq")
    here = lax.axis_index("seq")
    local_experts = expert_gate_up.shape[0]
    experts_all = local_experts * seq_count
    capacity = max(2, 3 * NEW * TOP // (2 * experts_all))
    dense = NEW <= 2 * capacity
    if dense:
        tp_here = lax.axis_index("tp")
        quarter_width = hidden.shape[1]
        tp_count = lax.axis_size("tp")
        pieces = [lax.dynamic_slice_in_dim(expert_down, tp_here * quarter_width, quarter_width, axis=2)]
        for shift in range(1, tp_count):
            target = (tp_here + shift) % tp_count
            piece = lax.dynamic_slice_in_dim(expert_down, target * quarter_width, quarter_width, axis=2)
            pairs = [(i, (i + shift) % tp_count) for i in range(tp_count)]
            pieces.append(lax.ppermute(piece, "tp", pairs))
        order = (tp_here - jnp.arange(tp_count, dtype=jnp.int32)) % tp_count
        down_full = jnp.take(jnp.stack(pieces), order, axis=0)
        down_full = jnp.transpose(down_full, (1, 0, 2, 3)).reshape(local_experts, -1, quarter_width)
        gate_up_flat = expert_gate_up.reshape(local_experts, D, -1)
        qkv_flat = qkv_proj.reshape(D, -1)
    local_width = new_queries.shape[1]
    local_heads = local_width // HEAD_DIM
    quarter = hidden.shape[1]
    span = cache_keys.shape[1]
    my_length = lax.dynamic_index_in_dim(cache_lengths, here, 0, keepdims=False)
    attended = flash_attention(
        my_length,
        new_queries,
        cache_keys.reshape(span, local_width),
        cache_values.reshape(span, local_width),
        new_keys,
        new_values,
    )
    if dense:
        attended, down_full, gate_up_flat, qkv_flat = lax.optimization_barrier(
            (attended, down_full, gate_up_flat, qkv_flat)
        )
    else:
        gate_up_flat = expert_gate_up
        qkv_flat = qkv_proj.reshape(D, -1)
    attn_term = jnp.dot(attended, out_proj, preferred_element_type=jnp.float32)
    residual = hidden.astype(jnp.float32) + lax.psum_scatter(
        attn_term.astype(jnp.bfloat16), "tp", scatter_dimension=1, tiled=True
    ).astype(jnp.float32)
    square_total = lax.psum(jnp.sum(residual * residual, axis=1), "tp")
    moe_in = (residual * lax.rsqrt(square_total / D + epsilon)[:, None] * moe_gain[None, :]).astype(
        jnp.bfloat16
    )
    if dense:
        moe_term = dense_experts(
            moe_in, expert_ids, route_weights, gate_up_flat, down_full, here, experts_all
        )
    else:
        moe_term = dispatch_experts(
            moe_in, expert_ids, route_weights, expert_gate_up, expert_down, experts_all, capacity
        )
    routed = residual + moe_term
    layer_out = routed.astype(jnp.bfloat16)
    scaled = (routed * next_gain[None, :]).astype(jnp.bfloat16)
    weight_rows = qkv_flat
    mixed = jnp.dot(
        lax.all_gather(scaled, "tp", axis=1, tiled=True),
        weight_rows,
        preferred_element_type=jnp.float32,
    )
    mixed = mixed.reshape(NEW, 3, local_width)
    squares_routed = jnp.sum(routed * routed, axis=1)
    routed_total, query_raw, key_raw = lax.psum(
        (
            squares_routed,
            jnp.sum(mixed[:, 0] * mixed[:, 0], axis=1),
            jnp.sum(mixed[:, 1] * mixed[:, 1], axis=1),
        ),
        "tp",
    )
    x_scale = lax.rsqrt(routed_total / D + epsilon)
    query_pre = mixed[:, 0] * x_scale[:, None]
    key_pre = mixed[:, 1] * x_scale[:, None]
    query_total = query_raw * x_scale * x_scale
    key_total = key_raw * x_scale * x_scale
    next_query = (
        query_pre * lax.rsqrt(query_total / D + epsilon)[:, None] * query_gain[None, :]
    ).astype(jnp.bfloat16)
    next_key = (key_pre * lax.rsqrt(key_total / D + epsilon)[:, None] * key_gain[None, :]).astype(
        jnp.bfloat16
    )
    next_value = (mixed[:, 2] * x_scale[:, None]).astype(jnp.bfloat16)
    return (layer_out, next_query, next_key, next_value)


def solution(mesh):
    return jax.shard_map(
        body,
        mesh=mesh,
        in_specs=(
            P("seq", "tp"),
            P("seq", "tp"),
            P("seq", "tp"),
            P("seq", "tp"),
            P("seq", None, "tp"),
            P("seq", None, "tp"),
            P(),
            P("tp", None),
            P("tp"),
            P("seq", None),
            P("seq", None),
            P("seq", None, None, "tp"),
            P("seq", "tp", None),
            P("tp"),
            P(None, None, "tp"),
            P("tp"),
            P("tp"),
        ),
        out_specs=(P("seq", "tp"), P("seq", "tp"), P("seq", "tp"), P("seq", "tp")),
        check_vma=False,
    )
```

```python
import functools
import math

import jax
import jax.numpy as jnp
from jax import lax
from jax.experimental import pallas as pl
from jax.experimental.pallas import tpu as pltpu
from jax.sharding import PartitionSpec as P

D = 2048
HEAD_DIM = 128
TOP = 8
NEW = 256


epsilon = 1e-05


def flash_kernel(len_ref, q_ref, k_ref, v_ref, nk_ref, nv_ref, o_ref, m_sc, l_sc, acc_sc, *, block, heads, steps):
    j = pl.program_id(0)
    length = len_ref[0]
    valid = (length + block - 1) // block
    tokens = q_ref.shape[0]
    scale = 1.0 / math.sqrt(HEAD_DIM)

    @pl.when(j == 0)
    def _():
        m_sc[...] = jnp.full(m_sc.shape, -1e30, jnp.float32)
        l_sc[...] = jnp.zeros(l_sc.shape, jnp.float32)
        acc_sc[...] = jnp.zeros(acc_sc.shape, jnp.float32)

    def update(keys_ref, values_ref, allowed):
        for h in range(heads):
            cols = slice(h * HEAD_DIM, (h + 1) * HEAD_DIM)
            q = q_ref[:, cols]
            k = keys_ref[:, cols]
            s = lax.dot_general(q, k, (((1,), (1,)), ((), ())), preferred_element_type=jnp.float32) * scale
            s = jnp.where(allowed, s, -1e30)
            m_old = m_sc[h]
            m_new = jnp.maximum(m_old, jnp.max(s, axis=1, keepdims=True))
            alpha = jnp.exp(m_old - m_new)
            p = jnp.where(allowed, jnp.exp(s - m_new), 0.0)
            l_sc[h] = alpha * l_sc[h] + jnp.sum(p, axis=1, keepdims=True)
            pv = jnp.dot(p.astype(jnp.bfloat16), values_ref[:, cols], preferred_element_type=jnp.float32)
            acc_sc[:, cols] = alpha * acc_sc[:, cols] + pv
            m_sc[h] = m_new

    @pl.when(j < valid)
    def _():
        pos = j * block + lax.broadcasted_iota(jnp.int32, (tokens, block), 1)
        update(k_ref, v_ref, pos < length)

    @pl.when(j == steps - 1)
    def _():
        row = lax.broadcasted_iota(jnp.int32, (tokens, tokens), 0)
        col = lax.broadcasted_iota(jnp.int32, (tokens, tokens), 1)
        update(nk_ref, nv_ref, col <= row)
        for h in range(heads):
            cols = slice(h * HEAD_DIM, (h + 1) * HEAD_DIM)
            o_ref[:, cols] = (acc_sc[:, cols] / l_sc[h]).astype(o_ref.dtype)


def flash_attention(length, queries, cache_k, cache_v, new_k, new_v, block=1024):
    tokens, width = queries.shape
    span = cache_k.shape[0]
    block = min(block, span)
    heads = width // HEAD_DIM
    steps = span // block + 1
    last = span // block - 1

    def cache_map(j, len_ref):
        valid = (len_ref[0] + block - 1) // block
        return (jnp.minimum(j, jnp.maximum(valid - 1, 0)), 0)

    grid_spec = pltpu.PrefetchScalarGridSpec(
        num_scalar_prefetch=1,
        grid=(steps,),
        in_specs=[
            pl.BlockSpec((tokens, width), lambda j, l: (0, 0)),
            pl.BlockSpec((block, width), cache_map),
            pl.BlockSpec((block, width), cache_map),
            pl.BlockSpec((tokens, width), lambda j, l: (0, 0)),
            pl.BlockSpec((tokens, width), lambda j, l: (0, 0)),
        ],
        out_specs=pl.BlockSpec((tokens, width), lambda j, l: (0, 0)),
        scratch_shapes=[
            pltpu.VMEM((heads, tokens, 1), jnp.float32),
            pltpu.VMEM((heads, tokens, 1), jnp.float32),
            pltpu.VMEM((tokens, width), jnp.float32),
        ],
    )
    kernel = functools.partial(flash_kernel, block=block, heads=heads, steps=steps)
    return pl.pallas_call(
        kernel,
        grid_spec=grid_spec,
        out_shape=jax.ShapeDtypeStruct((tokens, width), jnp.bfloat16),
        compiler_params=pltpu.CompilerParams(dimension_semantics=("arbitrary",)),
    )(length.reshape(1), queries, cache_k, cache_v, new_k, new_v)


def dense_experts(moe_in, expert_ids, route_weights, expert_gate_up, down_full, here, experts_all):
    local_experts = expert_gate_up.shape[0]
    hidden_quarter = expert_gate_up.shape[2] // 2
    tokens, quarter = moe_in.shape
    seq_count = experts_all // local_experts
    gate_w = jnp.sum(
        route_weights[:, :, None]
        * (expert_ids[:, :, None] == jnp.arange(experts_all, dtype=jnp.int32)[None, None, :]),
        axis=1,
    )
    gate_t = jnp.transpose(gate_w)
    gate_hi = gate_t.astype(jnp.bfloat16)
    gate_lo = (gate_t - gate_hi.astype(jnp.float32)).astype(jnp.bfloat16)
    info = jnp.concatenate([gate_hi, gate_lo], axis=0).reshape(-1, quarter)
    packed = jnp.concatenate([moe_in, info], axis=0)
    gathered = lax.all_gather(packed, "seq", axis=0, tiled=False)
    rows_q = gathered[:, :tokens].reshape(seq_count * tokens, quarter)
    info_all = gathered[:, tokens:].reshape(seq_count, 2, experts_all, tokens).astype(jnp.float32)
    gate_all = info_all[:, 0] + info_all[:, 1]
    gate_local = lax.dynamic_slice_in_dim(gate_all, here * local_experts, local_experts, axis=1)
    gate_local = jnp.transpose(gate_local, (1, 0, 2)).reshape(local_experts, seq_count * tokens)
    rows = lax.all_gather(rows_q, "tp", axis=1, tiled=True)
    projected = jnp.einsum("td,edf->etf", rows, expert_gate_up, preferred_element_type=jnp.float32)
    activated = jax.nn.silu(projected[..., :hidden_quarter]) * projected[..., hidden_quarter:]
    activated = activated.astype(jnp.bfloat16).astype(jnp.float32)
    weighted = (activated * gate_local[:, :, None]).astype(jnp.bfloat16)
    weighted = lax.all_gather(weighted, "tp", axis=2, tiled=True)
    partial = jnp.einsum(
        "etf,efd->td", weighted, down_full, preferred_element_type=jnp.float32
    ).astype(jnp.bfloat16)
    return ring_reduce_scatter(partial, here, seq_count)


def ring_reduce_scatter(partial, here, count):
    half = count // 2
    cycle = [2 * i for i in range(half)] + [2 * i + 1 for i in reversed(range(half))]
    if count % 2 or count < 4:
        cycle = list(range(count))
    place = [0] * count
    for p, device in enumerate(cycle):
        place[device] = p
    cycle_arr = jnp.array(cycle, jnp.int32)
    pos = jnp.array(place, jnp.int32)[here]
    tokens = partial.shape[0] // count
    width = partial.shape[1]
    blocks = partial.reshape(count, tokens, width)
    halves = []
    for direction in (1, -1):
        cols = slice(0, width // 2) if direction == 1 else slice(width // 2, width)
        pairs = [(cycle[p], cycle[(p + direction) % count]) for p in range(count)]

        def block_for(q, cols=cols):
            device = cycle_arr[q % count]
            return lax.dynamic_index_in_dim(blocks, device, 0, keepdims=False)[:, cols].astype(jnp.float32)

        acc = block_for(pos - direction)
        for step in range(count - 1):
            received = lax.ppermute(acc.astype(jnp.bfloat16), "seq", pairs)
            acc = received.astype(jnp.float32) + block_for(pos - direction * (step + 2))
        halves.append(acc)
    return jnp.concatenate(halves, axis=1)


def dispatch_experts(moe_in, expert_ids, route_weights, expert_gate_up, expert_down, experts_all, capacity):
    quarter = moe_in.shape[1]
    local_experts = expert_gate_up.shape[0]
    flat_ids = expert_ids.reshape(NEW * TOP)
    onehot = (flat_ids[:, None] == jnp.arange(experts_all, dtype=jnp.int32)[None, :]).astype(
        jnp.int32
    )
    ranks = jnp.sum((jnp.cumsum(onehot, axis=0) - onehot) * onehot, axis=1)
    target = (flat_ids * capacity + ranks).reshape(NEW, TOP)
    slot_ids = jnp.arange(experts_all * capacity, dtype=jnp.int32)
    selector = jnp.sum(
        (target[None, :, :] == slot_ids[:, None, None]).astype(jnp.int32), axis=2
    ).astype(jnp.bfloat16)
    send_rows = jnp.dot(selector, moe_in, preferred_element_type=jnp.float32).astype(jnp.bfloat16)
    send_rows = send_rows.reshape(experts_all, capacity, quarter)
    received = lax.all_to_all(send_rows, "seq", split_axis=0, concat_axis=1, tiled=True)
    hidden_quarter = expert_gate_up.shape[3]
    gate_up_local = expert_gate_up.reshape(local_experts, D, 2 * hidden_quarter)
    weight_rows = gate_up_local
    projected = jnp.einsum(
        "erd,edf->erf",
        lax.all_gather(received, "tp", axis=2, tiled=True),
        weight_rows,
        preferred_element_type=jnp.float32,
    )
    activated = (
        jax.nn.silu(projected[..., :hidden_quarter]) * projected[..., hidden_quarter:]
    ).astype(jnp.bfloat16)
    down_terms = jnp.einsum(
        "erf,efd->erd", activated, expert_down, preferred_element_type=jnp.float32
    )
    expert_result = lax.psum_scatter(
        down_terms.astype(jnp.bfloat16), "tp", scatter_dimension=2, tiled=True
    )
    returned = lax.all_to_all(
        expert_result, "seq", split_axis=1, concat_axis=0, tiled=True
    ).reshape(experts_all * capacity, quarter)
    picked = jnp.take(returned, target, axis=0)
    return jnp.sum(route_weights[:, :, None] * picked.astype(jnp.float32), axis=1)


def body(
    hidden,
    new_queries,
    new_keys,
    new_values,
    cache_keys,
    cache_values,
    cache_lengths,
    out_proj,
    moe_gain,
    expert_ids,
    route_weights,
    expert_gate_up,
    expert_down,
    next_gain,
    qkv_proj,
    query_gain,
    key_gain,
):
    seq_count = lax.axis_size("seq")
    here = lax.axis_index("seq")
    local_experts = expert_gate_up.shape[0]
    experts_all = local_experts * seq_count
    capacity = max(2, 3 * NEW * TOP // (2 * experts_all))
    dense = NEW <= 2 * capacity
    if dense:
        tp_here = lax.axis_index("tp")
        quarter_width = hidden.shape[1]
        tp_count = lax.axis_size("tp")
        pieces = [lax.dynamic_slice_in_dim(expert_down, tp_here * quarter_width, quarter_width, axis=2)]
        for shift in range(1, tp_count):
            target = (tp_here + shift) % tp_count
            piece = lax.dynamic_slice_in_dim(expert_down, target * quarter_width, quarter_width, axis=2)
            pairs = [(i, (i + shift) % tp_count) for i in range(tp_count)]
            pieces.append(lax.ppermute(piece, "tp", pairs))
        order = (tp_here - jnp.arange(tp_count, dtype=jnp.int32)) % tp_count
        down_full = jnp.take(jnp.stack(pieces), order, axis=0)
        down_full = jnp.transpose(down_full, (1, 0, 2, 3)).reshape(local_experts, -1, quarter_width)
        gate_up_flat = expert_gate_up.reshape(local_experts, D, -1)
        qkv_flat = qkv_proj.reshape(D, -1)
    local_width = new_queries.shape[1]
    local_heads = local_width // HEAD_DIM
    quarter = hidden.shape[1]
    span = cache_keys.shape[1]
    my_length = lax.dynamic_index_in_dim(cache_lengths, here, 0, keepdims=False)
    attended = flash_attention(
        my_length,
        new_queries,
        cache_keys.reshape(span, local_width),
        cache_values.reshape(span, local_width),
        new_keys,
        new_values,
    )
    if dense:
        attended, down_full, gate_up_flat, qkv_flat = lax.optimization_barrier(
            (attended, down_full, gate_up_flat, qkv_flat)
        )
    else:
        gate_up_flat = expert_gate_up
        qkv_flat = qkv_proj.reshape(D, -1)
    attn_term = jnp.dot(attended, out_proj, preferred_element_type=jnp.float32)
    residual = hidden.astype(jnp.float32) + lax.psum_scatter(
        attn_term.astype(jnp.bfloat16), "tp", scatter_dimension=1, tiled=True
    ).astype(jnp.float32)
    square_total = lax.psum(jnp.sum(residual * residual, axis=1), "tp")
    moe_in = (residual * lax.rsqrt(square_total / D + epsilon)[:, None] * moe_gain[None, :]).astype(
        jnp.bfloat16
    )
    if dense:
        moe_term = dense_experts(
            moe_in, expert_ids, route_weights, gate_up_flat, down_full, here, experts_all
        )
    else:
        moe_term = dispatch_experts(
            moe_in, expert_ids, route_weights, expert_gate_up, expert_down, experts_all, capacity
        )
    routed = residual + moe_term
    layer_out = routed.astype(jnp.bfloat16)
    scaled = (routed * next_gain[None, :]).astype(jnp.bfloat16)
    weight_rows = qkv_flat
    mixed = jnp.dot(
        lax.all_gather(scaled, "tp", axis=1, tiled=True),
        weight_rows,
        preferred_element_type=jnp.float32,
    )
    mixed = mixed.reshape(NEW, 3, local_width)
    squares_routed = jnp.sum(routed * routed, axis=1)
    routed_total, query_raw, key_raw = lax.psum(
        (
            squares_routed,
            jnp.sum(mixed[:, 0] * mixed[:, 0], axis=1),
            jnp.sum(mixed[:, 1] * mixed[:, 1], axis=1),
        ),
        "tp",
    )
    x_scale = lax.rsqrt(routed_total / D + epsilon)
    query_pre = mixed[:, 0] * x_scale[:, None]
    key_pre = mixed[:, 1] * x_scale[:, None]
    query_total = query_raw * x_scale * x_scale
    key_total = key_raw * x_scale * x_scale
    next_query = (
        query_pre * lax.rsqrt(query_total / D + epsilon)[:, None] * query_gain[None, :]
    ).astype(jnp.bfloat16)
    next_key = (key_pre * lax.rsqrt(key_total / D + epsilon)[:, None] * key_gain[None, :]).astype(
        jnp.bfloat16
    )
    next_value = (mixed[:, 2] * x_scale[:, None]).astype(jnp.bfloat16)
    return (layer_out, next_query, next_key, next_value)


def solution(mesh):
    return jax.shard_map(
        body,
        mesh=mesh,
        in_specs=(
            P("seq", "tp"),
            P("seq", "tp"),
            P("seq", "tp"),
            P("seq", "tp"),
            P("seq", None, "tp"),
            P("seq", None, "tp"),
            P(),
            P("tp", None),
            P("tp"),
            P("seq", None),
            P("seq", None),
            P("seq", None, None, "tp"),
            P("seq", "tp", None),
            P("tp"),
            P(None, None, "tp"),
            P("tp"),
            P("tp"),
        ),
        out_specs=(P("seq", "tp"), P("seq", "tp"), P("seq", "tp"), P("seq", "tp")),
        check_vma=False,
    )
```

```python
import functools
import math

import jax
import jax.numpy as jnp
from jax import lax
from jax.experimental import pallas as pl
from jax.experimental.pallas import tpu as pltpu
from jax.sharding import PartitionSpec as P

D = 2048
HEAD_DIM = 128
TOP = 8
NEW = 256


epsilon = 1e-05


def flash_kernel(len_ref, q_ref, k_ref, v_ref, nk_ref, nv_ref, o_ref, m_sc, l_sc, acc_sc, *, block, heads, steps):
    j = pl.program_id(0)
    length = len_ref[0]
    valid = (length + block - 1) // block
    tokens = q_ref.shape[0]
    scale = 1.0 / math.sqrt(HEAD_DIM)

    @pl.when(j == 0)
    def _():
        m_sc[...] = jnp.full(m_sc.shape, -1e30, jnp.float32)
        l_sc[...] = jnp.zeros(l_sc.shape, jnp.float32)
        acc_sc[...] = jnp.zeros(acc_sc.shape, jnp.float32)

    def update(keys_ref, values_ref, allowed):
        for h in range(heads):
            cols = slice(h * HEAD_DIM, (h + 1) * HEAD_DIM)
            q = q_ref[:, cols]
            k = keys_ref[:, cols]
            s = lax.dot_general(q, k, (((1,), (1,)), ((), ())), preferred_element_type=jnp.float32) * scale
            s = jnp.where(allowed, s, -1e30)
            m_old = m_sc[h]
            m_new = jnp.maximum(m_old, jnp.max(s, axis=1, keepdims=True))
            alpha = jnp.exp(m_old - m_new)
            p = jnp.where(allowed, jnp.exp(s - m_new), 0.0)
            l_sc[h] = alpha * l_sc[h] + jnp.sum(p, axis=1, keepdims=True)
            pv = jnp.dot(p.astype(jnp.bfloat16), values_ref[:, cols], preferred_element_type=jnp.float32)
            acc_sc[:, cols] = alpha * acc_sc[:, cols] + pv
            m_sc[h] = m_new

    @pl.when(j < valid)
    def _():
        pos = j * block + lax.broadcasted_iota(jnp.int32, (tokens, block), 1)
        update(k_ref, v_ref, pos < length)

    @pl.when(j == steps - 1)
    def _():
        row = lax.broadcasted_iota(jnp.int32, (tokens, tokens), 0)
        col = lax.broadcasted_iota(jnp.int32, (tokens, tokens), 1)
        update(nk_ref, nv_ref, col <= row)
        for h in range(heads):
            cols = slice(h * HEAD_DIM, (h + 1) * HEAD_DIM)
            o_ref[:, cols] = (acc_sc[:, cols] / l_sc[h]).astype(o_ref.dtype)


def flash_attention(length, queries, cache_k, cache_v, new_k, new_v, block=1024):
    tokens, width = queries.shape
    span = cache_k.shape[0]
    block = min(block, span)
    heads = width // HEAD_DIM
    steps = span // block + 1
    last = span // block - 1

    def cache_map(j, len_ref):
        valid = (len_ref[0] + block - 1) // block
        return (jnp.minimum(j, jnp.maximum(valid - 1, 0)), 0)

    grid_spec = pltpu.PrefetchScalarGridSpec(
        num_scalar_prefetch=1,
        grid=(steps,),
        in_specs=[
            pl.BlockSpec((tokens, width), lambda j, l: (0, 0)),
            pl.BlockSpec((block, width), cache_map),
            pl.BlockSpec((block, width), cache_map),
            pl.BlockSpec((tokens, width), lambda j, l: (0, 0)),
            pl.BlockSpec((tokens, width), lambda j, l: (0, 0)),
        ],
        out_specs=pl.BlockSpec((tokens, width), lambda j, l: (0, 0)),
        scratch_shapes=[
            pltpu.VMEM((heads, tokens, 1), jnp.float32),
            pltpu.VMEM((heads, tokens, 1), jnp.float32),
            pltpu.VMEM((tokens, width), jnp.float32),
        ],
    )
    kernel = functools.partial(flash_kernel, block=block, heads=heads, steps=steps)
    return pl.pallas_call(
        kernel,
        grid_spec=grid_spec,
        out_shape=jax.ShapeDtypeStruct((tokens, width), jnp.bfloat16),
        compiler_params=pltpu.CompilerParams(dimension_semantics=("arbitrary",)),
    )(length.reshape(1), queries, cache_k, cache_v, new_k, new_v)


def dense_experts(moe_in, expert_ids, route_weights, expert_gate_up, down_full, here, experts_all):
    local_experts = expert_gate_up.shape[0]
    hidden_quarter = expert_gate_up.shape[2] // 2
    tokens, quarter = moe_in.shape
    seq_count = experts_all // local_experts
    gate_w = jnp.sum(
        route_weights[:, :, None]
        * (expert_ids[:, :, None] == jnp.arange(experts_all, dtype=jnp.int32)[None, None, :]),
        axis=1,
    )
    gate_t = jnp.transpose(gate_w)
    gate_hi = gate_t.astype(jnp.bfloat16)
    gate_lo = (gate_t - gate_hi.astype(jnp.float32)).astype(jnp.bfloat16)
    info = jnp.concatenate([gate_hi, gate_lo], axis=0).reshape(-1, quarter)
    packed = jnp.concatenate([moe_in, info], axis=0)
    ring = ring_order(seq_count)
    gathered = ring_all_gather(packed, here, ring)
    rows_q = gathered[:, :tokens].reshape(seq_count * tokens, quarter)
    info_all = gathered[:, tokens:].reshape(seq_count, 2, experts_all, tokens).astype(jnp.float32)
    gate_all = info_all[:, 0] + info_all[:, 1]
    gate_local = lax.dynamic_slice_in_dim(gate_all, here * local_experts, local_experts, axis=1)
    gate_local = jnp.transpose(gate_local, (1, 0, 2)).reshape(local_experts, seq_count * tokens)
    rows = lax.all_gather(rows_q, "tp", axis=1, tiled=True)
    projected = jnp.einsum("td,edf->etf", rows, expert_gate_up, preferred_element_type=jnp.float32)
    activated = jax.nn.silu(projected[..., :hidden_quarter]) * projected[..., hidden_quarter:]
    activated = activated.astype(jnp.bfloat16).astype(jnp.float32)
    weighted = (activated * gate_local[:, :, None]).astype(jnp.bfloat16)
    weighted = lax.all_gather(weighted, "tp", axis=2, tiled=True)
    partial = jnp.einsum(
        "etf,efd->td", weighted, down_full, preferred_element_type=jnp.float32
    ).astype(jnp.bfloat16)
    return ring_reduce_scatter(partial, ring)


def ring_order(count):
    half = count // 2
    if count % 2 or count < 4:
        return list(range(count))
    return [2 * i for i in range(half)] + [2 * i + 1 for i in reversed(range(half))]


def ring_all_gather(block, here, cycle):
    count = len(cycle)
    forward = [(cycle[p], cycle[(p + 1) % count]) for p in range(count)]
    backward = [(cycle[p], cycle[(p - 1) % count]) for p in range(count)]
    by_offset = [block] * count
    ahead = block
    for step in range(1, count // 2 + 1):
        ahead = lax.ppermute(ahead, "seq", forward)
        by_offset[(-step) % count] = ahead
    behind = block
    for step in range(1, count - count // 2):
        behind = lax.ppermute(behind, "seq", backward)
        by_offset[step] = behind
    return jnp.stack(by_offset)


def ring_reduce_scatter(partial, cycle):
    count = len(cycle)
    tokens = partial.shape[0] // count
    width = partial.shape[1]
    blocks = partial.reshape(count, tokens, width)
    halves = []
    for direction in (1, -1):
        cols = slice(0, width // 2) if direction == 1 else slice(width // 2, width)
        pairs = [(cycle[p], cycle[(p + direction) % count]) for p in range(count)]
        acc = blocks[(-direction) % count, :, cols].astype(jnp.float32)
        for step in range(count - 1):
            received = lax.ppermute(acc.astype(jnp.bfloat16), "seq", pairs)
            offset = (-direction * (step + 2)) % count
            acc = received.astype(jnp.float32) + blocks[offset, :, cols].astype(jnp.float32)
        halves.append(acc)
    return jnp.concatenate(halves, axis=1)


def dispatch_experts(moe_in, expert_ids, route_weights, expert_gate_up, expert_down, experts_all, capacity):
    quarter = moe_in.shape[1]
    local_experts = expert_gate_up.shape[0]
    flat_ids = expert_ids.reshape(NEW * TOP)
    onehot = (flat_ids[:, None] == jnp.arange(experts_all, dtype=jnp.int32)[None, :]).astype(
        jnp.int32
    )
    ranks = jnp.sum((jnp.cumsum(onehot, axis=0) - onehot) * onehot, axis=1)
    target = (flat_ids * capacity + ranks).reshape(NEW, TOP)
    slot_ids = jnp.arange(experts_all * capacity, dtype=jnp.int32)
    selector = jnp.sum(
        (target[None, :, :] == slot_ids[:, None, None]).astype(jnp.int32), axis=2
    ).astype(jnp.bfloat16)
    send_rows = jnp.dot(selector, moe_in, preferred_element_type=jnp.float32).astype(jnp.bfloat16)
    send_rows = send_rows.reshape(experts_all, capacity, quarter)
    received = lax.all_to_all(send_rows, "seq", split_axis=0, concat_axis=1, tiled=True)
    hidden_quarter = expert_gate_up.shape[3]
    gate_up_local = expert_gate_up.reshape(local_experts, D, 2 * hidden_quarter)
    weight_rows = gate_up_local
    projected = jnp.einsum(
        "erd,edf->erf",
        lax.all_gather(received, "tp", axis=2, tiled=True),
        weight_rows,
        preferred_element_type=jnp.float32,
    )
    activated = (
        jax.nn.silu(projected[..., :hidden_quarter]) * projected[..., hidden_quarter:]
    ).astype(jnp.bfloat16)
    down_terms = jnp.einsum(
        "erf,efd->erd", activated, expert_down, preferred_element_type=jnp.float32
    )
    expert_result = lax.psum_scatter(
        down_terms.astype(jnp.bfloat16), "tp", scatter_dimension=2, tiled=True
    )
    returned = lax.all_to_all(
        expert_result, "seq", split_axis=1, concat_axis=0, tiled=True
    ).reshape(experts_all * capacity, quarter)
    picked = jnp.take(returned, target, axis=0)
    return jnp.sum(route_weights[:, :, None] * picked.astype(jnp.float32), axis=1)


def body(
    hidden,
    new_queries,
    new_keys,
    new_values,
    cache_keys,
    cache_values,
    cache_lengths,
    out_proj,
    moe_gain,
    expert_ids,
    route_weights,
    expert_gate_up,
    expert_down,
    next_gain,
    qkv_proj,
    query_gain,
    key_gain,
):
    seq_count = lax.axis_size("seq")
    here = lax.axis_index("seq")
    local_experts = expert_gate_up.shape[0]
    experts_all = local_experts * seq_count
    capacity = max(2, 3 * NEW * TOP // (2 * experts_all))
    dense = NEW <= 2 * capacity
    if dense:
        tp_here = lax.axis_index("tp")
        quarter_width = hidden.shape[1]
        tp_count = lax.axis_size("tp")
        pieces = [lax.dynamic_slice_in_dim(expert_down, tp_here * quarter_width, quarter_width, axis=2)]
        for shift in range(1, tp_count):
            target = (tp_here + shift) % tp_count
            piece = lax.dynamic_slice_in_dim(expert_down, target * quarter_width, quarter_width, axis=2)
            pairs = [(i, (i + shift) % tp_count) for i in range(tp_count)]
            pieces.append(lax.ppermute(piece, "tp", pairs))
        order = (tp_here - jnp.arange(tp_count, dtype=jnp.int32)) % tp_count
        down_full = jnp.take(jnp.stack(pieces), order, axis=0)
        down_full = jnp.transpose(down_full, (1, 0, 2, 3)).reshape(local_experts, -1, quarter_width)
        gate_up_flat = expert_gate_up.reshape(local_experts, D, -1)
        qkv_flat = qkv_proj.reshape(D, -1)
    local_width = new_queries.shape[1]
    local_heads = local_width // HEAD_DIM
    quarter = hidden.shape[1]
    span = cache_keys.shape[1]
    my_length = lax.dynamic_index_in_dim(cache_lengths, here, 0, keepdims=False)
    attended = flash_attention(
        my_length,
        new_queries,
        cache_keys.reshape(span, local_width),
        cache_values.reshape(span, local_width),
        new_keys,
        new_values,
    )
    if dense:
        attended, down_full, gate_up_flat, qkv_flat = lax.optimization_barrier(
            (attended, down_full, gate_up_flat, qkv_flat)
        )
    else:
        gate_up_flat = expert_gate_up
        qkv_flat = qkv_proj.reshape(D, -1)
    attn_term = jnp.dot(attended, out_proj, preferred_element_type=jnp.float32)
    residual = hidden.astype(jnp.float32) + lax.psum_scatter(
        attn_term.astype(jnp.bfloat16), "tp", scatter_dimension=1, tiled=True
    ).astype(jnp.float32)
    square_total = lax.psum(jnp.sum(residual * residual, axis=1), "tp")
    moe_in = (residual * lax.rsqrt(square_total / D + epsilon)[:, None] * moe_gain[None, :]).astype(
        jnp.bfloat16
    )
    if dense:
        moe_term = dense_experts(
            moe_in, expert_ids, route_weights, gate_up_flat, down_full, here, experts_all
        )
    else:
        moe_term = dispatch_experts(
            moe_in, expert_ids, route_weights, expert_gate_up, expert_down, experts_all, capacity
        )
    routed = residual + moe_term
    layer_out = routed.astype(jnp.bfloat16)
    scaled = (routed * next_gain[None, :]).astype(jnp.bfloat16)
    weight_rows = qkv_flat
    mixed = jnp.dot(
        lax.all_gather(scaled, "tp", axis=1, tiled=True),
        weight_rows,
        preferred_element_type=jnp.float32,
    )
    mixed = mixed.reshape(NEW, 3, local_width)
    squares_routed = jnp.sum(routed * routed, axis=1)
    routed_total, query_raw, key_raw = lax.psum(
        (
            squares_routed,
            jnp.sum(mixed[:, 0] * mixed[:, 0], axis=1),
            jnp.sum(mixed[:, 1] * mixed[:, 1], axis=1),
        ),
        "tp",
    )
    x_scale = lax.rsqrt(routed_total / D + epsilon)
    query_pre = mixed[:, 0] * x_scale[:, None]
    key_pre = mixed[:, 1] * x_scale[:, None]
    query_total = query_raw * x_scale * x_scale
    key_total = key_raw * x_scale * x_scale
    next_query = (
        query_pre * lax.rsqrt(query_total / D + epsilon)[:, None] * query_gain[None, :]
    ).astype(jnp.bfloat16)
    next_key = (key_pre * lax.rsqrt(key_total / D + epsilon)[:, None] * key_gain[None, :]).astype(
        jnp.bfloat16
    )
    next_value = (mixed[:, 2] * x_scale[:, None]).astype(jnp.bfloat16)
    return (layer_out, next_query, next_key, next_value)


def solution(mesh):
    return jax.shard_map(
        body,
        mesh=mesh,
        in_specs=(
            P("seq", "tp"),
            P("seq", "tp"),
            P("seq", "tp"),
            P("seq", "tp"),
            P("seq", None, "tp"),
            P("seq", None, "tp"),
            P(),
            P("tp", None),
            P("tp"),
            P("seq", None),
            P("seq", None),
            P("seq", None, None, "tp"),
            P("seq", "tp", None),
            P("tp"),
            P(None, None, "tp"),
            P("tp"),
            P("tp"),
        ),
        out_specs=(P("seq", "tp"), P("seq", "tp"), P("seq", "tp"), P("seq", "tp")),
        check_vma=False,
    )
```

```python
import functools
import math

import jax
import jax.numpy as jnp
from jax import lax
from jax.experimental import pallas as pl
from jax.experimental.pallas import tpu as pltpu
from jax.sharding import PartitionSpec as P

D = 2048
HEAD_DIM = 128
TOP = 8
NEW = 256


epsilon = 1e-05


def flash_kernel(len_ref, q_ref, k_ref, v_ref, nk_ref, nv_ref, o_ref, m_sc, l_sc, acc_sc, *, block, heads, steps):
    j = pl.program_id(0)
    length = len_ref[0]
    valid = (length + block - 1) // block
    tokens = q_ref.shape[0]
    scale = 1.0 / math.sqrt(HEAD_DIM)

    @pl.when(j == 0)
    def _():
        m_sc[...] = jnp.full(m_sc.shape, -1e30, jnp.float32)
        l_sc[...] = jnp.zeros(l_sc.shape, jnp.float32)
        acc_sc[...] = jnp.zeros(acc_sc.shape, jnp.float32)

    def update(keys_ref, values_ref, allowed):
        for h in range(heads):
            cols = slice(h * HEAD_DIM, (h + 1) * HEAD_DIM)
            q = q_ref[:, cols]
            k = keys_ref[:, cols]
            s = lax.dot_general(q, k, (((1,), (1,)), ((), ())), preferred_element_type=jnp.float32) * scale
            s = jnp.where(allowed, s, -1e30)
            m_old = m_sc[h]
            m_new = jnp.maximum(m_old, jnp.max(s, axis=1, keepdims=True))
            alpha = jnp.exp(m_old - m_new)
            p = jnp.where(allowed, jnp.exp(s - m_new), 0.0)
            l_sc[h] = alpha * l_sc[h] + jnp.sum(p, axis=1, keepdims=True)
            pv = jnp.dot(p.astype(jnp.bfloat16), values_ref[:, cols], preferred_element_type=jnp.float32)
            acc_sc[:, cols] = alpha * acc_sc[:, cols] + pv
            m_sc[h] = m_new

    @pl.when(j < valid)
    def _():
        pos = j * block + lax.broadcasted_iota(jnp.int32, (tokens, block), 1)
        update(k_ref, v_ref, pos < length)

    @pl.when(j == steps - 1)
    def _():
        row = lax.broadcasted_iota(jnp.int32, (tokens, tokens), 0)
        col = lax.broadcasted_iota(jnp.int32, (tokens, tokens), 1)
        update(nk_ref, nv_ref, col <= row)
        for h in range(heads):
            cols = slice(h * HEAD_DIM, (h + 1) * HEAD_DIM)
            o_ref[:, cols] = (acc_sc[:, cols] / l_sc[h]).astype(o_ref.dtype)


def flash_attention(length, queries, cache_k, cache_v, new_k, new_v, block=1024):
    tokens, width = queries.shape
    span = cache_k.shape[0]
    block = min(block, span)
    heads = width // HEAD_DIM
    steps = span // block + 1
    last = span // block - 1

    def cache_map(j, len_ref):
        valid = (len_ref[0] + block - 1) // block
        return (jnp.minimum(j, jnp.maximum(valid - 1, 0)), 0)

    grid_spec = pltpu.PrefetchScalarGridSpec(
        num_scalar_prefetch=1,
        grid=(steps,),
        in_specs=[
            pl.BlockSpec((tokens, width), lambda j, l: (0, 0)),
            pl.BlockSpec((block, width), cache_map),
            pl.BlockSpec((block, width), cache_map),
            pl.BlockSpec((tokens, width), lambda j, l: (0, 0)),
            pl.BlockSpec((tokens, width), lambda j, l: (0, 0)),
        ],
        out_specs=pl.BlockSpec((tokens, width), lambda j, l: (0, 0)),
        scratch_shapes=[
            pltpu.VMEM((heads, tokens, 1), jnp.float32),
            pltpu.VMEM((heads, tokens, 1), jnp.float32),
            pltpu.VMEM((tokens, width), jnp.float32),
        ],
    )
    kernel = functools.partial(flash_kernel, block=block, heads=heads, steps=steps)
    return pl.pallas_call(
        kernel,
        grid_spec=grid_spec,
        out_shape=jax.ShapeDtypeStruct((tokens, width), jnp.bfloat16),
        compiler_params=pltpu.CompilerParams(dimension_semantics=("arbitrary",)),
    )(length.reshape(1), queries, cache_k, cache_v, new_k, new_v)


def dense_experts(moe_in, expert_ids, route_weights, expert_gate_up, down_full, here, experts_all):
    local_experts = expert_gate_up.shape[0]
    hidden_quarter = expert_gate_up.shape[2] // 2
    tokens, quarter = moe_in.shape
    seq_count = experts_all // local_experts
    gate_w = jnp.sum(
        route_weights[:, :, None]
        * (expert_ids[:, :, None] == jnp.arange(experts_all, dtype=jnp.int32)[None, None, :]),
        axis=1,
    )
    gate_t = jnp.transpose(gate_w)
    gate_hi = gate_t.astype(jnp.bfloat16)
    gate_lo = (gate_t - gate_hi.astype(jnp.float32)).astype(jnp.bfloat16)
    info = jnp.concatenate([gate_hi, gate_lo], axis=0).reshape(-1, quarter)
    packed = jnp.concatenate([moe_in, info], axis=0)
    ring = ring_order(seq_count)
    offsets, blocks = ring_all_gather(packed, ring)
    first = min(len(blocks), 5)
    chunks = [(0, first), (first, len(blocks))] if first < len(blocks) else [(0, first)]
    outputs = []
    for begin, end in chunks:
        gathered = jnp.stack(blocks[begin:end])
        count = end - begin
        rows_q = gathered[:, :tokens].reshape(count * tokens, quarter)
        info_all = gathered[:, tokens:].reshape(count, 2, experts_all, tokens).astype(jnp.float32)
        gate_all = info_all[:, 0] + info_all[:, 1]
        gate_local = lax.dynamic_slice_in_dim(gate_all, here * local_experts, local_experts, axis=1)
        gate_local = jnp.transpose(gate_local, (1, 0, 2)).reshape(local_experts, count * tokens)
        rows = lax.all_gather(rows_q, "tp", axis=1, tiled=True)
        projected = jnp.einsum("td,edf->etf", rows, expert_gate_up, preferred_element_type=jnp.float32)
        activated = jax.nn.silu(projected[..., :hidden_quarter]) * projected[..., hidden_quarter:]
        activated = activated.astype(jnp.bfloat16).astype(jnp.float32)
        weighted = (activated * gate_local[:, :, None]).astype(jnp.bfloat16)
        weighted = lax.all_gather(weighted, "tp", axis=2, tiled=True)
        partial = jnp.einsum(
            "etf,efd->td", weighted, down_full, preferred_element_type=jnp.float32
        ).astype(jnp.bfloat16)
        outputs.append(partial.reshape(count, tokens, -1))
    by_offset = {}
    index = 0
    for part in outputs:
        for i in range(part.shape[0]):
            by_offset[offsets[index]] = part[i]
            index += 1
    return ring_reduce_scatter(by_offset, ring)


def ring_order(count):
    half = count // 2
    if count % 2 or count < 4:
        return list(range(count))
    return [2 * i for i in range(half)] + [2 * i + 1 for i in reversed(range(half))]


def ring_all_gather(block, cycle):
    count = len(cycle)
    forward = [(cycle[p], cycle[(p + 1) % count]) for p in range(count)]
    backward = [(cycle[p], cycle[(p - 1) % count]) for p in range(count)]
    offsets, blocks = [0], [block]
    ahead, behind = block, block
    for step in range(1, count // 2 + 1):
        ahead = lax.ppermute(ahead, "seq", forward)
        offsets.append((-step) % count)
        blocks.append(ahead)
        if step < count - count // 2:
            behind = lax.ppermute(behind, "seq", backward)
            offsets.append(step)
            blocks.append(behind)
    return offsets, blocks


def ring_reduce_scatter(by_offset, cycle):
    count = len(cycle)
    width = by_offset[0].shape[1]
    halves = []
    for direction in (1, -1):
        cols = slice(0, width // 2) if direction == 1 else slice(width // 2, width)
        pairs = [(cycle[p], cycle[(p + direction) % count]) for p in range(count)]
        acc = by_offset[(-direction) % count][:, cols].astype(jnp.float32)
        for step in range(count - 1):
            received = lax.ppermute(acc.astype(jnp.bfloat16), "seq", pairs)
            offset = (-direction * (step + 2)) % count
            acc = received.astype(jnp.float32) + by_offset[offset][:, cols].astype(jnp.float32)
        halves.append(acc)
    return jnp.concatenate(halves, axis=1)


def dispatch_experts(moe_in, expert_ids, route_weights, expert_gate_up, expert_down, experts_all, capacity):
    quarter = moe_in.shape[1]
    local_experts = expert_gate_up.shape[0]
    flat_ids = expert_ids.reshape(NEW * TOP)
    onehot = (flat_ids[:, None] == jnp.arange(experts_all, dtype=jnp.int32)[None, :]).astype(
        jnp.int32
    )
    ranks = jnp.sum((jnp.cumsum(onehot, axis=0) - onehot) * onehot, axis=1)
    target = (flat_ids * capacity + ranks).reshape(NEW, TOP)
    slot_ids = jnp.arange(experts_all * capacity, dtype=jnp.int32)
    selector = jnp.sum(
        (target[None, :, :] == slot_ids[:, None, None]).astype(jnp.int32), axis=2
    ).astype(jnp.bfloat16)
    send_rows = jnp.dot(selector, moe_in, preferred_element_type=jnp.float32).astype(jnp.bfloat16)
    send_rows = send_rows.reshape(experts_all, capacity, quarter)
    received = lax.all_to_all(send_rows, "seq", split_axis=0, concat_axis=1, tiled=True)
    hidden_quarter = expert_gate_up.shape[3]
    gate_up_local = expert_gate_up.reshape(local_experts, D, 2 * hidden_quarter)
    weight_rows = gate_up_local
    projected = jnp.einsum(
        "erd,edf->erf",
        lax.all_gather(received, "tp", axis=2, tiled=True),
        weight_rows,
        preferred_element_type=jnp.float32,
    )
    activated = (
        jax.nn.silu(projected[..., :hidden_quarter]) * projected[..., hidden_quarter:]
    ).astype(jnp.bfloat16)
    down_terms = jnp.einsum(
        "erf,efd->erd", activated, expert_down, preferred_element_type=jnp.float32
    )
    expert_result = lax.psum_scatter(
        down_terms.astype(jnp.bfloat16), "tp", scatter_dimension=2, tiled=True
    )
    returned = lax.all_to_all(
        expert_result, "seq", split_axis=1, concat_axis=0, tiled=True
    ).reshape(experts_all * capacity, quarter)
    picked = jnp.take(returned, target, axis=0)
    return jnp.sum(route_weights[:, :, None] * picked.astype(jnp.float32), axis=1)


def body(
    hidden,
    new_queries,
    new_keys,
    new_values,
    cache_keys,
    cache_values,
    cache_lengths,
    out_proj,
    moe_gain,
    expert_ids,
    route_weights,
    expert_gate_up,
    expert_down,
    next_gain,
    qkv_proj,
    query_gain,
    key_gain,
):
    seq_count = lax.axis_size("seq")
    here = lax.axis_index("seq")
    local_experts = expert_gate_up.shape[0]
    experts_all = local_experts * seq_count
    capacity = max(2, 3 * NEW * TOP // (2 * experts_all))
    dense = NEW <= 2 * capacity
    if dense:
        tp_here = lax.axis_index("tp")
        quarter_width = hidden.shape[1]
        tp_count = lax.axis_size("tp")
        pieces = [lax.dynamic_slice_in_dim(expert_down, tp_here * quarter_width, quarter_width, axis=2)]
        for shift in range(1, tp_count):
            target = (tp_here + shift) % tp_count
            piece = lax.dynamic_slice_in_dim(expert_down, target * quarter_width, quarter_width, axis=2)
            pairs = [(i, (i + shift) % tp_count) for i in range(tp_count)]
            pieces.append(lax.ppermute(piece, "tp", pairs))
        order = (tp_here - jnp.arange(tp_count, dtype=jnp.int32)) % tp_count
        down_full = jnp.take(jnp.stack(pieces), order, axis=0)
        down_full = jnp.transpose(down_full, (1, 0, 2, 3)).reshape(local_experts, -1, quarter_width)
        gate_up_flat = expert_gate_up.reshape(local_experts, D, -1)
        qkv_flat = qkv_proj.reshape(D, -1)
    local_width = new_queries.shape[1]
    local_heads = local_width // HEAD_DIM
    quarter = hidden.shape[1]
    span = cache_keys.shape[1]
    my_length = lax.dynamic_index_in_dim(cache_lengths, here, 0, keepdims=False)
    attended = flash_attention(
        my_length,
        new_queries,
        cache_keys.reshape(span, local_width),
        cache_values.reshape(span, local_width),
        new_keys,
        new_values,
    )
    if dense:
        attended, down_full, gate_up_flat, qkv_flat = lax.optimization_barrier(
            (attended, down_full, gate_up_flat, qkv_flat)
        )
    else:
        gate_up_flat = expert_gate_up
        qkv_flat = qkv_proj.reshape(D, -1)
    attn_term = jnp.dot(attended, out_proj, preferred_element_type=jnp.float32)
    residual = hidden.astype(jnp.float32) + lax.psum_scatter(
        attn_term.astype(jnp.bfloat16), "tp", scatter_dimension=1, tiled=True
    ).astype(jnp.float32)
    square_total = lax.psum(jnp.sum(residual * residual, axis=1), "tp")
    moe_in = (residual * lax.rsqrt(square_total / D + epsilon)[:, None] * moe_gain[None, :]).astype(
        jnp.bfloat16
    )
    if dense:
        moe_term = dense_experts(
            moe_in, expert_ids, route_weights, gate_up_flat, down_full, here, experts_all
        )
    else:
        moe_term = dispatch_experts(
            moe_in, expert_ids, route_weights, expert_gate_up, expert_down, experts_all, capacity
        )
    routed = residual + moe_term
    layer_out = routed.astype(jnp.bfloat16)
    scaled = (routed * next_gain[None, :]).astype(jnp.bfloat16)
    weight_rows = qkv_flat
    mixed = jnp.dot(
        lax.all_gather(scaled, "tp", axis=1, tiled=True),
        weight_rows,
        preferred_element_type=jnp.float32,
    )
    mixed = mixed.reshape(NEW, 3, local_width)
    squares_routed = jnp.sum(routed * routed, axis=1)
    routed_total, query_raw, key_raw = lax.psum(
        (
            squares_routed,
            jnp.sum(mixed[:, 0] * mixed[:, 0], axis=1),
            jnp.sum(mixed[:, 1] * mixed[:, 1], axis=1),
        ),
        "tp",
    )
    x_scale = lax.rsqrt(routed_total / D + epsilon)
    query_pre = mixed[:, 0] * x_scale[:, None]
    key_pre = mixed[:, 1] * x_scale[:, None]
    query_total = query_raw * x_scale * x_scale
    key_total = key_raw * x_scale * x_scale
    next_query = (
        query_pre * lax.rsqrt(query_total / D + epsilon)[:, None] * query_gain[None, :]
    ).astype(jnp.bfloat16)
    next_key = (key_pre * lax.rsqrt(key_total / D + epsilon)[:, None] * key_gain[None, :]).astype(
        jnp.bfloat16
    )
    next_value = (mixed[:, 2] * x_scale[:, None]).astype(jnp.bfloat16)
    return (layer_out, next_query, next_key, next_value)


def solution(mesh):
    return jax.shard_map(
        body,
        mesh=mesh,
        in_specs=(
            P("seq", "tp"),
            P("seq", "tp"),
            P("seq", "tp"),
            P("seq", "tp"),
            P("seq", None, "tp"),
            P("seq", None, "tp"),
            P(),
            P("tp", None),
            P("tp"),
            P("seq", None),
            P("seq", None),
            P("seq", None, None, "tp"),
            P("seq", "tp", None),
            P("tp"),
            P(None, None, "tp"),
            P("tp"),
            P("tp"),
        ),
        out_specs=(P("seq", "tp"), P("seq", "tp"), P("seq", "tp"), P("seq", "tp")),
        check_vma=False,
    )
```

```python
import functools
import math

import jax
import jax.numpy as jnp
from jax import lax
from jax.experimental import pallas as pl
from jax.experimental.pallas import tpu as pltpu
from jax.sharding import PartitionSpec as P

D = 2048
HEAD_DIM = 128
TOP = 8
NEW = 256


epsilon = 1e-05


def flash_kernel(len_ref, q_ref, k_ref, v_ref, nk_ref, nv_ref, o_ref, m_sc, l_sc, acc_sc, *, block, heads, steps):
    j = pl.program_id(0)
    length = len_ref[0]
    valid = (length + block - 1) // block
    tokens = q_ref.shape[0]
    scale = 1.0 / math.sqrt(HEAD_DIM)

    @pl.when(j == 0)
    def _():
        m_sc[...] = jnp.full(m_sc.shape, -1e30, jnp.float32)
        l_sc[...] = jnp.zeros(l_sc.shape, jnp.float32)
        acc_sc[...] = jnp.zeros(acc_sc.shape, jnp.float32)

    def update(keys_ref, values_ref, allowed):
        for h in range(heads):
            cols = slice(h * HEAD_DIM, (h + 1) * HEAD_DIM)
            q = q_ref[:, cols]
            k = keys_ref[:, cols]
            s = lax.dot_general(q, k, (((1,), (1,)), ((), ())), preferred_element_type=jnp.float32) * scale
            s = jnp.where(allowed, s, -1e30)
            m_old = m_sc[h]
            m_new = jnp.maximum(m_old, jnp.max(s, axis=1, keepdims=True))
            alpha = jnp.exp(m_old - m_new)
            p = jnp.where(allowed, jnp.exp(s - m_new), 0.0)
            l_sc[h] = alpha * l_sc[h] + jnp.sum(p, axis=1, keepdims=True)
            pv = jnp.dot(p.astype(jnp.bfloat16), values_ref[:, cols], preferred_element_type=jnp.float32)
            acc_sc[:, cols] = alpha * acc_sc[:, cols] + pv
            m_sc[h] = m_new

    @pl.when(j < valid)
    def _():
        pos = j * block + lax.broadcasted_iota(jnp.int32, (tokens, block), 1)
        update(k_ref, v_ref, pos < length)

    @pl.when(j == steps - 1)
    def _():
        row = lax.broadcasted_iota(jnp.int32, (tokens, tokens), 0)
        col = lax.broadcasted_iota(jnp.int32, (tokens, tokens), 1)
        update(nk_ref, nv_ref, col <= row)
        for h in range(heads):
            cols = slice(h * HEAD_DIM, (h + 1) * HEAD_DIM)
            o_ref[:, cols] = (acc_sc[:, cols] / l_sc[h]).astype(o_ref.dtype)


def flash_attention(length, queries, cache_k, cache_v, new_k, new_v, block=1024):
    tokens, width = queries.shape
    span = cache_k.shape[0]
    block = min(block, span)
    heads = width // HEAD_DIM
    steps = span // block + 1
    last = span // block - 1

    def cache_map(j, len_ref):
        valid = (len_ref[0] + block - 1) // block
        return (jnp.minimum(j, jnp.maximum(valid - 1, 0)), 0)

    grid_spec = pltpu.PrefetchScalarGridSpec(
        num_scalar_prefetch=1,
        grid=(steps,),
        in_specs=[
            pl.BlockSpec((tokens, width), lambda j, l: (0, 0)),
            pl.BlockSpec((block, width), cache_map),
            pl.BlockSpec((block, width), cache_map),
            pl.BlockSpec((tokens, width), lambda j, l: (0, 0)),
            pl.BlockSpec((tokens, width), lambda j, l: (0, 0)),
        ],
        out_specs=pl.BlockSpec((tokens, width), lambda j, l: (0, 0)),
        scratch_shapes=[
            pltpu.VMEM((heads, tokens, 1), jnp.float32),
            pltpu.VMEM((heads, tokens, 1), jnp.float32),
            pltpu.VMEM((tokens, width), jnp.float32),
        ],
    )
    kernel = functools.partial(flash_kernel, block=block, heads=heads, steps=steps)
    return pl.pallas_call(
        kernel,
        grid_spec=grid_spec,
        out_shape=jax.ShapeDtypeStruct((tokens, width), jnp.bfloat16),
        compiler_params=pltpu.CompilerParams(dimension_semantics=("arbitrary",)),
    )(length.reshape(1), queries, cache_k, cache_v, new_k, new_v)


def dense_experts(moe_in, expert_ids, route_weights, expert_gate_up, down_full, here, experts_all):
    local_experts = expert_gate_up.shape[0]
    hidden_quarter = expert_gate_up.shape[2] // 2
    tokens, quarter = moe_in.shape
    seq_count = experts_all // local_experts
    gate_w = jnp.sum(
        route_weights[:, :, None]
        * (expert_ids[:, :, None] == jnp.arange(experts_all, dtype=jnp.int32)[None, None, :]),
        axis=1,
    )
    gate_t = jnp.transpose(gate_w)
    gate_hi = gate_t.astype(jnp.bfloat16)
    gate_lo = (gate_t - gate_hi.astype(jnp.float32)).astype(jnp.bfloat16)
    info = jnp.concatenate([gate_hi, gate_lo], axis=0).reshape(-1, quarter)
    packed = jnp.concatenate([moe_in, info], axis=0)
    ring = ring_order(seq_count)
    offsets, blocks = ring_all_gather(packed, ring)
    first = min(len(blocks), 5)
    chunks = [(0, first), (first, len(blocks))] if first < len(blocks) else [(0, first)]
    outputs = []
    for begin, end in chunks:
        gathered = jnp.stack(blocks[begin:end])
        count = end - begin
        rows_q = gathered[:, :tokens].reshape(count * tokens, quarter)
        info_all = gathered[:, tokens:].reshape(count, 2, experts_all, tokens).astype(jnp.float32)
        gate_all = info_all[:, 0] + info_all[:, 1]
        gate_local = lax.dynamic_slice_in_dim(gate_all, here * local_experts, local_experts, axis=1)
        gate_local = jnp.transpose(gate_local, (1, 0, 2)).reshape(local_experts, count * tokens)
        rows = lax.all_gather(rows_q, "tp", axis=1, tiled=True)
        projected = jnp.einsum("td,edf->etf", rows, expert_gate_up, preferred_element_type=jnp.float32)
        activated = jax.nn.silu(projected[..., :hidden_quarter]) * projected[..., hidden_quarter:]
        activated = activated.astype(jnp.bfloat16).astype(jnp.float32)
        weighted = (activated * gate_local[:, :, None]).astype(jnp.bfloat16)
        weighted = lax.all_gather(weighted, "tp", axis=2, tiled=True)
        partial = jnp.einsum(
            "etf,efd->td", weighted, down_full, preferred_element_type=jnp.float32
        ).astype(jnp.bfloat16)
        outputs.append(partial.reshape(count, tokens, -1))
    by_offset = {}
    index = 0
    for part in outputs:
        for i in range(part.shape[0]):
            by_offset[offsets[index]] = part[i]
            index += 1
    return ring_reduce_scatter(by_offset, ring)


def permute_reduce_scatter(term, width):
    tp_count = lax.axis_size("tp")
    tp_here = lax.axis_index("tp")
    total = lax.dynamic_slice_in_dim(term, tp_here * width, width, axis=1)
    for shift in range(1, tp_count):
        target = (tp_here + shift) % tp_count
        piece = lax.dynamic_slice_in_dim(term, target * width, width, axis=1).astype(jnp.bfloat16)
        pairs = [(i, (i + shift) % tp_count) for i in range(tp_count)]
        total = total + lax.ppermute(piece, "tp", pairs).astype(jnp.float32)
    return total


def permute_gather_dot(rows, weight):
    tp_count = lax.axis_size("tp")
    tp_here = lax.axis_index("tp")
    width = rows.shape[1]
    total = jnp.dot(
        rows,
        lax.dynamic_slice_in_dim(weight, tp_here * width, width, axis=0),
        preferred_element_type=jnp.float32,
    )
    for shift in range(1, tp_count):
        source = (tp_here - shift) % tp_count
        pairs = [(i, (i + shift) % tp_count) for i in range(tp_count)]
        piece = lax.ppermute(rows, "tp", pairs)
        total = total + jnp.dot(
            piece,
            lax.dynamic_slice_in_dim(weight, source * width, width, axis=0),
            preferred_element_type=jnp.float32,
        )
    return total


def ring_order(count):
    half = count // 2
    if count % 2 or count < 4:
        return list(range(count))
    return [2 * i for i in range(half)] + [2 * i + 1 for i in reversed(range(half))]


def ring_all_gather(block, cycle):
    count = len(cycle)
    forward = [(cycle[p], cycle[(p + 1) % count]) for p in range(count)]
    backward = [(cycle[p], cycle[(p - 1) % count]) for p in range(count)]
    offsets, blocks = [0], [block]
    ahead, behind = block, block
    for step in range(1, count // 2 + 1):
        ahead = lax.ppermute(ahead, "seq", forward)
        offsets.append((-step) % count)
        blocks.append(ahead)
        if step < count - count // 2:
            behind = lax.ppermute(behind, "seq", backward)
            offsets.append(step)
            blocks.append(behind)
    return offsets, blocks


def ring_reduce_scatter(by_offset, cycle):
    count = len(cycle)
    width = by_offset[0].shape[1]
    halves = []
    for direction in (1, -1):
        cols = slice(0, width // 2) if direction == 1 else slice(width // 2, width)
        pairs = [(cycle[p], cycle[(p + direction) % count]) for p in range(count)]
        acc = by_offset[(-direction) % count][:, cols].astype(jnp.float32)
        for step in range(count - 1):
            received = lax.ppermute(acc.astype(jnp.bfloat16), "seq", pairs)
            offset = (-direction * (step + 2)) % count
            acc = received.astype(jnp.float32) + by_offset[offset][:, cols].astype(jnp.float32)
        halves.append(acc)
    return jnp.concatenate(halves, axis=1)


def dispatch_experts(moe_in, expert_ids, route_weights, expert_gate_up, expert_down, experts_all, capacity):
    quarter = moe_in.shape[1]
    local_experts = expert_gate_up.shape[0]
    flat_ids = expert_ids.reshape(NEW * TOP)
    onehot = (flat_ids[:, None] == jnp.arange(experts_all, dtype=jnp.int32)[None, :]).astype(
        jnp.int32
    )
    ranks = jnp.sum((jnp.cumsum(onehot, axis=0) - onehot) * onehot, axis=1)
    target = (flat_ids * capacity + ranks).reshape(NEW, TOP)
    slot_ids = jnp.arange(experts_all * capacity, dtype=jnp.int32)
    selector = jnp.sum(
        (target[None, :, :] == slot_ids[:, None, None]).astype(jnp.int32), axis=2
    ).astype(jnp.bfloat16)
    send_rows = jnp.dot(selector, moe_in, preferred_element_type=jnp.float32).astype(jnp.bfloat16)
    send_rows = send_rows.reshape(experts_all, capacity, quarter)
    received = lax.all_to_all(send_rows, "seq", split_axis=0, concat_axis=1, tiled=True)
    hidden_quarter = expert_gate_up.shape[3]
    gate_up_local = expert_gate_up.reshape(local_experts, D, 2 * hidden_quarter)
    weight_rows = gate_up_local
    projected = jnp.einsum(
        "erd,edf->erf",
        lax.all_gather(received, "tp", axis=2, tiled=True),
        weight_rows,
        preferred_element_type=jnp.float32,
    )
    activated = (
        jax.nn.silu(projected[..., :hidden_quarter]) * projected[..., hidden_quarter:]
    ).astype(jnp.bfloat16)
    down_terms = jnp.einsum(
        "erf,efd->erd", activated, expert_down, preferred_element_type=jnp.float32
    )
    expert_result = lax.psum_scatter(
        down_terms.astype(jnp.bfloat16), "tp", scatter_dimension=2, tiled=True
    )
    returned = lax.all_to_all(
        expert_result, "seq", split_axis=1, concat_axis=0, tiled=True
    ).reshape(experts_all * capacity, quarter)
    picked = jnp.take(returned, target, axis=0)
    return jnp.sum(route_weights[:, :, None] * picked.astype(jnp.float32), axis=1)


def body(
    hidden,
    new_queries,
    new_keys,
    new_values,
    cache_keys,
    cache_values,
    cache_lengths,
    out_proj,
    moe_gain,
    expert_ids,
    route_weights,
    expert_gate_up,
    expert_down,
    next_gain,
    qkv_proj,
    query_gain,
    key_gain,
):
    seq_count = lax.axis_size("seq")
    here = lax.axis_index("seq")
    local_experts = expert_gate_up.shape[0]
    experts_all = local_experts * seq_count
    capacity = max(2, 3 * NEW * TOP // (2 * experts_all))
    dense = NEW <= 2 * capacity
    if dense:
        tp_here = lax.axis_index("tp")
        quarter_width = hidden.shape[1]
        tp_count = lax.axis_size("tp")
        pieces = [lax.dynamic_slice_in_dim(expert_down, tp_here * quarter_width, quarter_width, axis=2)]
        for shift in range(1, tp_count):
            target = (tp_here + shift) % tp_count
            piece = lax.dynamic_slice_in_dim(expert_down, target * quarter_width, quarter_width, axis=2)
            pairs = [(i, (i + shift) % tp_count) for i in range(tp_count)]
            pieces.append(lax.ppermute(piece, "tp", pairs))
        order = (tp_here - jnp.arange(tp_count, dtype=jnp.int32)) % tp_count
        down_full = jnp.take(jnp.stack(pieces), order, axis=0)
        down_full = jnp.transpose(down_full, (1, 0, 2, 3)).reshape(local_experts, -1, quarter_width)
        gate_up_flat = expert_gate_up.reshape(local_experts, D, -1)
        qkv_flat = qkv_proj.reshape(D, -1)
    local_width = new_queries.shape[1]
    local_heads = local_width // HEAD_DIM
    quarter = hidden.shape[1]
    span = cache_keys.shape[1]
    my_length = lax.dynamic_index_in_dim(cache_lengths, here, 0, keepdims=False)
    attended = flash_attention(
        my_length,
        new_queries,
        cache_keys.reshape(span, local_width),
        cache_values.reshape(span, local_width),
        new_keys,
        new_values,
    )
    if dense:
        attended, down_full, gate_up_flat, qkv_flat = lax.optimization_barrier(
            (attended, down_full, gate_up_flat, qkv_flat)
        )
    else:
        gate_up_flat = expert_gate_up
        qkv_flat = qkv_proj.reshape(D, -1)
    attn_term = jnp.dot(attended, out_proj, preferred_element_type=jnp.float32)
    if dense:
        residual = hidden.astype(jnp.float32) + permute_reduce_scatter(attn_term, local_width)
    else:
        residual = hidden.astype(jnp.float32) + lax.psum_scatter(
            attn_term.astype(jnp.bfloat16), "tp", scatter_dimension=1, tiled=True
        ).astype(jnp.float32)
    square_total = lax.psum(jnp.sum(residual * residual, axis=1), "tp")
    moe_in = (residual * lax.rsqrt(square_total / D + epsilon)[:, None] * moe_gain[None, :]).astype(
        jnp.bfloat16
    )
    if dense:
        moe_term = dense_experts(
            moe_in, expert_ids, route_weights, gate_up_flat, down_full, here, experts_all
        )
    else:
        moe_term = dispatch_experts(
            moe_in, expert_ids, route_weights, expert_gate_up, expert_down, experts_all, capacity
        )
    routed = residual + moe_term
    layer_out = routed.astype(jnp.bfloat16)
    scaled = (routed * next_gain[None, :]).astype(jnp.bfloat16)
    weight_rows = qkv_flat
    if dense:
        mixed = permute_gather_dot(scaled, weight_rows)
    else:
        mixed = jnp.dot(
            lax.all_gather(scaled, "tp", axis=1, tiled=True),
            weight_rows,
            preferred_element_type=jnp.float32,
        )
    mixed = mixed.reshape(NEW, 3, local_width)
    squares_routed = jnp.sum(routed * routed, axis=1)
    routed_total, query_raw, key_raw = lax.psum(
        (
            squares_routed,
            jnp.sum(mixed[:, 0] * mixed[:, 0], axis=1),
            jnp.sum(mixed[:, 1] * mixed[:, 1], axis=1),
        ),
        "tp",
    )
    x_scale = lax.rsqrt(routed_total / D + epsilon)
    query_pre = mixed[:, 0] * x_scale[:, None]
    key_pre = mixed[:, 1] * x_scale[:, None]
    query_total = query_raw * x_scale * x_scale
    key_total = key_raw * x_scale * x_scale
    next_query = (
        query_pre * lax.rsqrt(query_total / D + epsilon)[:, None] * query_gain[None, :]
    ).astype(jnp.bfloat16)
    next_key = (key_pre * lax.rsqrt(key_total / D + epsilon)[:, None] * key_gain[None, :]).astype(
        jnp.bfloat16
    )
    next_value = (mixed[:, 2] * x_scale[:, None]).astype(jnp.bfloat16)
    return (layer_out, next_query, next_key, next_value)


def solution(mesh):
    return jax.shard_map(
        body,
        mesh=mesh,
        in_specs=(
            P("seq", "tp"),
            P("seq", "tp"),
            P("seq", "tp"),
            P("seq", "tp"),
            P("seq", None, "tp"),
            P("seq", None, "tp"),
            P(),
            P("tp", None),
            P("tp"),
            P("seq", None),
            P("seq", None),
            P("seq", None, None, "tp"),
            P("seq", "tp", None),
            P("tp"),
            P(None, None, "tp"),
            P("tp"),
            P("tp"),
        ),
        out_specs=(P("seq", "tp"), P("seq", "tp"), P("seq", "tp"), P("seq", "tp")),
        check_vma=False,
    )
```

```python
import functools
import math

import jax
import jax.numpy as jnp
from jax import lax
from jax.experimental import pallas as pl
from jax.experimental.pallas import tpu as pltpu
from jax.sharding import PartitionSpec as P

D = 2048
HEAD_DIM = 128
TOP = 8
NEW = 256


epsilon = 1e-05


def flash_kernel(len_ref, q_ref, k_ref, v_ref, nk_ref, nv_ref, o_ref, m_sc, l_sc, acc_sc, *, block, heads, steps):
    j = pl.program_id(0)
    length = len_ref[0]
    valid = (length + block - 1) // block
    tokens = q_ref.shape[0]
    scale = 1.0 / math.sqrt(HEAD_DIM)

    @pl.when(j == 0)
    def _():
        m_sc[...] = jnp.full(m_sc.shape, -1e30, jnp.float32)
        l_sc[...] = jnp.zeros(l_sc.shape, jnp.float32)
        acc_sc[...] = jnp.zeros(acc_sc.shape, jnp.float32)

    def update(keys_ref, values_ref, allowed):
        for h in range(heads):
            cols = slice(h * HEAD_DIM, (h + 1) * HEAD_DIM)
            q = q_ref[:, cols]
            k = keys_ref[:, cols]
            s = lax.dot_general(q, k, (((1,), (1,)), ((), ())), preferred_element_type=jnp.float32) * scale
            s = jnp.where(allowed, s, -1e30)
            m_old = m_sc[h]
            m_new = jnp.maximum(m_old, jnp.max(s, axis=1, keepdims=True))
            alpha = jnp.exp(m_old - m_new)
            p = jnp.where(allowed, jnp.exp(s - m_new), 0.0)
            l_sc[h] = alpha * l_sc[h] + jnp.sum(p, axis=1, keepdims=True)
            pv = jnp.dot(p.astype(jnp.bfloat16), values_ref[:, cols], preferred_element_type=jnp.float32)
            acc_sc[:, cols] = alpha * acc_sc[:, cols] + pv
            m_sc[h] = m_new

    @pl.when(j < valid)
    def _():
        pos = j * block + lax.broadcasted_iota(jnp.int32, (tokens, block), 1)
        update(k_ref, v_ref, pos < length)

    @pl.when(j == steps - 1)
    def _():
        row = lax.broadcasted_iota(jnp.int32, (tokens, tokens), 0)
        col = lax.broadcasted_iota(jnp.int32, (tokens, tokens), 1)
        update(nk_ref, nv_ref, col <= row)
        for h in range(heads):
            cols = slice(h * HEAD_DIM, (h + 1) * HEAD_DIM)
            o_ref[:, cols] = (acc_sc[:, cols] / l_sc[h]).astype(o_ref.dtype)


def flash_attention(length, queries, cache_k, cache_v, new_k, new_v, block=1024):
    tokens, width = queries.shape
    span = cache_k.shape[0]
    block = min(block, span)
    heads = width // HEAD_DIM
    steps = span // block + 1
    last = span // block - 1

    def cache_map(j, len_ref):
        valid = (len_ref[0] + block - 1) // block
        return (jnp.minimum(j, jnp.maximum(valid - 1, 0)), 0)

    grid_spec = pltpu.PrefetchScalarGridSpec(
        num_scalar_prefetch=1,
        grid=(steps,),
        in_specs=[
            pl.BlockSpec((tokens, width), lambda j, l: (0, 0)),
            pl.BlockSpec((block, width), cache_map),
            pl.BlockSpec((block, width), cache_map),
            pl.BlockSpec((tokens, width), lambda j, l: (0, 0)),
            pl.BlockSpec((tokens, width), lambda j, l: (0, 0)),
        ],
        out_specs=pl.BlockSpec((tokens, width), lambda j, l: (0, 0)),
        scratch_shapes=[
            pltpu.VMEM((heads, tokens, 1), jnp.float32),
            pltpu.VMEM((heads, tokens, 1), jnp.float32),
            pltpu.VMEM((tokens, width), jnp.float32),
        ],
    )
    kernel = functools.partial(flash_kernel, block=block, heads=heads, steps=steps)
    return pl.pallas_call(
        kernel,
        grid_spec=grid_spec,
        out_shape=jax.ShapeDtypeStruct((tokens, width), jnp.bfloat16),
        compiler_params=pltpu.CompilerParams(dimension_semantics=("arbitrary",)),
    )(length.reshape(1), queries, cache_k, cache_v, new_k, new_v)


def dense_experts(moe_in, expert_ids, route_weights, expert_gate_up, down_full, qkv_flat, here, experts_all):
    local_experts = expert_gate_up.shape[0]
    hidden_quarter = expert_gate_up.shape[2] // 2
    tokens, quarter = moe_in.shape
    seq_count = experts_all // local_experts
    gate_w = jnp.sum(
        route_weights[:, :, None]
        * (expert_ids[:, :, None] == jnp.arange(experts_all, dtype=jnp.int32)[None, None, :]),
        axis=1,
    )
    gate_t = jnp.transpose(gate_w)
    gate_hi = gate_t.astype(jnp.bfloat16)
    gate_lo = (gate_t - gate_hi.astype(jnp.float32)).astype(jnp.bfloat16)
    info = jnp.concatenate([gate_hi, gate_lo], axis=0).reshape(-1, quarter)
    packed = jnp.concatenate([moe_in, info], axis=0)
    ring = ring_order(seq_count)
    offsets, blocks, (expert_gate_up, qkv_flat) = ring_all_gather(packed, ring, (expert_gate_up, qkv_flat))
    first = min(len(blocks), 5)
    chunks = [(0, first), (first, len(blocks))] if first < len(blocks) else [(0, first)]
    outputs = []
    for begin, end in chunks:
        gathered = jnp.stack(blocks[begin:end])
        count = end - begin
        rows_q = gathered[:, :tokens].reshape(count * tokens, quarter)
        info_all = gathered[:, tokens:].reshape(count, 2, experts_all, tokens).astype(jnp.float32)
        gate_all = info_all[:, 0] + info_all[:, 1]
        gate_local = lax.dynamic_slice_in_dim(gate_all, here * local_experts, local_experts, axis=1)
        gate_local = jnp.transpose(gate_local, (1, 0, 2)).reshape(local_experts, count * tokens)
        rows = lax.all_gather(rows_q, "tp", axis=1, tiled=True)
        projected = jnp.einsum("td,edf->etf", rows, expert_gate_up, preferred_element_type=jnp.float32)
        activated = jax.nn.silu(projected[..., :hidden_quarter]) * projected[..., hidden_quarter:]
        activated = activated.astype(jnp.bfloat16).astype(jnp.float32)
        weighted = (activated * gate_local[:, :, None]).astype(jnp.bfloat16)
        weighted = lax.all_gather(weighted, "tp", axis=2, tiled=True)
        partial = jnp.einsum(
            "etf,efd->td", weighted, down_full, preferred_element_type=jnp.float32
        ).astype(jnp.bfloat16)
        outputs.append(partial.reshape(count, tokens, -1))
    by_offset = {}
    index = 0
    for part in outputs:
        for i in range(part.shape[0]):
            by_offset[offsets[index]] = part[i]
            index += 1
    return ring_reduce_scatter(by_offset, ring), qkv_flat


def permute_reduce_scatter(term, width):
    tp_count = lax.axis_size("tp")
    tp_here = lax.axis_index("tp")
    total = lax.dynamic_slice_in_dim(term, tp_here * width, width, axis=1)
    for shift in range(1, tp_count):
        target = (tp_here + shift) % tp_count
        piece = lax.dynamic_slice_in_dim(term, target * width, width, axis=1).astype(jnp.bfloat16)
        pairs = [(i, (i + shift) % tp_count) for i in range(tp_count)]
        total = total + lax.ppermute(piece, "tp", pairs).astype(jnp.float32)
    return total


def permute_gather_dot(rows, weight):
    tp_count = lax.axis_size("tp")
    tp_here = lax.axis_index("tp")
    width = rows.shape[1]
    total = jnp.dot(
        rows,
        lax.dynamic_slice_in_dim(weight, tp_here * width, width, axis=0),
        preferred_element_type=jnp.float32,
    )
    for shift in range(1, tp_count):
        source = (tp_here - shift) % tp_count
        pairs = [(i, (i + shift) % tp_count) for i in range(tp_count)]
        piece = lax.ppermute(rows, "tp", pairs)
        total = total + jnp.dot(
            piece,
            lax.dynamic_slice_in_dim(weight, source * width, width, axis=0),
            preferred_element_type=jnp.float32,
        )
    return total


def ring_order(count):
    half = count // 2
    if count % 2 or count < 4:
        return list(range(count))
    return [2 * i for i in range(half)] + [2 * i + 1 for i in reversed(range(half))]


def ring_all_gather(block, cycle, riders):
    count = len(cycle)
    forward = [(cycle[p], cycle[(p + 1) % count]) for p in range(count)]
    backward = [(cycle[p], cycle[(p - 1) % count]) for p in range(count)]
    offsets, blocks = [0], [block]
    ahead, behind = block, block
    for step in range(1, count // 2 + 1):
        ahead = lax.ppermute(ahead, "seq", forward)
        offsets.append((-step) % count)
        blocks.append(ahead)
        if step < count - count // 2:
            behind = lax.ppermute(behind, "seq", backward)
            offsets.append(step)
            blocks.append(behind)
        if step == 1:
            ahead, behind, riders = lax.optimization_barrier((ahead, behind, riders))
            blocks[1:] = [ahead, behind][: len(blocks) - 1]
    return offsets, blocks, riders


def ring_reduce_scatter(by_offset, cycle):
    count = len(cycle)
    width = by_offset[0].shape[1]
    halves = []
    for direction in (1, -1):
        cols = slice(0, width // 2) if direction == 1 else slice(width // 2, width)
        pairs = [(cycle[p], cycle[(p + direction) % count]) for p in range(count)]
        acc = by_offset[(-direction) % count][:, cols].astype(jnp.float32)
        for step in range(count - 1):
            received = lax.ppermute(acc.astype(jnp.bfloat16), "seq", pairs)
            offset = (-direction * (step + 2)) % count
            acc = received.astype(jnp.float32) + by_offset[offset][:, cols].astype(jnp.float32)
        halves.append(acc)
    return jnp.concatenate(halves, axis=1)


def dispatch_experts(moe_in, expert_ids, route_weights, expert_gate_up, expert_down, experts_all, capacity):
    quarter = moe_in.shape[1]
    local_experts = expert_gate_up.shape[0]
    flat_ids = expert_ids.reshape(NEW * TOP)
    onehot = (flat_ids[:, None] == jnp.arange(experts_all, dtype=jnp.int32)[None, :]).astype(
        jnp.int32
    )
    ranks = jnp.sum((jnp.cumsum(onehot, axis=0) - onehot) * onehot, axis=1)
    target = (flat_ids * capacity + ranks).reshape(NEW, TOP)
    slot_ids = jnp.arange(experts_all * capacity, dtype=jnp.int32)
    selector = jnp.sum(
        (target[None, :, :] == slot_ids[:, None, None]).astype(jnp.int32), axis=2
    ).astype(jnp.bfloat16)
    send_rows = jnp.dot(selector, moe_in, preferred_element_type=jnp.float32).astype(jnp.bfloat16)
    send_rows = send_rows.reshape(experts_all, capacity, quarter)
    received = lax.all_to_all(send_rows, "seq", split_axis=0, concat_axis=1, tiled=True)
    hidden_quarter = expert_gate_up.shape[3]
    gate_up_local = expert_gate_up.reshape(local_experts, D, 2 * hidden_quarter)
    weight_rows = gate_up_local
    projected = jnp.einsum(
        "erd,edf->erf",
        lax.all_gather(received, "tp", axis=2, tiled=True),
        weight_rows,
        preferred_element_type=jnp.float32,
    )
    activated = (
        jax.nn.silu(projected[..., :hidden_quarter]) * projected[..., hidden_quarter:]
    ).astype(jnp.bfloat16)
    down_terms = jnp.einsum(
        "erf,efd->erd", activated, expert_down, preferred_element_type=jnp.float32
    )
    expert_result = lax.psum_scatter(
        down_terms.astype(jnp.bfloat16), "tp", scatter_dimension=2, tiled=True
    )
    returned = lax.all_to_all(
        expert_result, "seq", split_axis=1, concat_axis=0, tiled=True
    ).reshape(experts_all * capacity, quarter)
    picked = jnp.take(returned, target, axis=0)
    return jnp.sum(route_weights[:, :, None] * picked.astype(jnp.float32), axis=1)


def body(
    hidden,
    new_queries,
    new_keys,
    new_values,
    cache_keys,
    cache_values,
    cache_lengths,
    out_proj,
    moe_gain,
    expert_ids,
    route_weights,
    expert_gate_up,
    expert_down,
    next_gain,
    qkv_proj,
    query_gain,
    key_gain,
):
    seq_count = lax.axis_size("seq")
    here = lax.axis_index("seq")
    local_experts = expert_gate_up.shape[0]
    experts_all = local_experts * seq_count
    capacity = max(2, 3 * NEW * TOP // (2 * experts_all))
    dense = NEW <= 2 * capacity
    if dense:
        tp_here = lax.axis_index("tp")
        quarter_width = hidden.shape[1]
        tp_count = lax.axis_size("tp")
        pieces = [lax.dynamic_slice_in_dim(expert_down, tp_here * quarter_width, quarter_width, axis=2)]
        for shift in range(1, tp_count):
            target = (tp_here + shift) % tp_count
            piece = lax.dynamic_slice_in_dim(expert_down, target * quarter_width, quarter_width, axis=2)
            pairs = [(i, (i + shift) % tp_count) for i in range(tp_count)]
            pieces.append(lax.ppermute(piece, "tp", pairs))
        order = (tp_here - jnp.arange(tp_count, dtype=jnp.int32)) % tp_count
        down_full = jnp.take(jnp.stack(pieces), order, axis=0)
        down_full = jnp.transpose(down_full, (1, 0, 2, 3)).reshape(local_experts, -1, quarter_width)
        gate_up_flat = expert_gate_up.reshape(local_experts, D, -1)
        qkv_flat = qkv_proj.reshape(D, -1)
    local_width = new_queries.shape[1]
    local_heads = local_width // HEAD_DIM
    quarter = hidden.shape[1]
    span = cache_keys.shape[1]
    my_length = lax.dynamic_index_in_dim(cache_lengths, here, 0, keepdims=False)
    attended = flash_attention(
        my_length,
        new_queries,
        cache_keys.reshape(span, local_width),
        cache_values.reshape(span, local_width),
        new_keys,
        new_values,
    )
    if dense:
        attended, down_full = lax.optimization_barrier((attended, down_full))
    else:
        gate_up_flat = expert_gate_up
        qkv_flat = qkv_proj.reshape(D, -1)
    attn_term = jnp.dot(attended, out_proj, preferred_element_type=jnp.float32)
    if dense:
        residual = hidden.astype(jnp.float32) + permute_reduce_scatter(attn_term, local_width)
    else:
        residual = hidden.astype(jnp.float32) + lax.psum_scatter(
            attn_term.astype(jnp.bfloat16), "tp", scatter_dimension=1, tiled=True
        ).astype(jnp.float32)
    square_total = lax.psum(jnp.sum(residual * residual, axis=1), "tp")
    moe_in = (residual * lax.rsqrt(square_total / D + epsilon)[:, None] * moe_gain[None, :]).astype(
        jnp.bfloat16
    )
    if dense:
        moe_term, qkv_flat = dense_experts(
            moe_in, expert_ids, route_weights, gate_up_flat, down_full, qkv_flat, here, experts_all
        )
    else:
        moe_term = dispatch_experts(
            moe_in, expert_ids, route_weights, expert_gate_up, expert_down, experts_all, capacity
        )
    routed = residual + moe_term
    layer_out = routed.astype(jnp.bfloat16)
    scaled = (routed * next_gain[None, :]).astype(jnp.bfloat16)
    weight_rows = qkv_flat
    if dense:
        mixed = permute_gather_dot(scaled, weight_rows)
    else:
        mixed = jnp.dot(
            lax.all_gather(scaled, "tp", axis=1, tiled=True),
            weight_rows,
            preferred_element_type=jnp.float32,
        )
    mixed = mixed.reshape(NEW, 3, local_width)
    squares_routed = jnp.sum(routed * routed, axis=1)
    routed_total, query_raw, key_raw = lax.psum(
        (
            squares_routed,
            jnp.sum(mixed[:, 0] * mixed[:, 0], axis=1),
            jnp.sum(mixed[:, 1] * mixed[:, 1], axis=1),
        ),
        "tp",
    )
    x_scale = lax.rsqrt(routed_total / D + epsilon)
    query_pre = mixed[:, 0] * x_scale[:, None]
    key_pre = mixed[:, 1] * x_scale[:, None]
    query_total = query_raw * x_scale * x_scale
    key_total = key_raw * x_scale * x_scale
    next_query = (
        query_pre * lax.rsqrt(query_total / D + epsilon)[:, None] * query_gain[None, :]
    ).astype(jnp.bfloat16)
    next_key = (key_pre * lax.rsqrt(key_total / D + epsilon)[:, None] * key_gain[None, :]).astype(
        jnp.bfloat16
    )
    next_value = (mixed[:, 2] * x_scale[:, None]).astype(jnp.bfloat16)
    return (layer_out, next_query, next_key, next_value)


def solution(mesh):
    return jax.shard_map(
        body,
        mesh=mesh,
        in_specs=(
            P("seq", "tp"),
            P("seq", "tp"),
            P("seq", "tp"),
            P("seq", "tp"),
            P("seq", None, "tp"),
            P("seq", None, "tp"),
            P(),
            P("tp", None),
            P("tp"),
            P("seq", None),
            P("seq", None),
            P("seq", None, None, "tp"),
            P("seq", "tp", None),
            P("tp"),
            P(None, None, "tp"),
            P("tp"),
            P("tp"),
        ),
        out_specs=(P("seq", "tp"), P("seq", "tp"), P("seq", "tp"), P("seq", "tp")),
        check_vma=False,
    )
```

```python
import functools
import math

import jax
import jax.numpy as jnp
from jax import lax
from jax.experimental import pallas as pl
from jax.experimental.pallas import tpu as pltpu
from jax.sharding import PartitionSpec as P

D = 2048
HEAD_DIM = 128
TOP = 8
NEW = 256


epsilon = 1e-05


def flash_kernel(len_ref, q_ref, k_ref, v_ref, nk_ref, nv_ref, o_ref, m_sc, l_sc, acc_sc, *, block, heads, steps):
    j = pl.program_id(0)
    length = len_ref[0]
    valid = (length + block - 1) // block
    tokens = q_ref.shape[0]
    scale = 1.0 / math.sqrt(HEAD_DIM)

    @pl.when(j == 0)
    def _():
        m_sc[...] = jnp.full(m_sc.shape, -1e30, jnp.float32)
        l_sc[...] = jnp.zeros(l_sc.shape, jnp.float32)
        acc_sc[...] = jnp.zeros(acc_sc.shape, jnp.float32)

    def update(keys_ref, values_ref, allowed):
        for h in range(heads):
            cols = slice(h * HEAD_DIM, (h + 1) * HEAD_DIM)
            q = q_ref[:, cols]
            k = keys_ref[:, cols]
            s = lax.dot_general(q, k, (((1,), (1,)), ((), ())), preferred_element_type=jnp.float32) * scale
            s = jnp.where(allowed, s, -1e30)
            m_old = m_sc[h]
            m_new = jnp.maximum(m_old, jnp.max(s, axis=1, keepdims=True))
            alpha = jnp.exp(m_old - m_new)
            p = jnp.where(allowed, jnp.exp(s - m_new), 0.0)
            l_sc[h] = alpha * l_sc[h] + jnp.sum(p, axis=1, keepdims=True)
            pv = jnp.dot(p.astype(jnp.bfloat16), values_ref[:, cols], preferred_element_type=jnp.float32)
            acc_sc[:, cols] = alpha * acc_sc[:, cols] + pv
            m_sc[h] = m_new

    @pl.when(j < valid)
    def _():
        pos = j * block + lax.broadcasted_iota(jnp.int32, (tokens, block), 1)
        update(k_ref, v_ref, pos < length)

    @pl.when(j == steps - 1)
    def _():
        row = lax.broadcasted_iota(jnp.int32, (tokens, tokens), 0)
        col = lax.broadcasted_iota(jnp.int32, (tokens, tokens), 1)
        update(nk_ref, nv_ref, col <= row)
        for h in range(heads):
            cols = slice(h * HEAD_DIM, (h + 1) * HEAD_DIM)
            o_ref[:, cols] = (acc_sc[:, cols] / l_sc[h]).astype(o_ref.dtype)


def flash_attention(length, queries, cache_k, cache_v, new_k, new_v, block=1024):
    tokens, width = queries.shape
    span = cache_k.shape[0]
    block = min(block, span)
    heads = width // HEAD_DIM
    steps = span // block + 1
    last = span // block - 1

    def cache_map(j, len_ref):
        valid = (len_ref[0] + block - 1) // block
        return (jnp.minimum(j, jnp.maximum(valid - 1, 0)), 0)

    grid_spec = pltpu.PrefetchScalarGridSpec(
        num_scalar_prefetch=1,
        grid=(steps,),
        in_specs=[
            pl.BlockSpec((tokens, width), lambda j, l: (0, 0)),
            pl.BlockSpec((block, width), cache_map),
            pl.BlockSpec((block, width), cache_map),
            pl.BlockSpec((tokens, width), lambda j, l: (0, 0)),
            pl.BlockSpec((tokens, width), lambda j, l: (0, 0)),
        ],
        out_specs=pl.BlockSpec((tokens, width), lambda j, l: (0, 0)),
        scratch_shapes=[
            pltpu.VMEM((heads, tokens, 1), jnp.float32),
            pltpu.VMEM((heads, tokens, 1), jnp.float32),
            pltpu.VMEM((tokens, width), jnp.float32),
        ],
    )
    kernel = functools.partial(flash_kernel, block=block, heads=heads, steps=steps)
    return pl.pallas_call(
        kernel,
        grid_spec=grid_spec,
        out_shape=jax.ShapeDtypeStruct((tokens, width), jnp.bfloat16),
        compiler_params=pltpu.CompilerParams(dimension_semantics=("arbitrary",)),
    )(length.reshape(1), queries, cache_k, cache_v, new_k, new_v)


def dense_experts(moe_in, expert_ids, route_weights, expert_gate_up, down_full, qkv_flat, here, experts_all):
    local_experts = expert_gate_up.shape[0]
    hidden_quarter = expert_gate_up.shape[2] // 2
    tokens, quarter = moe_in.shape
    seq_count = experts_all // local_experts
    gate_w = jnp.sum(
        route_weights[:, :, None]
        * (expert_ids[:, :, None] == jnp.arange(experts_all, dtype=jnp.int32)[None, None, :]),
        axis=1,
    )
    gate_t = jnp.transpose(gate_w)
    gate_hi = gate_t.astype(jnp.bfloat16)
    gate_lo = (gate_t - gate_hi.astype(jnp.float32)).astype(jnp.bfloat16)
    info = jnp.concatenate([gate_hi, gate_lo], axis=0).reshape(-1, quarter)
    packed = jnp.concatenate([moe_in, info], axis=0)
    ring = ring_order(seq_count)
    offsets, blocks = ring_all_gather(packed, ring)
    first = min(len(blocks), 5)
    chunks = [(0, first), (first, len(blocks))] if first < len(blocks) else [(0, first)]
    outputs = []
    for begin, end in chunks:
        gathered = jnp.stack(blocks[begin:end])
        count = end - begin
        rows_q = gathered[:, :tokens].reshape(count * tokens, quarter)
        info_all = gathered[:, tokens:].reshape(count, 2, experts_all, tokens).astype(jnp.float32)
        gate_all = info_all[:, 0] + info_all[:, 1]
        gate_local = lax.dynamic_slice_in_dim(gate_all, here * local_experts, local_experts, axis=1)
        gate_local = jnp.transpose(gate_local, (1, 0, 2)).reshape(local_experts, count * tokens)
        rows = lax.all_gather(rows_q, "tp", axis=1, tiled=True)
        if begin == 0:
            rows, expert_gate_up, qkv_flat, down_full = lax.optimization_barrier(
                (rows, expert_gate_up, qkv_flat, down_full)
            )
        projected = jnp.einsum("td,edf->etf", rows, expert_gate_up, preferred_element_type=jnp.float32)
        activated = jax.nn.silu(projected[..., :hidden_quarter]) * projected[..., hidden_quarter:]
        activated = activated.astype(jnp.bfloat16).astype(jnp.float32)
        weighted = (activated * gate_local[:, :, None]).astype(jnp.bfloat16)
        weighted = lax.all_gather(weighted, "tp", axis=2, tiled=True)
        partial = jnp.einsum(
            "etf,efd->td", weighted, down_full, preferred_element_type=jnp.float32
        ).astype(jnp.bfloat16)
        outputs.append(partial.reshape(count, tokens, -1))
    by_offset = {}
    index = 0
    for part in outputs:
        for i in range(part.shape[0]):
            by_offset[offsets[index]] = part[i]
            index += 1
    return ring_reduce_scatter(by_offset, ring), qkv_flat


def permute_reduce_scatter(term, width):
    tp_count = lax.axis_size("tp")
    tp_here = lax.axis_index("tp")
    total = lax.dynamic_slice_in_dim(term, tp_here * width, width, axis=1)
    for shift in range(1, tp_count):
        target = (tp_here + shift) % tp_count
        piece = lax.dynamic_slice_in_dim(term, target * width, width, axis=1).astype(jnp.bfloat16)
        pairs = [(i, (i + shift) % tp_count) for i in range(tp_count)]
        total = total + lax.ppermute(piece, "tp", pairs).astype(jnp.float32)
    return total


def permute_gather_dot(rows, weight):
    tp_count = lax.axis_size("tp")
    tp_here = lax.axis_index("tp")
    width = rows.shape[1]
    total = jnp.dot(
        rows,
        lax.dynamic_slice_in_dim(weight, tp_here * width, width, axis=0),
        preferred_element_type=jnp.float32,
    )
    for shift in range(1, tp_count):
        source = (tp_here - shift) % tp_count
        pairs = [(i, (i + shift) % tp_count) for i in range(tp_count)]
        piece = lax.ppermute(rows, "tp", pairs)
        total = total + jnp.dot(
            piece,
            lax.dynamic_slice_in_dim(weight, source * width, width, axis=0),
            preferred_element_type=jnp.float32,
        )
    return total


def ring_order(count):
    half = count // 2
    if count % 2 or count < 4:
        return list(range(count))
    return [2 * i for i in range(half)] + [2 * i + 1 for i in reversed(range(half))]


def ring_all_gather(block, cycle):
    count = len(cycle)
    forward = [(cycle[p], cycle[(p + 1) % count]) for p in range(count)]
    backward = [(cycle[p], cycle[(p - 1) % count]) for p in range(count)]
    offsets, blocks = [0], [block]
    ahead, behind = block, block
    for step in range(1, count // 2 + 1):
        ahead = lax.ppermute(ahead, "seq", forward)
        offsets.append((-step) % count)
        blocks.append(ahead)
        if step < count - count // 2:
            behind = lax.ppermute(behind, "seq", backward)
            offsets.append(step)
            blocks.append(behind)
    return offsets, blocks


def ring_reduce_scatter(by_offset, cycle):
    count = len(cycle)
    width = by_offset[0].shape[1]
    halves = []
    for direction in (1, -1):
        cols = slice(0, width // 2) if direction == 1 else slice(width // 2, width)
        pairs = [(cycle[p], cycle[(p + direction) % count]) for p in range(count)]
        acc = by_offset[(-direction) % count][:, cols].astype(jnp.float32)
        for step in range(count - 1):
            received = lax.ppermute(acc.astype(jnp.bfloat16), "seq", pairs)
            offset = (-direction * (step + 2)) % count
            acc = received.astype(jnp.float32) + by_offset[offset][:, cols].astype(jnp.float32)
        halves.append(acc)
    return jnp.concatenate(halves, axis=1)


def dispatch_experts(moe_in, expert_ids, route_weights, expert_gate_up, expert_down, experts_all, capacity):
    quarter = moe_in.shape[1]
    local_experts = expert_gate_up.shape[0]
    flat_ids = expert_ids.reshape(NEW * TOP)
    onehot = (flat_ids[:, None] == jnp.arange(experts_all, dtype=jnp.int32)[None, :]).astype(
        jnp.int32
    )
    ranks = jnp.sum((jnp.cumsum(onehot, axis=0) - onehot) * onehot, axis=1)
    target = (flat_ids * capacity + ranks).reshape(NEW, TOP)
    slot_ids = jnp.arange(experts_all * capacity, dtype=jnp.int32)
    selector = jnp.sum(
        (target[None, :, :] == slot_ids[:, None, None]).astype(jnp.int32), axis=2
    ).astype(jnp.bfloat16)
    send_rows = jnp.dot(selector, moe_in, preferred_element_type=jnp.float32).astype(jnp.bfloat16)
    send_rows = send_rows.reshape(experts_all, capacity, quarter)
    received = lax.all_to_all(send_rows, "seq", split_axis=0, concat_axis=1, tiled=True)
    hidden_quarter = expert_gate_up.shape[3]
    gate_up_local = expert_gate_up.reshape(local_experts, D, 2 * hidden_quarter)
    weight_rows = gate_up_local
    projected = jnp.einsum(
        "erd,edf->erf",
        lax.all_gather(received, "tp", axis=2, tiled=True),
        weight_rows,
        preferred_element_type=jnp.float32,
    )
    activated = (
        jax.nn.silu(projected[..., :hidden_quarter]) * projected[..., hidden_quarter:]
    ).astype(jnp.bfloat16)
    down_terms = jnp.einsum(
        "erf,efd->erd", activated, expert_down, preferred_element_type=jnp.float32
    )
    expert_result = lax.psum_scatter(
        down_terms.astype(jnp.bfloat16), "tp", scatter_dimension=2, tiled=True
    )
    returned = lax.all_to_all(
        expert_result, "seq", split_axis=1, concat_axis=0, tiled=True
    ).reshape(experts_all * capacity, quarter)
    picked = jnp.take(returned, target, axis=0)
    return jnp.sum(route_weights[:, :, None] * picked.astype(jnp.float32), axis=1)


def body(
    hidden,
    new_queries,
    new_keys,
    new_values,
    cache_keys,
    cache_values,
    cache_lengths,
    out_proj,
    moe_gain,
    expert_ids,
    route_weights,
    expert_gate_up,
    expert_down,
    next_gain,
    qkv_proj,
    query_gain,
    key_gain,
):
    seq_count = lax.axis_size("seq")
    here = lax.axis_index("seq")
    local_experts = expert_gate_up.shape[0]
    experts_all = local_experts * seq_count
    capacity = max(2, 3 * NEW * TOP // (2 * experts_all))
    dense = NEW <= 2 * capacity
    if dense:
        tp_here = lax.axis_index("tp")
        quarter_width = hidden.shape[1]
        tp_count = lax.axis_size("tp")
        pieces = [lax.dynamic_slice_in_dim(expert_down, tp_here * quarter_width, quarter_width, axis=2)]
        for shift in range(1, tp_count):
            target = (tp_here + shift) % tp_count
            piece = lax.dynamic_slice_in_dim(expert_down, target * quarter_width, quarter_width, axis=2)
            pairs = [(i, (i + shift) % tp_count) for i in range(tp_count)]
            pieces.append(lax.ppermute(piece, "tp", pairs))
        order = (tp_here - jnp.arange(tp_count, dtype=jnp.int32)) % tp_count
        down_full = jnp.take(jnp.stack(pieces), order, axis=0)
        down_full = jnp.transpose(down_full, (1, 0, 2, 3)).reshape(local_experts, -1, quarter_width)
        gate_up_flat = expert_gate_up.reshape(local_experts, D, -1)
        qkv_flat = qkv_proj.reshape(D, -1)
    local_width = new_queries.shape[1]
    local_heads = local_width // HEAD_DIM
    quarter = hidden.shape[1]
    span = cache_keys.shape[1]
    my_length = lax.dynamic_index_in_dim(cache_lengths, here, 0, keepdims=False)
    attended = flash_attention(
        my_length,
        new_queries,
        cache_keys.reshape(span, local_width),
        cache_values.reshape(span, local_width),
        new_keys,
        new_values,
    )
    if not dense:
        gate_up_flat = expert_gate_up
        qkv_flat = qkv_proj.reshape(D, -1)
    attn_term = jnp.dot(attended, out_proj, preferred_element_type=jnp.float32)
    if dense:
        residual = hidden.astype(jnp.float32) + permute_reduce_scatter(attn_term, local_width)
    else:
        residual = hidden.astype(jnp.float32) + lax.psum_scatter(
            attn_term.astype(jnp.bfloat16), "tp", scatter_dimension=1, tiled=True
        ).astype(jnp.float32)
    square_total = lax.psum(jnp.sum(residual * residual, axis=1), "tp")
    moe_in = (residual * lax.rsqrt(square_total / D + epsilon)[:, None] * moe_gain[None, :]).astype(
        jnp.bfloat16
    )
    if dense:
        moe_term, qkv_flat = dense_experts(
            moe_in, expert_ids, route_weights, gate_up_flat, down_full, qkv_flat, here, experts_all
        )
    else:
        moe_term = dispatch_experts(
            moe_in, expert_ids, route_weights, expert_gate_up, expert_down, experts_all, capacity
        )
    routed = residual + moe_term
    layer_out = routed.astype(jnp.bfloat16)
    scaled = (routed * next_gain[None, :]).astype(jnp.bfloat16)
    weight_rows = qkv_flat
    if dense:
        mixed = permute_gather_dot(scaled, weight_rows)
    else:
        mixed = jnp.dot(
            lax.all_gather(scaled, "tp", axis=1, tiled=True),
            weight_rows,
            preferred_element_type=jnp.float32,
        )
    mixed = mixed.reshape(NEW, 3, local_width)
    squares_routed = jnp.sum(routed * routed, axis=1)
    routed_total, query_raw, key_raw = lax.psum(
        (
            squares_routed,
            jnp.sum(mixed[:, 0] * mixed[:, 0], axis=1),
            jnp.sum(mixed[:, 1] * mixed[:, 1], axis=1),
        ),
        "tp",
    )
    x_scale = lax.rsqrt(routed_total / D + epsilon)
    query_pre = mixed[:, 0] * x_scale[:, None]
    key_pre = mixed[:, 1] * x_scale[:, None]
    query_total = query_raw * x_scale * x_scale
    key_total = key_raw * x_scale * x_scale
    next_query = (
        query_pre * lax.rsqrt(query_total / D + epsilon)[:, None] * query_gain[None, :]
    ).astype(jnp.bfloat16)
    next_key = (key_pre * lax.rsqrt(key_total / D + epsilon)[:, None] * key_gain[None, :]).astype(
        jnp.bfloat16
    )
    next_value = (mixed[:, 2] * x_scale[:, None]).astype(jnp.bfloat16)
    return (layer_out, next_query, next_key, next_value)


def solution(mesh):
    return jax.shard_map(
        body,
        mesh=mesh,
        in_specs=(
            P("seq", "tp"),
            P("seq", "tp"),
            P("seq", "tp"),
            P("seq", "tp"),
            P("seq", None, "tp"),
            P("seq", None, "tp"),
            P(),
            P("tp", None),
            P("tp"),
            P("seq", None),
            P("seq", None),
            P("seq", None, None, "tp"),
            P("seq", "tp", None),
            P("tp"),
            P(None, None, "tp"),
            P("tp"),
            P("tp"),
        ),
        out_specs=(P("seq", "tp"), P("seq", "tp"), P("seq", "tp"), P("seq", "tp")),
        check_vma=False,
    )
```

```python
import functools
import math

import jax
import jax.numpy as jnp
from jax import lax
from jax.experimental import pallas as pl
from jax.experimental.pallas import tpu as pltpu
from jax.sharding import PartitionSpec as P

D = 2048
HEAD_DIM = 128
TOP = 8
NEW = 256


epsilon = 1e-05


def flash_kernel(len_ref, q_ref, k_ref, v_ref, nk_ref, nv_ref, o_ref, m_sc, l_sc, acc_sc, *, block, heads, steps):
    j = pl.program_id(0)
    length = len_ref[0]
    valid = (length + block - 1) // block
    tokens = q_ref.shape[0]
    scale = 1.0 / math.sqrt(HEAD_DIM)

    @pl.when(j == 0)
    def _():
        m_sc[...] = jnp.full(m_sc.shape, -1e30, jnp.float32)
        l_sc[...] = jnp.zeros(l_sc.shape, jnp.float32)
        acc_sc[...] = jnp.zeros(acc_sc.shape, jnp.float32)

    def update(keys_ref, values_ref, allowed):
        for h in range(heads):
            cols = slice(h * HEAD_DIM, (h + 1) * HEAD_DIM)
            q = q_ref[:, cols]
            k = keys_ref[:, cols]
            s = lax.dot_general(q, k, (((1,), (1,)), ((), ())), preferred_element_type=jnp.float32) * scale
            s = jnp.where(allowed, s, -1e30)
            m_old = m_sc[h]
            m_new = jnp.maximum(m_old, jnp.max(s, axis=1, keepdims=True))
            alpha = jnp.exp(m_old - m_new)
            p = jnp.where(allowed, jnp.exp(s - m_new), 0.0)
            l_sc[h] = alpha * l_sc[h] + jnp.sum(p, axis=1, keepdims=True)
            pv = jnp.dot(p.astype(jnp.bfloat16), values_ref[:, cols], preferred_element_type=jnp.float32)
            acc_sc[:, cols] = alpha * acc_sc[:, cols] + pv
            m_sc[h] = m_new

    @pl.when(j < valid)
    def _():
        pos = j * block + lax.broadcasted_iota(jnp.int32, (tokens, block), 1)
        update(k_ref, v_ref, pos < length)

    @pl.when(j == steps - 1)
    def _():
        row = lax.broadcasted_iota(jnp.int32, (tokens, tokens), 0)
        col = lax.broadcasted_iota(jnp.int32, (tokens, tokens), 1)
        update(nk_ref, nv_ref, col <= row)
        for h in range(heads):
            cols = slice(h * HEAD_DIM, (h + 1) * HEAD_DIM)
            o_ref[:, cols] = (acc_sc[:, cols] / l_sc[h]).astype(o_ref.dtype)


def flash_attention(length, queries, cache_k, cache_v, new_k, new_v, block=1024):
    tokens, width = queries.shape
    span = cache_k.shape[0]
    block = min(block, span)
    heads = width // HEAD_DIM
    steps = span // block + 1
    last = span // block - 1

    def cache_map(j, len_ref):
        valid = (len_ref[0] + block - 1) // block
        return (jnp.minimum(j, jnp.maximum(valid - 1, 0)), 0)

    grid_spec = pltpu.PrefetchScalarGridSpec(
        num_scalar_prefetch=1,
        grid=(steps,),
        in_specs=[
            pl.BlockSpec((tokens, width), lambda j, l: (0, 0)),
            pl.BlockSpec((block, width), cache_map),
            pl.BlockSpec((block, width), cache_map),
            pl.BlockSpec((tokens, width), lambda j, l: (0, 0)),
            pl.BlockSpec((tokens, width), lambda j, l: (0, 0)),
        ],
        out_specs=pl.BlockSpec((tokens, width), lambda j, l: (0, 0)),
        scratch_shapes=[
            pltpu.VMEM((heads, tokens, 1), jnp.float32),
            pltpu.VMEM((heads, tokens, 1), jnp.float32),
            pltpu.VMEM((tokens, width), jnp.float32),
        ],
    )
    kernel = functools.partial(flash_kernel, block=block, heads=heads, steps=steps)
    return pl.pallas_call(
        kernel,
        grid_spec=grid_spec,
        out_shape=jax.ShapeDtypeStruct((tokens, width), jnp.bfloat16),
        compiler_params=pltpu.CompilerParams(dimension_semantics=("arbitrary",)),
    )(length.reshape(1), queries, cache_k, cache_v, new_k, new_v)


def dense_experts(moe_in, expert_ids, route_weights, expert_gate_up, down_full, qkv_flat, here, experts_all):
    local_experts = expert_gate_up.shape[0]
    hidden_quarter = expert_gate_up.shape[2] // 2
    tokens, quarter = moe_in.shape
    seq_count = experts_all // local_experts
    gate_w = jnp.sum(
        route_weights[:, :, None]
        * (expert_ids[:, :, None] == jnp.arange(experts_all, dtype=jnp.int32)[None, None, :]),
        axis=1,
    )
    gate_t = jnp.transpose(gate_w)
    gate_hi = gate_t.astype(jnp.bfloat16)
    gate_lo = (gate_t - gate_hi.astype(jnp.float32)).astype(jnp.bfloat16)
    info = jnp.concatenate([gate_hi, gate_lo], axis=0).reshape(-1, quarter)
    packed = jnp.concatenate([moe_in, info], axis=0)
    ring = ring_order(seq_count)
    offsets, blocks = ring_all_gather(packed, ring)
    first = min(len(blocks), 5)
    chunks = [(0, first), (first, len(blocks))] if first < len(blocks) else [(0, first)]
    outputs = []
    for begin, end in chunks:
        gathered = jnp.stack(blocks[begin:end])
        count = end - begin
        rows_q = gathered[:, :tokens].reshape(count * tokens, quarter)
        info_all = gathered[:, tokens:].reshape(count, 2, experts_all, tokens).astype(jnp.float32)
        gate_all = info_all[:, 0] + info_all[:, 1]
        gate_local = lax.dynamic_slice_in_dim(gate_all, here * local_experts, local_experts, axis=1)
        gate_local = jnp.transpose(gate_local, (1, 0, 2)).reshape(local_experts, count * tokens)
        rows = lax.all_gather(rows_q, "tp", axis=0, tiled=False)
        if begin == 0:
            rows, expert_gate_up, qkv_flat, down_full = lax.optimization_barrier(
                (rows, expert_gate_up, qkv_flat, down_full)
            )
        gate_up_split = expert_gate_up.reshape(local_experts, rows.shape[0], quarter, -1)
        projected = jnp.einsum("qtd,eqdf->etf", rows, gate_up_split, preferred_element_type=jnp.float32)
        activated = jax.nn.silu(projected[..., :hidden_quarter]) * projected[..., hidden_quarter:]
        activated = activated.astype(jnp.bfloat16).astype(jnp.float32)
        weighted = (activated * gate_local[:, :, None]).astype(jnp.bfloat16)
        weighted = lax.all_gather(weighted, "tp", axis=0, tiled=False)
        partial = jnp.einsum(
            "qetf,qefd->td", weighted, down_full, preferred_element_type=jnp.float32
        ).astype(jnp.bfloat16)
        outputs.append(partial.reshape(count, tokens, -1))
    by_offset = {}
    index = 0
    for part in outputs:
        for i in range(part.shape[0]):
            by_offset[offsets[index]] = part[i]
            index += 1
    return ring_reduce_scatter(by_offset, ring), qkv_flat


def permute_reduce_scatter(term, width):
    tp_count = lax.axis_size("tp")
    tp_here = lax.axis_index("tp")
    total = lax.dynamic_slice_in_dim(term, tp_here * width, width, axis=1)
    for shift in range(1, tp_count):
        target = (tp_here + shift) % tp_count
        piece = lax.dynamic_slice_in_dim(term, target * width, width, axis=1).astype(jnp.bfloat16)
        pairs = [(i, (i + shift) % tp_count) for i in range(tp_count)]
        total = total + lax.ppermute(piece, "tp", pairs).astype(jnp.float32)
    return total


def permute_gather_dot(rows, weight):
    tp_count = lax.axis_size("tp")
    tp_here = lax.axis_index("tp")
    width = rows.shape[1]
    total = jnp.dot(
        rows,
        lax.dynamic_slice_in_dim(weight, tp_here * width, width, axis=0),
        preferred_element_type=jnp.float32,
    )
    for shift in range(1, tp_count):
        source = (tp_here - shift) % tp_count
        pairs = [(i, (i + shift) % tp_count) for i in range(tp_count)]
        piece = lax.ppermute(rows, "tp", pairs)
        total = total + jnp.dot(
            piece,
            lax.dynamic_slice_in_dim(weight, source * width, width, axis=0),
            preferred_element_type=jnp.float32,
        )
    return total


def ring_order(count):
    half = count // 2
    if count % 2 or count < 4:
        return list(range(count))
    return [2 * i for i in range(half)] + [2 * i + 1 for i in reversed(range(half))]


def ring_all_gather(block, cycle):
    count = len(cycle)
    forward = [(cycle[p], cycle[(p + 1) % count]) for p in range(count)]
    backward = [(cycle[p], cycle[(p - 1) % count]) for p in range(count)]
    offsets, blocks = [0], [block]
    ahead, behind = block, block
    for step in range(1, count // 2 + 1):
        ahead = lax.ppermute(ahead, "seq", forward)
        offsets.append((-step) % count)
        blocks.append(ahead)
        if step < count - count // 2:
            behind = lax.ppermute(behind, "seq", backward)
            offsets.append(step)
            blocks.append(behind)
    return offsets, blocks


def ring_reduce_scatter(by_offset, cycle):
    count = len(cycle)
    width = by_offset[0].shape[1]
    halves = []
    for direction in (1, -1):
        cols = slice(0, width // 2) if direction == 1 else slice(width // 2, width)
        pairs = [(cycle[p], cycle[(p + direction) % count]) for p in range(count)]
        acc = by_offset[(-direction) % count][:, cols].astype(jnp.float32)
        for step in range(count - 1):
            received = lax.ppermute(acc.astype(jnp.bfloat16), "seq", pairs)
            offset = (-direction * (step + 2)) % count
            acc = received.astype(jnp.float32) + by_offset[offset][:, cols].astype(jnp.float32)
        halves.append(acc)
    return jnp.concatenate(halves, axis=1)


def dispatch_experts(moe_in, expert_ids, route_weights, expert_gate_up, expert_down, experts_all, capacity):
    quarter = moe_in.shape[1]
    local_experts = expert_gate_up.shape[0]
    flat_ids = expert_ids.reshape(NEW * TOP)
    onehot = (flat_ids[:, None] == jnp.arange(experts_all, dtype=jnp.int32)[None, :]).astype(
        jnp.int32
    )
    ranks = jnp.sum((jnp.cumsum(onehot, axis=0) - onehot) * onehot, axis=1)
    target = (flat_ids * capacity + ranks).reshape(NEW, TOP)
    slot_ids = jnp.arange(experts_all * capacity, dtype=jnp.int32)
    selector = jnp.sum(
        (target[None, :, :] == slot_ids[:, None, None]).astype(jnp.int32), axis=2
    ).astype(jnp.bfloat16)
    send_rows = jnp.dot(selector, moe_in, preferred_element_type=jnp.float32).astype(jnp.bfloat16)
    send_rows = send_rows.reshape(experts_all, capacity, quarter)
    received = lax.all_to_all(send_rows, "seq", split_axis=0, concat_axis=1, tiled=True)
    hidden_quarter = expert_gate_up.shape[3]
    gate_up_local = expert_gate_up.reshape(local_experts, D, 2 * hidden_quarter)
    weight_rows = gate_up_local
    projected = jnp.einsum(
        "erd,edf->erf",
        lax.all_gather(received, "tp", axis=2, tiled=True),
        weight_rows,
        preferred_element_type=jnp.float32,
    )
    activated = (
        jax.nn.silu(projected[..., :hidden_quarter]) * projected[..., hidden_quarter:]
    ).astype(jnp.bfloat16)
    down_terms = jnp.einsum(
        "erf,efd->erd", activated, expert_down, preferred_element_type=jnp.float32
    )
    expert_result = lax.psum_scatter(
        down_terms.astype(jnp.bfloat16), "tp", scatter_dimension=2, tiled=True
    )
    returned = lax.all_to_all(
        expert_result, "seq", split_axis=1, concat_axis=0, tiled=True
    ).reshape(experts_all * capacity, quarter)
    picked = jnp.take(returned, target, axis=0)
    return jnp.sum(route_weights[:, :, None] * picked.astype(jnp.float32), axis=1)


def body(
    hidden,
    new_queries,
    new_keys,
    new_values,
    cache_keys,
    cache_values,
    cache_lengths,
    out_proj,
    moe_gain,
    expert_ids,
    route_weights,
    expert_gate_up,
    expert_down,
    next_gain,
    qkv_proj,
    query_gain,
    key_gain,
):
    seq_count = lax.axis_size("seq")
    here = lax.axis_index("seq")
    local_experts = expert_gate_up.shape[0]
    experts_all = local_experts * seq_count
    capacity = max(2, 3 * NEW * TOP // (2 * experts_all))
    dense = NEW <= 2 * capacity
    if dense:
        tp_here = lax.axis_index("tp")
        quarter_width = hidden.shape[1]
        tp_count = lax.axis_size("tp")
        pieces = [lax.dynamic_slice_in_dim(expert_down, tp_here * quarter_width, quarter_width, axis=2)]
        for shift in range(1, tp_count):
            target = (tp_here + shift) % tp_count
            piece = lax.dynamic_slice_in_dim(expert_down, target * quarter_width, quarter_width, axis=2)
            pairs = [(i, (i + shift) % tp_count) for i in range(tp_count)]
            pieces.append(lax.ppermute(piece, "tp", pairs))
        order = (tp_here - jnp.arange(tp_count, dtype=jnp.int32)) % tp_count
        down_full = jnp.take(jnp.stack(pieces), order, axis=0)
        gate_up_flat = expert_gate_up.reshape(local_experts, D, -1)
        qkv_flat = qkv_proj.reshape(D, -1)
    local_width = new_queries.shape[1]
    local_heads = local_width // HEAD_DIM
    quarter = hidden.shape[1]
    span = cache_keys.shape[1]
    my_length = lax.dynamic_index_in_dim(cache_lengths, here, 0, keepdims=False)
    attended = flash_attention(
        my_length,
        new_queries,
        cache_keys.reshape(span, local_width),
        cache_values.reshape(span, local_width),
        new_keys,
        new_values,
    )
    if not dense:
        gate_up_flat = expert_gate_up
        qkv_flat = qkv_proj.reshape(D, -1)
    attn_term = jnp.dot(attended, out_proj, preferred_element_type=jnp.float32)
    if dense:
        residual = hidden.astype(jnp.float32) + permute_reduce_scatter(attn_term, local_width)
    else:
        residual = hidden.astype(jnp.float32) + lax.psum_scatter(
            attn_term.astype(jnp.bfloat16), "tp", scatter_dimension=1, tiled=True
        ).astype(jnp.float32)
    square_total = lax.psum(jnp.sum(residual * residual, axis=1), "tp")
    moe_in = (residual * lax.rsqrt(square_total / D + epsilon)[:, None] * moe_gain[None, :]).astype(
        jnp.bfloat16
    )
    if dense:
        moe_term, qkv_flat = dense_experts(
            moe_in, expert_ids, route_weights, gate_up_flat, down_full, qkv_flat, here, experts_all
        )
    else:
        moe_term = dispatch_experts(
            moe_in, expert_ids, route_weights, expert_gate_up, expert_down, experts_all, capacity
        )
    routed = residual + moe_term
    layer_out = routed.astype(jnp.bfloat16)
    scaled = (routed * next_gain[None, :]).astype(jnp.bfloat16)
    weight_rows = qkv_flat
    if dense:
        mixed = permute_gather_dot(scaled, weight_rows)
    else:
        mixed = jnp.dot(
            lax.all_gather(scaled, "tp", axis=1, tiled=True),
            weight_rows,
            preferred_element_type=jnp.float32,
        )
    mixed = mixed.reshape(NEW, 3, local_width)
    squares_routed = jnp.sum(routed * routed, axis=1)
    routed_total, query_raw, key_raw = lax.psum(
        (
            squares_routed,
            jnp.sum(mixed[:, 0] * mixed[:, 0], axis=1),
            jnp.sum(mixed[:, 1] * mixed[:, 1], axis=1),
        ),
        "tp",
    )
    x_scale = lax.rsqrt(routed_total / D + epsilon)
    query_pre = mixed[:, 0] * x_scale[:, None]
    key_pre = mixed[:, 1] * x_scale[:, None]
    query_total = query_raw * x_scale * x_scale
    key_total = key_raw * x_scale * x_scale
    next_query = (
        query_pre * lax.rsqrt(query_total / D + epsilon)[:, None] * query_gain[None, :]
    ).astype(jnp.bfloat16)
    next_key = (key_pre * lax.rsqrt(key_total / D + epsilon)[:, None] * key_gain[None, :]).astype(
        jnp.bfloat16
    )
    next_value = (mixed[:, 2] * x_scale[:, None]).astype(jnp.bfloat16)
    return (layer_out, next_query, next_key, next_value)


def solution(mesh):
    return jax.shard_map(
        body,
        mesh=mesh,
        in_specs=(
            P("seq", "tp"),
            P("seq", "tp"),
            P("seq", "tp"),
            P("seq", "tp"),
            P("seq", None, "tp"),
            P("seq", None, "tp"),
            P(),
            P("tp", None),
            P("tp"),
            P("seq", None),
            P("seq", None),
            P("seq", None, None, "tp"),
            P("seq", "tp", None),
            P("tp"),
            P(None, None, "tp"),
            P("tp"),
            P("tp"),
        ),
        out_specs=(P("seq", "tp"), P("seq", "tp"), P("seq", "tp"), P("seq", "tp")),
        check_vma=False,
    )
```

```python
import functools
import math

import jax
import jax.numpy as jnp
from jax import lax
from jax.experimental import pallas as pl
from jax.experimental.pallas import tpu as pltpu
from jax.sharding import PartitionSpec as P

D = 2048
HEAD_DIM = 128
TOP = 8
NEW = 256


epsilon = 1e-05


def flash_kernel(len_ref, q_ref, k_ref, v_ref, nk_ref, nv_ref, o_ref, m_sc, l_sc, acc_sc, *, block, heads, steps):
    j = pl.program_id(0)
    length = len_ref[0]
    valid = (length + block - 1) // block
    tokens = q_ref.shape[0]
    scale = 1.0 / math.sqrt(HEAD_DIM)

    @pl.when(j == 0)
    def _():
        m_sc[...] = jnp.full(m_sc.shape, -1e30, jnp.float32)
        l_sc[...] = jnp.zeros(l_sc.shape, jnp.float32)
        acc_sc[...] = jnp.zeros(acc_sc.shape, jnp.float32)

    def update(keys_ref, values_ref, allowed):
        for h in range(heads):
            cols = slice(h * HEAD_DIM, (h + 1) * HEAD_DIM)
            q = q_ref[:, cols]
            k = keys_ref[:, cols]
            s = lax.dot_general(q, k, (((1,), (1,)), ((), ())), preferred_element_type=jnp.float32) * scale
            s = jnp.where(allowed, s, -1e30)
            m_old = m_sc[h]
            m_new = jnp.maximum(m_old, jnp.max(s, axis=1, keepdims=True))
            alpha = jnp.exp(m_old - m_new)
            p = jnp.where(allowed, jnp.exp(s - m_new), 0.0)
            l_sc[h] = alpha * l_sc[h] + jnp.sum(p, axis=1, keepdims=True)
            pv = jnp.dot(p.astype(jnp.bfloat16), values_ref[:, cols], preferred_element_type=jnp.float32)
            acc_sc[:, cols] = alpha * acc_sc[:, cols] + pv
            m_sc[h] = m_new

    @pl.when(j < valid)
    def _():
        pos = j * block + lax.broadcasted_iota(jnp.int32, (tokens, block), 1)
        update(k_ref, v_ref, pos < length)

    @pl.when(j == steps - 1)
    def _():
        row = lax.broadcasted_iota(jnp.int32, (tokens, tokens), 0)
        col = lax.broadcasted_iota(jnp.int32, (tokens, tokens), 1)
        update(nk_ref, nv_ref, col <= row)
        for h in range(heads):
            cols = slice(h * HEAD_DIM, (h + 1) * HEAD_DIM)
            o_ref[:, cols] = (acc_sc[:, cols] / l_sc[h]).astype(o_ref.dtype)


def flash_attention(length, queries, cache_k, cache_v, new_k, new_v, block=1024):
    tokens, width = queries.shape
    span = cache_k.shape[0]
    block = min(block, span)
    heads = width // HEAD_DIM
    steps = span // block + 1
    last = span // block - 1

    def cache_map(j, len_ref):
        valid = (len_ref[0] + block - 1) // block
        return (jnp.minimum(j, jnp.maximum(valid - 1, 0)), 0)

    grid_spec = pltpu.PrefetchScalarGridSpec(
        num_scalar_prefetch=1,
        grid=(steps,),
        in_specs=[
            pl.BlockSpec((tokens, width), lambda j, l: (0, 0)),
            pl.BlockSpec((block, width), cache_map),
            pl.BlockSpec((block, width), cache_map),
            pl.BlockSpec((tokens, width), lambda j, l: (0, 0)),
            pl.BlockSpec((tokens, width), lambda j, l: (0, 0)),
        ],
        out_specs=pl.BlockSpec((tokens, width), lambda j, l: (0, 0)),
        scratch_shapes=[
            pltpu.VMEM((heads, tokens, 1), jnp.float32),
            pltpu.VMEM((heads, tokens, 1), jnp.float32),
            pltpu.VMEM((tokens, width), jnp.float32),
        ],
    )
    kernel = functools.partial(flash_kernel, block=block, heads=heads, steps=steps)
    return pl.pallas_call(
        kernel,
        grid_spec=grid_spec,
        out_shape=jax.ShapeDtypeStruct((tokens, width), jnp.bfloat16),
        compiler_params=pltpu.CompilerParams(dimension_semantics=("arbitrary",)),
    )(length.reshape(1), queries, cache_k, cache_v, new_k, new_v)


def dense_experts(moe_in, expert_ids, route_weights, expert_gate_up, down_full, qkv_flat, here, experts_all):
    local_experts = expert_gate_up.shape[0]
    hidden_quarter = expert_gate_up.shape[2] // 2
    tokens, quarter = moe_in.shape
    seq_count = experts_all // local_experts
    gate_w = jnp.sum(
        route_weights[:, :, None]
        * (expert_ids[:, :, None] == jnp.arange(experts_all, dtype=jnp.int32)[None, None, :]),
        axis=1,
    )
    gate_t = jnp.transpose(gate_w)
    gate_hi = gate_t.astype(jnp.bfloat16)
    gate_lo = (gate_t - gate_hi.astype(jnp.float32)).astype(jnp.bfloat16)
    info = jnp.concatenate([gate_hi, gate_lo], axis=0).reshape(-1, quarter)
    packed = jnp.concatenate([moe_in, info], axis=0)
    ring = ring_order(seq_count)
    offsets, blocks = ring_all_gather(packed, ring)
    first = min(len(blocks), 5)
    chunks = [(0, first), (first, len(blocks))] if first < len(blocks) else [(0, first)]
    outputs = []
    for begin, end in chunks:
        gathered = jnp.stack(blocks[begin:end])
        count = end - begin
        rows_q = gathered[:, :tokens].reshape(count * tokens, quarter)
        info_all = gathered[:, tokens:].reshape(count, 2, experts_all, tokens).astype(jnp.float32)
        gate_all = info_all[:, 0] + info_all[:, 1]
        gate_local = lax.dynamic_slice_in_dim(gate_all, here * local_experts, local_experts, axis=1)
        gate_local = jnp.transpose(gate_local, (1, 0, 2)).reshape(local_experts, count * tokens)
        rows = lax.all_gather(rows_q, "tp", axis=0, tiled=False)
        if begin == 0:
            rows, expert_gate_up, qkv_flat, down_full = lax.optimization_barrier(
                (rows, expert_gate_up, qkv_flat, down_full)
            )
        gate_up_split = expert_gate_up.reshape(local_experts, rows.shape[0], quarter, -1)
        projected = jnp.einsum("qtd,eqdf->etf", rows, gate_up_split, preferred_element_type=jnp.float32)
        activated = jax.nn.silu(projected[..., :hidden_quarter]) * projected[..., hidden_quarter:]
        activated = activated.astype(jnp.bfloat16).astype(jnp.float32)
        weighted = (activated * gate_local[:, :, None]).astype(jnp.bfloat16)
        weighted = lax.all_gather(weighted, "tp", axis=0, tiled=False)
        partial = jnp.einsum(
            "qetf,qefd->td", weighted, down_full, preferred_element_type=jnp.float32
        ).astype(jnp.bfloat16)
        outputs.append(partial.reshape(count, tokens, -1))
    by_offset = {}
    index = 0
    for part in outputs:
        for i in range(part.shape[0]):
            by_offset[offsets[index]] = part[i]
            index += 1
    return ring_reduce_scatter(by_offset, ring), qkv_flat


def permute_reduce_scatter(term, width):
    tp_count = lax.axis_size("tp")
    tp_here = lax.axis_index("tp")
    total = lax.dynamic_slice_in_dim(term, tp_here * width, width, axis=1)
    for shift in range(1, tp_count):
        target = (tp_here + shift) % tp_count
        piece = lax.dynamic_slice_in_dim(term, target * width, width, axis=1).astype(jnp.bfloat16)
        pairs = [(i, (i + shift) % tp_count) for i in range(tp_count)]
        total = total + lax.ppermute(piece, "tp", pairs).astype(jnp.float32)
    return total


def permute_gather_dot(rows, weight):
    tp_count = lax.axis_size("tp")
    tp_here = lax.axis_index("tp")
    width = rows.shape[1]
    total = jnp.dot(
        rows,
        lax.dynamic_slice_in_dim(weight, tp_here * width, width, axis=0),
        preferred_element_type=jnp.float32,
    )
    for shift in range(1, tp_count):
        source = (tp_here - shift) % tp_count
        pairs = [(i, (i + shift) % tp_count) for i in range(tp_count)]
        piece = lax.ppermute(rows, "tp", pairs)
        total = total + jnp.dot(
            piece,
            lax.dynamic_slice_in_dim(weight, source * width, width, axis=0),
            preferred_element_type=jnp.float32,
        )
    return total


def ring_order(count):
    half = count // 2
    if count % 2 or count < 4:
        return list(range(count))
    return [2 * i for i in range(half)] + [2 * i + 1 for i in reversed(range(half))]


def ring_all_gather(block, cycle):
    count = len(cycle)
    forward = [(cycle[p], cycle[(p + 1) % count]) for p in range(count)]
    backward = [(cycle[p], cycle[(p - 1) % count]) for p in range(count)]
    offsets, blocks = [0], [block]
    ahead, behind = block, block
    for step in range(1, count // 2 + 1):
        ahead = lax.ppermute(ahead, "seq", forward)
        offsets.append((-step) % count)
        blocks.append(ahead)
        if step < count - count // 2:
            behind = lax.ppermute(behind, "seq", backward)
            offsets.append(step)
            blocks.append(behind)
    return offsets, blocks


def ring_reduce_scatter(by_offset, cycle):
    count = len(cycle)
    forward = [(cycle[p], cycle[(p + 1) % count]) for p in range(count)]
    backward = [(cycle[p], cycle[(p - 1) % count]) for p in range(count)]

    def block(offset):
        return by_offset[offset % count].astype(jnp.float32)

    total = block(0)
    for pairs, hops, sign in ((forward, count - 1 - count // 2, 1), (backward, count // 2, -1)):
        if hops == 0:
            continue
        acc = block(sign * hops)
        for step in range(1, hops + 1):
            received = lax.ppermute(acc.astype(jnp.bfloat16), "seq", pairs).astype(jnp.float32)
            if step < hops:
                acc = received + block(sign * (hops - step))
            else:
                total = total + received
    return total


def dispatch_experts(moe_in, expert_ids, route_weights, expert_gate_up, expert_down, experts_all, capacity):
    quarter = moe_in.shape[1]
    local_experts = expert_gate_up.shape[0]
    flat_ids = expert_ids.reshape(NEW * TOP)
    onehot = (flat_ids[:, None] == jnp.arange(experts_all, dtype=jnp.int32)[None, :]).astype(
        jnp.int32
    )
    ranks = jnp.sum((jnp.cumsum(onehot, axis=0) - onehot) * onehot, axis=1)
    target = (flat_ids * capacity + ranks).reshape(NEW, TOP)
    slot_ids = jnp.arange(experts_all * capacity, dtype=jnp.int32)
    selector = jnp.sum(
        (target[None, :, :] == slot_ids[:, None, None]).astype(jnp.int32), axis=2
    ).astype(jnp.bfloat16)
    send_rows = jnp.dot(selector, moe_in, preferred_element_type=jnp.float32).astype(jnp.bfloat16)
    send_rows = send_rows.reshape(experts_all, capacity, quarter)
    received = lax.all_to_all(send_rows, "seq", split_axis=0, concat_axis=1, tiled=True)
    hidden_quarter = expert_gate_up.shape[3]
    gate_up_local = expert_gate_up.reshape(local_experts, D, 2 * hidden_quarter)
    weight_rows = gate_up_local
    projected = jnp.einsum(
        "erd,edf->erf",
        lax.all_gather(received, "tp", axis=2, tiled=True),
        weight_rows,
        preferred_element_type=jnp.float32,
    )
    activated = (
        jax.nn.silu(projected[..., :hidden_quarter]) * projected[..., hidden_quarter:]
    ).astype(jnp.bfloat16)
    down_terms = jnp.einsum(
        "erf,efd->erd", activated, expert_down, preferred_element_type=jnp.float32
    )
    expert_result = lax.psum_scatter(
        down_terms.astype(jnp.bfloat16), "tp", scatter_dimension=2, tiled=True
    )
    returned = lax.all_to_all(
        expert_result, "seq", split_axis=1, concat_axis=0, tiled=True
    ).reshape(experts_all * capacity, quarter)
    picked = jnp.take(returned, target, axis=0)
    return jnp.sum(route_weights[:, :, None] * picked.astype(jnp.float32), axis=1)


def body(
    hidden,
    new_queries,
    new_keys,
    new_values,
    cache_keys,
    cache_values,
    cache_lengths,
    out_proj,
    moe_gain,
    expert_ids,
    route_weights,
    expert_gate_up,
    expert_down,
    next_gain,
    qkv_proj,
    query_gain,
    key_gain,
):
    seq_count = lax.axis_size("seq")
    here = lax.axis_index("seq")
    local_experts = expert_gate_up.shape[0]
    experts_all = local_experts * seq_count
    capacity = max(2, 3 * NEW * TOP // (2 * experts_all))
    dense = NEW <= 2 * capacity
    if dense:
        tp_here = lax.axis_index("tp")
        quarter_width = hidden.shape[1]
        tp_count = lax.axis_size("tp")
        pieces = [lax.dynamic_slice_in_dim(expert_down, tp_here * quarter_width, quarter_width, axis=2)]
        for shift in range(1, tp_count):
            target = (tp_here + shift) % tp_count
            piece = lax.dynamic_slice_in_dim(expert_down, target * quarter_width, quarter_width, axis=2)
            pairs = [(i, (i + shift) % tp_count) for i in range(tp_count)]
            pieces.append(lax.ppermute(piece, "tp", pairs))
        order = (tp_here - jnp.arange(tp_count, dtype=jnp.int32)) % tp_count
        down_full = jnp.take(jnp.stack(pieces), order, axis=0)
        gate_up_flat = expert_gate_up.reshape(local_experts, D, -1)
        qkv_flat = qkv_proj.reshape(D, -1)
    local_width = new_queries.shape[1]
    local_heads = local_width // HEAD_DIM
    quarter = hidden.shape[1]
    span = cache_keys.shape[1]
    my_length = lax.dynamic_index_in_dim(cache_lengths, here, 0, keepdims=False)
    attended = flash_attention(
        my_length,
        new_queries,
        cache_keys.reshape(span, local_width),
        cache_values.reshape(span, local_width),
        new_keys,
        new_values,
    )
    if not dense:
        gate_up_flat = expert_gate_up
        qkv_flat = qkv_proj.reshape(D, -1)
    attn_term = jnp.dot(attended, out_proj, preferred_element_type=jnp.float32)
    if dense:
        residual = hidden.astype(jnp.float32) + permute_reduce_scatter(attn_term, local_width)
    else:
        residual = hidden.astype(jnp.float32) + lax.psum_scatter(
            attn_term.astype(jnp.bfloat16), "tp", scatter_dimension=1, tiled=True
        ).astype(jnp.float32)
    square_total = lax.psum(jnp.sum(residual * residual, axis=1), "tp")
    moe_in = (residual * lax.rsqrt(square_total / D + epsilon)[:, None] * moe_gain[None, :]).astype(
        jnp.bfloat16
    )
    if dense:
        moe_term, qkv_flat = dense_experts(
            moe_in, expert_ids, route_weights, gate_up_flat, down_full, qkv_flat, here, experts_all
        )
    else:
        moe_term = dispatch_experts(
            moe_in, expert_ids, route_weights, expert_gate_up, expert_down, experts_all, capacity
        )
    routed = residual + moe_term
    layer_out = routed.astype(jnp.bfloat16)
    scaled = (routed * next_gain[None, :]).astype(jnp.bfloat16)
    weight_rows = qkv_flat
    if dense:
        mixed = permute_gather_dot(scaled, weight_rows)
    else:
        mixed = jnp.dot(
            lax.all_gather(scaled, "tp", axis=1, tiled=True),
            weight_rows,
            preferred_element_type=jnp.float32,
        )
    mixed = mixed.reshape(NEW, 3, local_width)
    squares_routed = jnp.sum(routed * routed, axis=1)
    routed_total, query_raw, key_raw = lax.psum(
        (
            squares_routed,
            jnp.sum(mixed[:, 0] * mixed[:, 0], axis=1),
            jnp.sum(mixed[:, 1] * mixed[:, 1], axis=1),
        ),
        "tp",
    )
    x_scale = lax.rsqrt(routed_total / D + epsilon)
    query_pre = mixed[:, 0] * x_scale[:, None]
    key_pre = mixed[:, 1] * x_scale[:, None]
    query_total = query_raw * x_scale * x_scale
    key_total = key_raw * x_scale * x_scale
    next_query = (
        query_pre * lax.rsqrt(query_total / D + epsilon)[:, None] * query_gain[None, :]
    ).astype(jnp.bfloat16)
    next_key = (key_pre * lax.rsqrt(key_total / D + epsilon)[:, None] * key_gain[None, :]).astype(
        jnp.bfloat16
    )
    next_value = (mixed[:, 2] * x_scale[:, None]).astype(jnp.bfloat16)
    return (layer_out, next_query, next_key, next_value)


def solution(mesh):
    return jax.shard_map(
        body,
        mesh=mesh,
        in_specs=(
            P("seq", "tp"),
            P("seq", "tp"),
            P("seq", "tp"),
            P("seq", "tp"),
            P("seq", None, "tp"),
            P("seq", None, "tp"),
            P(),
            P("tp", None),
            P("tp"),
            P("seq", None),
            P("seq", None),
            P("seq", None, None, "tp"),
            P("seq", "tp", None),
            P("tp"),
            P(None, None, "tp"),
            P("tp"),
            P("tp"),
        ),
        out_specs=(P("seq", "tp"), P("seq", "tp"), P("seq", "tp"), P("seq", "tp")),
        check_vma=False,
    )
```

```python
import functools
import math

import jax
import jax.numpy as jnp
from jax import lax
from jax.experimental import pallas as pl
from jax.experimental.pallas import tpu as pltpu
from jax.sharding import PartitionSpec as P

D = 2048
HEAD_DIM = 128
TOP = 8
NEW = 256


epsilon = 1e-05


def flash_kernel(len_ref, q_ref, k_ref, v_ref, nk_ref, nv_ref, o_ref, m_sc, l_sc, acc_sc, *, block, heads, steps):
    j = pl.program_id(0)
    length = len_ref[0]
    valid = (length + block - 1) // block
    tokens = q_ref.shape[0]
    scale = 1.0 / math.sqrt(HEAD_DIM)

    @pl.when(j == 0)
    def _():
        m_sc[...] = jnp.full(m_sc.shape, -1e30, jnp.float32)
        l_sc[...] = jnp.zeros(l_sc.shape, jnp.float32)
        acc_sc[...] = jnp.zeros(acc_sc.shape, jnp.float32)

    def update(keys_ref, values_ref, allowed):
        for h in range(heads):
            cols = slice(h * HEAD_DIM, (h + 1) * HEAD_DIM)
            q = q_ref[:, cols]
            k = keys_ref[:, cols]
            s = lax.dot_general(q, k, (((1,), (1,)), ((), ())), preferred_element_type=jnp.float32) * scale
            s = jnp.where(allowed, s, -1e30)
            m_old = m_sc[h]
            m_new = jnp.maximum(m_old, jnp.max(s, axis=1, keepdims=True))
            alpha = jnp.exp(m_old - m_new)
            p = jnp.where(allowed, jnp.exp(s - m_new), 0.0)
            l_sc[h] = alpha * l_sc[h] + jnp.sum(p, axis=1, keepdims=True)
            pv = jnp.dot(p.astype(jnp.bfloat16), values_ref[:, cols], preferred_element_type=jnp.float32)
            acc_sc[:, cols] = alpha * acc_sc[:, cols] + pv
            m_sc[h] = m_new

    @pl.when(j < valid)
    def _():
        pos = j * block + lax.broadcasted_iota(jnp.int32, (tokens, block), 1)
        update(k_ref, v_ref, pos < length)

    @pl.when(j == steps - 1)
    def _():
        row = lax.broadcasted_iota(jnp.int32, (tokens, tokens), 0)
        col = lax.broadcasted_iota(jnp.int32, (tokens, tokens), 1)
        update(nk_ref, nv_ref, col <= row)
        for h in range(heads):
            cols = slice(h * HEAD_DIM, (h + 1) * HEAD_DIM)
            o_ref[:, cols] = (acc_sc[:, cols] / l_sc[h]).astype(o_ref.dtype)


def flash_attention(length, queries, cache_k, cache_v, new_k, new_v, block=1024):
    tokens, width = queries.shape
    span = cache_k.shape[0]
    block = min(block, span)
    heads = width // HEAD_DIM
    steps = span // block + 1
    last = span // block - 1

    def cache_map(j, len_ref):
        valid = (len_ref[0] + block - 1) // block
        return (jnp.minimum(j, jnp.maximum(valid - 1, 0)), 0)

    grid_spec = pltpu.PrefetchScalarGridSpec(
        num_scalar_prefetch=1,
        grid=(steps,),
        in_specs=[
            pl.BlockSpec((tokens, width), lambda j, l: (0, 0)),
            pl.BlockSpec((block, width), cache_map),
            pl.BlockSpec((block, width), cache_map),
            pl.BlockSpec((tokens, width), lambda j, l: (0, 0)),
            pl.BlockSpec((tokens, width), lambda j, l: (0, 0)),
        ],
        out_specs=pl.BlockSpec((tokens, width), lambda j, l: (0, 0)),
        scratch_shapes=[
            pltpu.VMEM((heads, tokens, 1), jnp.float32),
            pltpu.VMEM((heads, tokens, 1), jnp.float32),
            pltpu.VMEM((tokens, width), jnp.float32),
        ],
    )
    kernel = functools.partial(flash_kernel, block=block, heads=heads, steps=steps)
    return pl.pallas_call(
        kernel,
        grid_spec=grid_spec,
        out_shape=jax.ShapeDtypeStruct((tokens, width), jnp.bfloat16),
        compiler_params=pltpu.CompilerParams(dimension_semantics=("arbitrary",)),
    )(length.reshape(1), queries, cache_k, cache_v, new_k, new_v)


def dense_experts(moe_in, expert_ids, route_weights, expert_gate_up, down_full, qkv_flat, here, experts_all):
    local_experts = expert_gate_up.shape[0]
    hidden_quarter = expert_gate_up.shape[2] // 2
    tokens, quarter = moe_in.shape
    seq_count = experts_all // local_experts
    gate_w = jnp.sum(
        route_weights[:, :, None]
        * (expert_ids[:, :, None] == jnp.arange(experts_all, dtype=jnp.int32)[None, None, :]),
        axis=1,
    )
    gate_t = jnp.transpose(gate_w)
    gate_hi = gate_t.astype(jnp.bfloat16)
    gate_lo = (gate_t - gate_hi.astype(jnp.float32)).astype(jnp.bfloat16)
    info = jnp.concatenate([gate_hi, gate_lo], axis=0).reshape(-1, quarter)
    packed = jnp.concatenate([moe_in, info], axis=0)
    ring = ring_order(seq_count)
    offsets, blocks = ring_all_gather(packed, ring)
    first = min(len(blocks), 5)
    chunks = [(0, first), (first, len(blocks))] if first < len(blocks) else [(0, first)]
    outputs = []
    for begin, end in chunks:
        gathered = jnp.stack(blocks[begin:end])
        count = end - begin
        rows_q = gathered[:, :tokens].reshape(count * tokens, quarter)
        info_all = gathered[:, tokens:].reshape(count, 2, experts_all, tokens).astype(jnp.float32)
        gate_all = info_all[:, 0] + info_all[:, 1]
        gate_local = lax.dynamic_slice_in_dim(gate_all, here * local_experts, local_experts, axis=1)
        gate_local = jnp.transpose(gate_local, (1, 0, 2)).reshape(local_experts, count * tokens)
        rows = lax.all_gather(rows_q, "tp", axis=0, tiled=False)
        if begin == 0:
            rows, expert_gate_up, qkv_flat = lax.optimization_barrier((rows, expert_gate_up, qkv_flat))
        gate_up_split = expert_gate_up.reshape(local_experts, rows.shape[0], quarter, -1)
        projected = jnp.einsum("qtd,eqdf->etf", rows, gate_up_split, preferred_element_type=jnp.float32)
        activated = jax.nn.silu(projected[..., :hidden_quarter]) * projected[..., hidden_quarter:]
        activated = activated.astype(jnp.bfloat16).astype(jnp.float32)
        weighted = (activated * gate_local[:, :, None]).astype(jnp.bfloat16)
        weighted = lax.all_gather(weighted, "tp", axis=0, tiled=False)
        partial = jnp.einsum(
            "qetf,qefd->td", weighted, down_full, preferred_element_type=jnp.float32
        ).astype(jnp.bfloat16)
        outputs.append(partial.reshape(count, tokens, -1))
    by_offset = {}
    index = 0
    for part in outputs:
        for i in range(part.shape[0]):
            by_offset[offsets[index]] = part[i]
            index += 1
    return ring_reduce_scatter(by_offset, ring), qkv_flat


def permute_reduce_scatter(term, width):
    tp_count = lax.axis_size("tp")
    tp_here = lax.axis_index("tp")
    total = lax.dynamic_slice_in_dim(term, tp_here * width, width, axis=1)
    for shift in range(1, tp_count):
        target = (tp_here + shift) % tp_count
        piece = lax.dynamic_slice_in_dim(term, target * width, width, axis=1).astype(jnp.bfloat16)
        pairs = [(i, (i + shift) % tp_count) for i in range(tp_count)]
        total = total + lax.ppermute(piece, "tp", pairs).astype(jnp.float32)
    return total


def permute_gather_dot(rows, weight):
    tp_count = lax.axis_size("tp")
    tp_here = lax.axis_index("tp")
    width = rows.shape[1]
    total = jnp.dot(
        rows,
        lax.dynamic_slice_in_dim(weight, tp_here * width, width, axis=0),
        preferred_element_type=jnp.float32,
    )
    for shift in range(1, tp_count):
        source = (tp_here - shift) % tp_count
        pairs = [(i, (i + shift) % tp_count) for i in range(tp_count)]
        piece = lax.ppermute(rows, "tp", pairs)
        total = total + jnp.dot(
            piece,
            lax.dynamic_slice_in_dim(weight, source * width, width, axis=0),
            preferred_element_type=jnp.float32,
        )
    return total


def ring_order(count):
    half = count // 2
    if count % 2 or count < 4:
        return list(range(count))
    return [2 * i for i in range(half)] + [2 * i + 1 for i in reversed(range(half))]


def ring_all_gather(block, cycle):
    count = len(cycle)
    forward = [(cycle[p], cycle[(p + 1) % count]) for p in range(count)]
    backward = [(cycle[p], cycle[(p - 1) % count]) for p in range(count)]
    offsets, blocks = [0], [block]
    ahead, behind = block, block
    for step in range(1, count // 2 + 1):
        ahead = lax.ppermute(ahead, "seq", forward)
        offsets.append((-step) % count)
        blocks.append(ahead)
        if step < count - count // 2:
            behind = lax.ppermute(behind, "seq", backward)
            offsets.append(step)
            blocks.append(behind)
    return offsets, blocks


def ring_reduce_scatter(by_offset, cycle):
    count = len(cycle)
    forward = [(cycle[p], cycle[(p + 1) % count]) for p in range(count)]
    backward = [(cycle[p], cycle[(p - 1) % count]) for p in range(count)]

    def block(offset):
        return by_offset[offset % count].astype(jnp.float32)

    total = block(0)
    for pairs, hops, sign in ((forward, count - 1 - count // 2, 1), (backward, count // 2, -1)):
        if hops == 0:
            continue
        acc = block(sign * hops)
        for step in range(1, hops + 1):
            received = lax.ppermute(acc.astype(jnp.bfloat16), "seq", pairs).astype(jnp.float32)
            if step < hops:
                acc = received + block(sign * (hops - step))
            else:
                total = total + received
    return total


def dispatch_experts(moe_in, expert_ids, route_weights, expert_gate_up, expert_down, experts_all, capacity):
    quarter = moe_in.shape[1]
    local_experts = expert_gate_up.shape[0]
    flat_ids = expert_ids.reshape(NEW * TOP)
    onehot = (flat_ids[:, None] == jnp.arange(experts_all, dtype=jnp.int32)[None, :]).astype(
        jnp.int32
    )
    ranks = jnp.sum((jnp.cumsum(onehot, axis=0) - onehot) * onehot, axis=1)
    target = (flat_ids * capacity + ranks).reshape(NEW, TOP)
    slot_ids = jnp.arange(experts_all * capacity, dtype=jnp.int32)
    selector = jnp.sum(
        (target[None, :, :] == slot_ids[:, None, None]).astype(jnp.int32), axis=2
    ).astype(jnp.bfloat16)
    send_rows = jnp.dot(selector, moe_in, preferred_element_type=jnp.float32).astype(jnp.bfloat16)
    send_rows = send_rows.reshape(experts_all, capacity, quarter)
    received = lax.all_to_all(send_rows, "seq", split_axis=0, concat_axis=1, tiled=True)
    hidden_quarter = expert_gate_up.shape[3]
    gate_up_local = expert_gate_up.reshape(local_experts, D, 2 * hidden_quarter)
    weight_rows = gate_up_local
    projected = jnp.einsum(
        "erd,edf->erf",
        lax.all_gather(received, "tp", axis=2, tiled=True),
        weight_rows,
        preferred_element_type=jnp.float32,
    )
    activated = (
        jax.nn.silu(projected[..., :hidden_quarter]) * projected[..., hidden_quarter:]
    ).astype(jnp.bfloat16)
    down_terms = jnp.einsum(
        "erf,efd->erd", activated, expert_down, preferred_element_type=jnp.float32
    )
    expert_result = lax.psum_scatter(
        down_terms.astype(jnp.bfloat16), "tp", scatter_dimension=2, tiled=True
    )
    returned = lax.all_to_all(
        expert_result, "seq", split_axis=1, concat_axis=0, tiled=True
    ).reshape(experts_all * capacity, quarter)
    picked = jnp.take(returned, target, axis=0)
    return jnp.sum(route_weights[:, :, None] * picked.astype(jnp.float32), axis=1)


def body(
    hidden,
    new_queries,
    new_keys,
    new_values,
    cache_keys,
    cache_values,
    cache_lengths,
    out_proj,
    moe_gain,
    expert_ids,
    route_weights,
    expert_gate_up,
    expert_down,
    next_gain,
    qkv_proj,
    query_gain,
    key_gain,
):
    seq_count = lax.axis_size("seq")
    here = lax.axis_index("seq")
    local_experts = expert_gate_up.shape[0]
    experts_all = local_experts * seq_count
    capacity = max(2, 3 * NEW * TOP // (2 * experts_all))
    dense = NEW <= 2 * capacity
    if dense:
        tp_here = lax.axis_index("tp")
        quarter_width = hidden.shape[1]
        tp_count = lax.axis_size("tp")
        pieces = [lax.dynamic_slice_in_dim(expert_down, tp_here * quarter_width, quarter_width, axis=2)]
        for shift in range(1, tp_count):
            target = (tp_here + shift) % tp_count
            piece = lax.dynamic_slice_in_dim(expert_down, target * quarter_width, quarter_width, axis=2)
            pairs = [(i, (i + shift) % tp_count) for i in range(tp_count)]
            pieces.append(lax.ppermute(piece, "tp", pairs))
        order = (tp_here - jnp.arange(tp_count, dtype=jnp.int32)) % tp_count
        down_full = jnp.take(jnp.stack(pieces), order, axis=0)
        gate_up_flat = expert_gate_up.reshape(local_experts, D, -1)
        qkv_flat = qkv_proj.reshape(D, -1)
    local_width = new_queries.shape[1]
    local_heads = local_width // HEAD_DIM
    quarter = hidden.shape[1]
    span = cache_keys.shape[1]
    my_length = lax.dynamic_index_in_dim(cache_lengths, here, 0, keepdims=False)
    attended = flash_attention(
        my_length,
        new_queries,
        cache_keys.reshape(span, local_width),
        cache_values.reshape(span, local_width),
        new_keys,
        new_values,
    )
    if dense:
        attended, down_full = lax.optimization_barrier((attended, down_full))
    else:
        gate_up_flat = expert_gate_up
        qkv_flat = qkv_proj.reshape(D, -1)
    attn_term = jnp.dot(attended, out_proj, preferred_element_type=jnp.float32)
    if dense:
        residual = hidden.astype(jnp.float32) + permute_reduce_scatter(attn_term, local_width)
    else:
        residual = hidden.astype(jnp.float32) + lax.psum_scatter(
            attn_term.astype(jnp.bfloat16), "tp", scatter_dimension=1, tiled=True
        ).astype(jnp.float32)
    square_total = lax.psum(jnp.sum(residual * residual, axis=1), "tp")
    moe_in = (residual * lax.rsqrt(square_total / D + epsilon)[:, None] * moe_gain[None, :]).astype(
        jnp.bfloat16
    )
    if dense:
        moe_term, qkv_flat = dense_experts(
            moe_in, expert_ids, route_weights, gate_up_flat, down_full, qkv_flat, here, experts_all
        )
    else:
        moe_term = dispatch_experts(
            moe_in, expert_ids, route_weights, expert_gate_up, expert_down, experts_all, capacity
        )
    routed = residual + moe_term
    layer_out = routed.astype(jnp.bfloat16)
    scaled = (routed * next_gain[None, :]).astype(jnp.bfloat16)
    weight_rows = qkv_flat
    if dense:
        mixed = permute_gather_dot(scaled, weight_rows)
    else:
        mixed = jnp.dot(
            lax.all_gather(scaled, "tp", axis=1, tiled=True),
            weight_rows,
            preferred_element_type=jnp.float32,
        )
    mixed = mixed.reshape(NEW, 3, local_width)
    squares_routed = jnp.sum(routed * routed, axis=1)
    routed_total, query_raw, key_raw = lax.psum(
        (
            squares_routed,
            jnp.sum(mixed[:, 0] * mixed[:, 0], axis=1),
            jnp.sum(mixed[:, 1] * mixed[:, 1], axis=1),
        ),
        "tp",
    )
    x_scale = lax.rsqrt(routed_total / D + epsilon)
    query_pre = mixed[:, 0] * x_scale[:, None]
    key_pre = mixed[:, 1] * x_scale[:, None]
    query_total = query_raw * x_scale * x_scale
    key_total = key_raw * x_scale * x_scale
    next_query = (
        query_pre * lax.rsqrt(query_total / D + epsilon)[:, None] * query_gain[None, :]
    ).astype(jnp.bfloat16)
    next_key = (key_pre * lax.rsqrt(key_total / D + epsilon)[:, None] * key_gain[None, :]).astype(
        jnp.bfloat16
    )
    next_value = (mixed[:, 2] * x_scale[:, None]).astype(jnp.bfloat16)
    return (layer_out, next_query, next_key, next_value)


def solution(mesh):
    return jax.shard_map(
        body,
        mesh=mesh,
        in_specs=(
            P("seq", "tp"),
            P("seq", "tp"),
            P("seq", "tp"),
            P("seq", "tp"),
            P("seq", None, "tp"),
            P("seq", None, "tp"),
            P(),
            P("tp", None),
            P("tp"),
            P("seq", None),
            P("seq", None),
            P("seq", None, None, "tp"),
            P("seq", "tp", None),
            P("tp"),
            P(None, None, "tp"),
            P("tp"),
            P("tp"),
        ),
        out_specs=(P("seq", "tp"), P("seq", "tp"), P("seq", "tp"), P("seq", "tp")),
        check_vma=False,
    )
```

```python
import functools
import math

import jax
import jax.numpy as jnp
from jax import lax
from jax.experimental import pallas as pl
from jax.experimental.pallas import tpu as pltpu
from jax.sharding import PartitionSpec as P

D = 2048
HEAD_DIM = 128
TOP = 8
NEW = 256


epsilon = 1e-05


def flash_kernel(len_ref, q_ref, k_ref, v_ref, nk_ref, nv_ref, o_ref, m_sc, l_sc, acc_sc, *, block, heads, steps):
    j = pl.program_id(0)
    length = len_ref[0]
    valid = (length + block - 1) // block
    tokens = q_ref.shape[0]
    scale = 1.0 / math.sqrt(HEAD_DIM)

    @pl.when(j == 0)
    def _():
        m_sc[...] = jnp.full(m_sc.shape, -1e30, jnp.float32)
        l_sc[...] = jnp.zeros(l_sc.shape, jnp.float32)
        acc_sc[...] = jnp.zeros(acc_sc.shape, jnp.float32)

    def update(keys_ref, values_ref, allowed):
        for h in range(heads):
            cols = slice(h * HEAD_DIM, (h + 1) * HEAD_DIM)
            q = q_ref[:, cols]
            k = keys_ref[:, cols]
            s = lax.dot_general(q, k, (((1,), (1,)), ((), ())), preferred_element_type=jnp.float32) * scale
            s = jnp.where(allowed, s, -1e30)
            m_old = m_sc[h]
            m_new = jnp.maximum(m_old, jnp.max(s, axis=1, keepdims=True))
            alpha = jnp.exp(m_old - m_new)
            p = jnp.where(allowed, jnp.exp(s - m_new), 0.0)
            l_sc[h] = alpha * l_sc[h] + jnp.sum(p, axis=1, keepdims=True)
            pv = jnp.dot(p.astype(jnp.bfloat16), values_ref[:, cols], preferred_element_type=jnp.float32)
            acc_sc[:, cols] = alpha * acc_sc[:, cols] + pv
            m_sc[h] = m_new

    @pl.when(j < valid)
    def _():
        pos = j * block + lax.broadcasted_iota(jnp.int32, (tokens, block), 1)
        update(k_ref, v_ref, pos < length)

    @pl.when(j == steps - 1)
    def _():
        row = lax.broadcasted_iota(jnp.int32, (tokens, tokens), 0)
        col = lax.broadcasted_iota(jnp.int32, (tokens, tokens), 1)
        update(nk_ref, nv_ref, col <= row)
        for h in range(heads):
            cols = slice(h * HEAD_DIM, (h + 1) * HEAD_DIM)
            o_ref[:, cols] = (acc_sc[:, cols] / l_sc[h]).astype(o_ref.dtype)


def flash_attention(length, queries, cache_k, cache_v, new_k, new_v, block=1024):
    tokens, width = queries.shape
    span = cache_k.shape[0]
    block = min(block, span)
    heads = width // HEAD_DIM
    steps = span // block + 1
    last = span // block - 1

    def cache_map(j, len_ref):
        valid = (len_ref[0] + block - 1) // block
        return (jnp.minimum(j, jnp.maximum(valid - 1, 0)), 0)

    grid_spec = pltpu.PrefetchScalarGridSpec(
        num_scalar_prefetch=1,
        grid=(steps,),
        in_specs=[
            pl.BlockSpec((tokens, width), lambda j, l: (0, 0)),
            pl.BlockSpec((block, width), cache_map),
            pl.BlockSpec((block, width), cache_map),
            pl.BlockSpec((tokens, width), lambda j, l: (0, 0)),
            pl.BlockSpec((tokens, width), lambda j, l: (0, 0)),
        ],
        out_specs=pl.BlockSpec((tokens, width), lambda j, l: (0, 0)),
        scratch_shapes=[
            pltpu.VMEM((heads, tokens, 1), jnp.float32),
            pltpu.VMEM((heads, tokens, 1), jnp.float32),
            pltpu.VMEM((tokens, width), jnp.float32),
        ],
    )
    kernel = functools.partial(flash_kernel, block=block, heads=heads, steps=steps)
    return pl.pallas_call(
        kernel,
        grid_spec=grid_spec,
        out_shape=jax.ShapeDtypeStruct((tokens, width), jnp.bfloat16),
        compiler_params=pltpu.CompilerParams(dimension_semantics=("arbitrary",)),
    )(length.reshape(1), queries, cache_k, cache_v, new_k, new_v)


def dense_experts(moe_in, expert_ids, route_weights, expert_gate_up, down_full, qkv_flat, here, experts_all):
    local_experts = expert_gate_up.shape[0]
    hidden_quarter = expert_gate_up.shape[2] // 2
    tokens, quarter = moe_in.shape
    seq_count = experts_all // local_experts
    gate_w = jnp.sum(
        route_weights[:, :, None]
        * (expert_ids[:, :, None] == jnp.arange(experts_all, dtype=jnp.int32)[None, None, :]),
        axis=1,
    )
    gate_t = jnp.transpose(gate_w)
    gate_hi = gate_t.astype(jnp.bfloat16)
    gate_lo = (gate_t - gate_hi.astype(jnp.float32)).astype(jnp.bfloat16)
    info = jnp.concatenate([gate_hi, gate_lo], axis=0).reshape(-1, quarter)
    packed = jnp.concatenate([moe_in, info], axis=0)
    ring = ring_order(seq_count)
    offsets, blocks = ring_all_gather(packed, ring)
    cuts = sorted({0, min(3, len(blocks)), min(6, len(blocks)), len(blocks)})
    chunks = list(zip(cuts[:-1], cuts[1:]))
    outputs = []
    for begin, end in chunks:
        gathered = jnp.stack(blocks[begin:end])
        count = end - begin
        rows_q = gathered[:, :tokens].reshape(count * tokens, quarter)
        info_all = gathered[:, tokens:].reshape(count, 2, experts_all, tokens).astype(jnp.float32)
        gate_all = info_all[:, 0] + info_all[:, 1]
        gate_local = lax.dynamic_slice_in_dim(gate_all, here * local_experts, local_experts, axis=1)
        gate_local = jnp.transpose(gate_local, (1, 0, 2)).reshape(local_experts, count * tokens)
        rows = lax.all_gather(rows_q, "tp", axis=0, tiled=False)
        if begin == 0:
            rows, expert_gate_up, qkv_flat = lax.optimization_barrier((rows, expert_gate_up, qkv_flat))
        gate_up_split = expert_gate_up.reshape(local_experts, rows.shape[0], quarter, -1)
        projected = jnp.einsum("qtd,eqdf->etf", rows, gate_up_split, preferred_element_type=jnp.float32)
        activated = jax.nn.silu(projected[..., :hidden_quarter]) * projected[..., hidden_quarter:]
        activated = activated.astype(jnp.bfloat16).astype(jnp.float32)
        weighted = (activated * gate_local[:, :, None]).astype(jnp.bfloat16)
        weighted = lax.all_gather(weighted, "tp", axis=0, tiled=False)
        partial = jnp.einsum(
            "qetf,qefd->td", weighted, down_full, preferred_element_type=jnp.float32
        ).astype(jnp.bfloat16)
        outputs.append(partial.reshape(count, tokens, -1))
    by_offset = {}
    index = 0
    for part in outputs:
        for i in range(part.shape[0]):
            by_offset[offsets[index]] = part[i]
            index += 1
    return ring_reduce_scatter(by_offset, ring), qkv_flat


def permute_reduce_scatter(term, width):
    tp_count = lax.axis_size("tp")
    tp_here = lax.axis_index("tp")
    total = lax.dynamic_slice_in_dim(term, tp_here * width, width, axis=1)
    for shift in range(1, tp_count):
        target = (tp_here + shift) % tp_count
        piece = lax.dynamic_slice_in_dim(term, target * width, width, axis=1).astype(jnp.bfloat16)
        pairs = [(i, (i + shift) % tp_count) for i in range(tp_count)]
        total = total + lax.ppermute(piece, "tp", pairs).astype(jnp.float32)
    return total


def permute_gather_dot(rows, weight):
    tp_count = lax.axis_size("tp")
    tp_here = lax.axis_index("tp")
    width = rows.shape[1]
    total = jnp.dot(
        rows,
        lax.dynamic_slice_in_dim(weight, tp_here * width, width, axis=0),
        preferred_element_type=jnp.float32,
    )
    for shift in range(1, tp_count):
        source = (tp_here - shift) % tp_count
        pairs = [(i, (i + shift) % tp_count) for i in range(tp_count)]
        piece = lax.ppermute(rows, "tp", pairs)
        total = total + jnp.dot(
            piece,
            lax.dynamic_slice_in_dim(weight, source * width, width, axis=0),
            preferred_element_type=jnp.float32,
        )
    return total


def ring_order(count):
    half = count // 2
    if count % 2 or count < 4:
        return list(range(count))
    return [2 * i for i in range(half)] + [2 * i + 1 for i in reversed(range(half))]


def ring_all_gather(block, cycle):
    count = len(cycle)
    forward = [(cycle[p], cycle[(p + 1) % count]) for p in range(count)]
    backward = [(cycle[p], cycle[(p - 1) % count]) for p in range(count)]
    offsets, blocks = [0], [block]
    ahead, behind = block, block
    for step in range(1, count // 2 + 1):
        ahead = lax.ppermute(ahead, "seq", forward)
        offsets.append((-step) % count)
        blocks.append(ahead)
        if step < count - count // 2:
            behind = lax.ppermute(behind, "seq", backward)
            offsets.append(step)
            blocks.append(behind)
    return offsets, blocks


def ring_reduce_scatter(by_offset, cycle):
    count = len(cycle)
    forward = [(cycle[p], cycle[(p + 1) % count]) for p in range(count)]
    backward = [(cycle[p], cycle[(p - 1) % count]) for p in range(count)]

    def block(offset):
        return by_offset[offset % count].astype(jnp.float32)

    total = block(0)
    for pairs, hops, sign in ((forward, count - 1 - count // 2, 1), (backward, count // 2, -1)):
        if hops == 0:
            continue
        acc = block(sign * hops)
        for step in range(1, hops + 1):
            received = lax.ppermute(acc.astype(jnp.bfloat16), "seq", pairs).astype(jnp.float32)
            if step < hops:
                acc = received + block(sign * (hops - step))
            else:
                total = total + received
    return total


def dispatch_experts(moe_in, expert_ids, route_weights, expert_gate_up, expert_down, experts_all, capacity):
    quarter = moe_in.shape[1]
    local_experts = expert_gate_up.shape[0]
    flat_ids = expert_ids.reshape(NEW * TOP)
    onehot = (flat_ids[:, None] == jnp.arange(experts_all, dtype=jnp.int32)[None, :]).astype(
        jnp.int32
    )
    ranks = jnp.sum((jnp.cumsum(onehot, axis=0) - onehot) * onehot, axis=1)
    target = (flat_ids * capacity + ranks).reshape(NEW, TOP)
    slot_ids = jnp.arange(experts_all * capacity, dtype=jnp.int32)
    selector = jnp.sum(
        (target[None, :, :] == slot_ids[:, None, None]).astype(jnp.int32), axis=2
    ).astype(jnp.bfloat16)
    send_rows = jnp.dot(selector, moe_in, preferred_element_type=jnp.float32).astype(jnp.bfloat16)
    send_rows = send_rows.reshape(experts_all, capacity, quarter)
    received = lax.all_to_all(send_rows, "seq", split_axis=0, concat_axis=1, tiled=True)
    hidden_quarter = expert_gate_up.shape[3]
    gate_up_local = expert_gate_up.reshape(local_experts, D, 2 * hidden_quarter)
    weight_rows = gate_up_local
    projected = jnp.einsum(
        "erd,edf->erf",
        lax.all_gather(received, "tp", axis=2, tiled=True),
        weight_rows,
        preferred_element_type=jnp.float32,
    )
    activated = (
        jax.nn.silu(projected[..., :hidden_quarter]) * projected[..., hidden_quarter:]
    ).astype(jnp.bfloat16)
    down_terms = jnp.einsum(
        "erf,efd->erd", activated, expert_down, preferred_element_type=jnp.float32
    )
    expert_result = lax.psum_scatter(
        down_terms.astype(jnp.bfloat16), "tp", scatter_dimension=2, tiled=True
    )
    returned = lax.all_to_all(
        expert_result, "seq", split_axis=1, concat_axis=0, tiled=True
    ).reshape(experts_all * capacity, quarter)
    picked = jnp.take(returned, target, axis=0)
    return jnp.sum(route_weights[:, :, None] * picked.astype(jnp.float32), axis=1)


def body(
    hidden,
    new_queries,
    new_keys,
    new_values,
    cache_keys,
    cache_values,
    cache_lengths,
    out_proj,
    moe_gain,
    expert_ids,
    route_weights,
    expert_gate_up,
    expert_down,
    next_gain,
    qkv_proj,
    query_gain,
    key_gain,
):
    seq_count = lax.axis_size("seq")
    here = lax.axis_index("seq")
    local_experts = expert_gate_up.shape[0]
    experts_all = local_experts * seq_count
    capacity = max(2, 3 * NEW * TOP // (2 * experts_all))
    dense = NEW <= 2 * capacity
    if dense:
        tp_here = lax.axis_index("tp")
        quarter_width = hidden.shape[1]
        tp_count = lax.axis_size("tp")
        pieces = [lax.dynamic_slice_in_dim(expert_down, tp_here * quarter_width, quarter_width, axis=2)]
        for shift in range(1, tp_count):
            target = (tp_here + shift) % tp_count
            piece = lax.dynamic_slice_in_dim(expert_down, target * quarter_width, quarter_width, axis=2)
            pairs = [(i, (i + shift) % tp_count) for i in range(tp_count)]
            pieces.append(lax.ppermute(piece, "tp", pairs))
        order = (tp_here - jnp.arange(tp_count, dtype=jnp.int32)) % tp_count
        down_full = jnp.take(jnp.stack(pieces), order, axis=0)
        gate_up_flat = expert_gate_up.reshape(local_experts, D, -1)
        qkv_flat = qkv_proj.reshape(D, -1)
    local_width = new_queries.shape[1]
    local_heads = local_width // HEAD_DIM
    quarter = hidden.shape[1]
    span = cache_keys.shape[1]
    my_length = lax.dynamic_index_in_dim(cache_lengths, here, 0, keepdims=False)
    attended = flash_attention(
        my_length,
        new_queries,
        cache_keys.reshape(span, local_width),
        cache_values.reshape(span, local_width),
        new_keys,
        new_values,
    )
    if dense:
        attended, down_full = lax.optimization_barrier((attended, down_full))
    else:
        gate_up_flat = expert_gate_up
        qkv_flat = qkv_proj.reshape(D, -1)
    attn_term = jnp.dot(attended, out_proj, preferred_element_type=jnp.float32)
    if dense:
        residual = hidden.astype(jnp.float32) + permute_reduce_scatter(attn_term, local_width)
    else:
        residual = hidden.astype(jnp.float32) + lax.psum_scatter(
            attn_term.astype(jnp.bfloat16), "tp", scatter_dimension=1, tiled=True
        ).astype(jnp.float32)
    square_total = lax.psum(jnp.sum(residual * residual, axis=1), "tp")
    moe_in = (residual * lax.rsqrt(square_total / D + epsilon)[:, None] * moe_gain[None, :]).astype(
        jnp.bfloat16
    )
    if dense:
        moe_term, qkv_flat = dense_experts(
            moe_in, expert_ids, route_weights, gate_up_flat, down_full, qkv_flat, here, experts_all
        )
    else:
        moe_term = dispatch_experts(
            moe_in, expert_ids, route_weights, expert_gate_up, expert_down, experts_all, capacity
        )
    routed = residual + moe_term
    layer_out = routed.astype(jnp.bfloat16)
    scaled = (routed * next_gain[None, :]).astype(jnp.bfloat16)
    weight_rows = qkv_flat
    if dense:
        mixed = permute_gather_dot(scaled, weight_rows)
    else:
        mixed = jnp.dot(
            lax.all_gather(scaled, "tp", axis=1, tiled=True),
            weight_rows,
            preferred_element_type=jnp.float32,
        )
    mixed = mixed.reshape(NEW, 3, local_width)
    squares_routed = jnp.sum(routed * routed, axis=1)
    routed_total, query_raw, key_raw = lax.psum(
        (
            squares_routed,
            jnp.sum(mixed[:, 0] * mixed[:, 0], axis=1),
            jnp.sum(mixed[:, 1] * mixed[:, 1], axis=1),
        ),
        "tp",
    )
    x_scale = lax.rsqrt(routed_total / D + epsilon)
    query_pre = mixed[:, 0] * x_scale[:, None]
    key_pre = mixed[:, 1] * x_scale[:, None]
    query_total = query_raw * x_scale * x_scale
    key_total = key_raw * x_scale * x_scale
    next_query = (
        query_pre * lax.rsqrt(query_total / D + epsilon)[:, None] * query_gain[None, :]
    ).astype(jnp.bfloat16)
    next_key = (key_pre * lax.rsqrt(key_total / D + epsilon)[:, None] * key_gain[None, :]).astype(
        jnp.bfloat16
    )
    next_value = (mixed[:, 2] * x_scale[:, None]).astype(jnp.bfloat16)
    return (layer_out, next_query, next_key, next_value)


def solution(mesh):
    return jax.shard_map(
        body,
        mesh=mesh,
        in_specs=(
            P("seq", "tp"),
            P("seq", "tp"),
            P("seq", "tp"),
            P("seq", "tp"),
            P("seq", None, "tp"),
            P("seq", None, "tp"),
            P(),
            P("tp", None),
            P("tp"),
            P("seq", None),
            P("seq", None),
            P("seq", None, None, "tp"),
            P("seq", "tp", None),
            P("tp"),
            P(None, None, "tp"),
            P("tp"),
            P("tp"),
        ),
        out_specs=(P("seq", "tp"), P("seq", "tp"), P("seq", "tp"), P("seq", "tp")),
        check_vma=False,
    )
```

```python
import functools
import math

import jax
import jax.numpy as jnp
from jax import lax
from jax.experimental import pallas as pl
from jax.experimental.pallas import tpu as pltpu
from jax.sharding import PartitionSpec as P

D = 2048
HEAD_DIM = 128
TOP = 8
NEW = 256


epsilon = 1e-05


def flash_kernel(len_ref, q_ref, k_ref, v_ref, nk_ref, nv_ref, o_ref, m_sc, l_sc, acc_sc, *, block, heads, steps):
    j = pl.program_id(0)
    length = len_ref[0]
    valid = (length + block - 1) // block
    tokens = q_ref.shape[0]
    scale = 1.0 / math.sqrt(HEAD_DIM)

    @pl.when(j == 0)
    def _():
        m_sc[...] = jnp.full(m_sc.shape, -1e30, jnp.float32)
        l_sc[...] = jnp.zeros(l_sc.shape, jnp.float32)
        acc_sc[...] = jnp.zeros(acc_sc.shape, jnp.float32)

    def update(keys_ref, values_ref, allowed):
        for h in range(heads):
            cols = slice(h * HEAD_DIM, (h + 1) * HEAD_DIM)
            q = q_ref[:, cols]
            k = keys_ref[:, cols]
            s = lax.dot_general(q, k, (((1,), (1,)), ((), ())), preferred_element_type=jnp.float32) * scale
            s = jnp.where(allowed, s, -1e30)
            m_old = m_sc[h]
            m_new = jnp.maximum(m_old, jnp.max(s, axis=1, keepdims=True))
            alpha = jnp.exp(m_old - m_new)
            p = jnp.where(allowed, jnp.exp(s - m_new), 0.0)
            l_sc[h] = alpha * l_sc[h] + jnp.sum(p, axis=1, keepdims=True)
            pv = jnp.dot(p.astype(jnp.bfloat16), values_ref[:, cols], preferred_element_type=jnp.float32)
            acc_sc[:, cols] = alpha * acc_sc[:, cols] + pv
            m_sc[h] = m_new

    @pl.when(j < valid)
    def _():
        pos = j * block + lax.broadcasted_iota(jnp.int32, (tokens, block), 1)
        update(k_ref, v_ref, pos < length)

    @pl.when(j == steps - 1)
    def _():
        row = lax.broadcasted_iota(jnp.int32, (tokens, tokens), 0)
        col = lax.broadcasted_iota(jnp.int32, (tokens, tokens), 1)
        update(nk_ref, nv_ref, col <= row)
        for h in range(heads):
            cols = slice(h * HEAD_DIM, (h + 1) * HEAD_DIM)
            o_ref[:, cols] = (acc_sc[:, cols] / l_sc[h]).astype(o_ref.dtype)


def flash_attention(length, queries, cache_k, cache_v, new_k, new_v, block=1024):
    tokens, width = queries.shape
    span = cache_k.shape[0]
    block = min(block, span)
    heads = width // HEAD_DIM
    steps = span // block + 1
    last = span // block - 1

    def cache_map(j, len_ref):
        valid = (len_ref[0] + block - 1) // block
        return (jnp.minimum(j, jnp.maximum(valid - 1, 0)), 0)

    grid_spec = pltpu.PrefetchScalarGridSpec(
        num_scalar_prefetch=1,
        grid=(steps,),
        in_specs=[
            pl.BlockSpec((tokens, width), lambda j, l: (0, 0)),
            pl.BlockSpec((block, width), cache_map),
            pl.BlockSpec((block, width), cache_map),
            pl.BlockSpec((tokens, width), lambda j, l: (0, 0)),
            pl.BlockSpec((tokens, width), lambda j, l: (0, 0)),
        ],
        out_specs=pl.BlockSpec((tokens, width), lambda j, l: (0, 0)),
        scratch_shapes=[
            pltpu.VMEM((heads, tokens, 1), jnp.float32),
            pltpu.VMEM((heads, tokens, 1), jnp.float32),
            pltpu.VMEM((tokens, width), jnp.float32),
        ],
    )
    kernel = functools.partial(flash_kernel, block=block, heads=heads, steps=steps)
    return pl.pallas_call(
        kernel,
        grid_spec=grid_spec,
        out_shape=jax.ShapeDtypeStruct((tokens, width), jnp.bfloat16),
        compiler_params=pltpu.CompilerParams(dimension_semantics=("arbitrary",)),
    )(length.reshape(1), queries, cache_k, cache_v, new_k, new_v)


def dense_experts(moe_in, expert_ids, route_weights, expert_gate_up, down_full, qkv_flat, here, experts_all):
    local_experts = expert_gate_up.shape[0]
    hidden_quarter = expert_gate_up.shape[2] // 2
    tokens, quarter = moe_in.shape
    seq_count = experts_all // local_experts
    gate_w = jnp.sum(
        route_weights[:, :, None]
        * (expert_ids[:, :, None] == jnp.arange(experts_all, dtype=jnp.int32)[None, None, :]),
        axis=1,
    )
    gate_t = jnp.transpose(gate_w)
    gate_hi = gate_t.astype(jnp.bfloat16)
    gate_lo = (gate_t - gate_hi.astype(jnp.float32)).astype(jnp.bfloat16)
    info = jnp.concatenate([gate_hi, gate_lo], axis=0).reshape(-1, quarter)
    packed = jnp.concatenate([moe_in, info], axis=0)
    ring = ring_order(seq_count)
    offsets, blocks = ring_all_gather(packed, ring)
    cuts = sorted({0, min(3, len(blocks)), min(6, len(blocks)), len(blocks)})
    chunks = list(zip(cuts[:-1], cuts[1:]))
    outputs = []
    for begin, end in chunks:
        gathered = jnp.stack(blocks[begin:end])
        count = end - begin
        rows_q = gathered[:, :tokens].reshape(count * tokens, quarter)
        info_all = gathered[:, tokens:].reshape(count, 2, experts_all, tokens).astype(jnp.float32)
        gate_all = info_all[:, 0] + info_all[:, 1]
        gate_local = lax.dynamic_slice_in_dim(gate_all, here * local_experts, local_experts, axis=1)
        gate_local = jnp.transpose(gate_local, (1, 0, 2)).reshape(local_experts, count * tokens)
        rows = lax.all_gather(rows_q, "tp", axis=0, tiled=False)
        if begin == 0:
            rows, expert_gate_up, qkv_flat = lax.optimization_barrier((rows, expert_gate_up, qkv_flat))
        gate_up_split = expert_gate_up.reshape(local_experts, rows.shape[0], quarter, -1)
        projected = jnp.einsum("qtd,eqdf->etf", rows, gate_up_split, preferred_element_type=jnp.float32)
        activated = jax.nn.silu(projected[..., :hidden_quarter]) * projected[..., hidden_quarter:]
        activated = activated.astype(jnp.bfloat16).astype(jnp.float32)
        weighted = (activated * gate_local[:, :, None]).astype(jnp.bfloat16)
        weighted = pair_gather(weighted)
        partial = jnp.einsum(
            "qetf,qefd->td", weighted, down_full, preferred_element_type=jnp.float32
        ).astype(jnp.bfloat16)
        outputs.append(partial.reshape(count, tokens, -1))
    by_offset = {}
    index = 0
    for part in outputs:
        for i in range(part.shape[0]):
            by_offset[offsets[index]] = part[i]
            index += 1
    return ring_reduce_scatter(by_offset, ring), qkv_flat


def permute_reduce_scatter(term, width):
    tp_count = lax.axis_size("tp")
    tp_here = lax.axis_index("tp")
    total = lax.dynamic_slice_in_dim(term, tp_here * width, width, axis=1)
    for shift in range(1, tp_count):
        target = (tp_here + shift) % tp_count
        piece = lax.dynamic_slice_in_dim(term, target * width, width, axis=1).astype(jnp.bfloat16)
        pairs = [(i, (i + shift) % tp_count) for i in range(tp_count)]
        total = total + lax.ppermute(piece, "tp", pairs).astype(jnp.float32)
    return total


def permute_gather_dot(rows, weight):
    tp_count = lax.axis_size("tp")
    tp_here = lax.axis_index("tp")
    width = rows.shape[1]
    total = jnp.dot(
        rows,
        lax.dynamic_slice_in_dim(weight, tp_here * width, width, axis=0),
        preferred_element_type=jnp.float32,
    )
    for shift in range(1, tp_count):
        source = (tp_here - shift) % tp_count
        pairs = [(i, (i + shift) % tp_count) for i in range(tp_count)]
        piece = lax.ppermute(rows, "tp", pairs)
        total = total + jnp.dot(
            piece,
            lax.dynamic_slice_in_dim(weight, source * width, width, axis=0),
            preferred_element_type=jnp.float32,
        )
    return total


def pair_gather(block):
    if lax.axis_size("tp") != 4:
        return lax.all_gather(block, "tp", axis=0, tiled=False)
    far = lax.ppermute(block, "tp", [(i, i ^ 2) for i in range(4)])
    near = lax.ppermute(jnp.stack([block, far]), "tp", [(i, i ^ 1) for i in range(4)])
    return jnp.stack([block, near[0], far, near[1]])


def ring_order(count):
    half = count // 2
    if count % 2 or count < 4:
        return list(range(count))
    return [2 * i for i in range(half)] + [2 * i + 1 for i in reversed(range(half))]


def ring_all_gather(block, cycle):
    count = len(cycle)
    forward = [(cycle[p], cycle[(p + 1) % count]) for p in range(count)]
    backward = [(cycle[p], cycle[(p - 1) % count]) for p in range(count)]
    offsets, blocks = [0], [block]
    ahead, behind = block, block
    for step in range(1, count // 2 + 1):
        ahead = lax.ppermute(ahead, "seq", forward)
        offsets.append((-step) % count)
        blocks.append(ahead)
        if step < count - count // 2:
            behind = lax.ppermute(behind, "seq", backward)
            offsets.append(step)
            blocks.append(behind)
    return offsets, blocks


def ring_reduce_scatter(by_offset, cycle):
    count = len(cycle)
    forward = [(cycle[p], cycle[(p + 1) % count]) for p in range(count)]
    backward = [(cycle[p], cycle[(p - 1) % count]) for p in range(count)]

    def block(offset):
        return by_offset[offset % count].astype(jnp.float32)

    total = block(0)
    for pairs, hops, sign in ((forward, count - 1 - count // 2, 1), (backward, count // 2, -1)):
        if hops == 0:
            continue
        acc = block(sign * hops)
        for step in range(1, hops + 1):
            received = lax.ppermute(acc.astype(jnp.bfloat16), "seq", pairs).astype(jnp.float32)
            if step < hops:
                acc = received + block(sign * (hops - step))
            else:
                total = total + received
    return total


def dispatch_experts(moe_in, expert_ids, route_weights, expert_gate_up, expert_down, experts_all, capacity):
    quarter = moe_in.shape[1]
    local_experts = expert_gate_up.shape[0]
    flat_ids = expert_ids.reshape(NEW * TOP)
    onehot = (flat_ids[:, None] == jnp.arange(experts_all, dtype=jnp.int32)[None, :]).astype(
        jnp.int32
    )
    ranks = jnp.sum((jnp.cumsum(onehot, axis=0) - onehot) * onehot, axis=1)
    target = (flat_ids * capacity + ranks).reshape(NEW, TOP)
    slot_ids = jnp.arange(experts_all * capacity, dtype=jnp.int32)
    selector = jnp.sum(
        (target[None, :, :] == slot_ids[:, None, None]).astype(jnp.int32), axis=2
    ).astype(jnp.bfloat16)
    send_rows = jnp.dot(selector, moe_in, preferred_element_type=jnp.float32).astype(jnp.bfloat16)
    send_rows = send_rows.reshape(experts_all, capacity, quarter)
    received = lax.all_to_all(send_rows, "seq", split_axis=0, concat_axis=1, tiled=True)
    hidden_quarter = expert_gate_up.shape[3]
    gate_up_local = expert_gate_up.reshape(local_experts, D, 2 * hidden_quarter)
    weight_rows = gate_up_local
    projected = jnp.einsum(
        "erd,edf->erf",
        lax.all_gather(received, "tp", axis=2, tiled=True),
        weight_rows,
        preferred_element_type=jnp.float32,
    )
    activated = (
        jax.nn.silu(projected[..., :hidden_quarter]) * projected[..., hidden_quarter:]
    ).astype(jnp.bfloat16)
    down_terms = jnp.einsum(
        "erf,efd->erd", activated, expert_down, preferred_element_type=jnp.float32
    )
    expert_result = lax.psum_scatter(
        down_terms.astype(jnp.bfloat16), "tp", scatter_dimension=2, tiled=True
    )
    returned = lax.all_to_all(
        expert_result, "seq", split_axis=1, concat_axis=0, tiled=True
    ).reshape(experts_all * capacity, quarter)
    picked = jnp.take(returned, target, axis=0)
    return jnp.sum(route_weights[:, :, None] * picked.astype(jnp.float32), axis=1)


def body(
    hidden,
    new_queries,
    new_keys,
    new_values,
    cache_keys,
    cache_values,
    cache_lengths,
    out_proj,
    moe_gain,
    expert_ids,
    route_weights,
    expert_gate_up,
    expert_down,
    next_gain,
    qkv_proj,
    query_gain,
    key_gain,
):
    seq_count = lax.axis_size("seq")
    here = lax.axis_index("seq")
    local_experts = expert_gate_up.shape[0]
    experts_all = local_experts * seq_count
    capacity = max(2, 3 * NEW * TOP // (2 * experts_all))
    dense = NEW <= 2 * capacity
    if dense:
        tp_here = lax.axis_index("tp")
        quarter_width = hidden.shape[1]
        tp_count = lax.axis_size("tp")
        pieces = [lax.dynamic_slice_in_dim(expert_down, tp_here * quarter_width, quarter_width, axis=2)]
        for shift in range(1, tp_count):
            target = (tp_here + shift) % tp_count
            piece = lax.dynamic_slice_in_dim(expert_down, target * quarter_width, quarter_width, axis=2)
            pairs = [(i, (i + shift) % tp_count) for i in range(tp_count)]
            pieces.append(lax.ppermute(piece, "tp", pairs))
        if tp_count == 4:
            order = (tp_here - (tp_here ^ jnp.arange(tp_count, dtype=jnp.int32))) % tp_count
        else:
            order = (tp_here - jnp.arange(tp_count, dtype=jnp.int32)) % tp_count
        down_full = jnp.take(jnp.stack(pieces), order, axis=0)
        gate_up_flat = expert_gate_up.reshape(local_experts, D, -1)
        qkv_flat = qkv_proj.reshape(D, -1)
    local_width = new_queries.shape[1]
    local_heads = local_width // HEAD_DIM
    quarter = hidden.shape[1]
    span = cache_keys.shape[1]
    my_length = lax.dynamic_index_in_dim(cache_lengths, here, 0, keepdims=False)
    attended = flash_attention(
        my_length,
        new_queries,
        cache_keys.reshape(span, local_width),
        cache_values.reshape(span, local_width),
        new_keys,
        new_values,
    )
    if dense:
        attended, down_full = lax.optimization_barrier((attended, down_full))
    else:
        gate_up_flat = expert_gate_up
        qkv_flat = qkv_proj.reshape(D, -1)
    attn_term = jnp.dot(attended, out_proj, preferred_element_type=jnp.float32)
    if dense:
        residual = hidden.astype(jnp.float32) + permute_reduce_scatter(attn_term, local_width)
    else:
        residual = hidden.astype(jnp.float32) + lax.psum_scatter(
            attn_term.astype(jnp.bfloat16), "tp", scatter_dimension=1, tiled=True
        ).astype(jnp.float32)
    square_total = lax.psum(jnp.sum(residual * residual, axis=1), "tp")
    moe_in = (residual * lax.rsqrt(square_total / D + epsilon)[:, None] * moe_gain[None, :]).astype(
        jnp.bfloat16
    )
    if dense:
        moe_term, qkv_flat = dense_experts(
            moe_in, expert_ids, route_weights, gate_up_flat, down_full, qkv_flat, here, experts_all
        )
    else:
        moe_term = dispatch_experts(
            moe_in, expert_ids, route_weights, expert_gate_up, expert_down, experts_all, capacity
        )
    routed = residual + moe_term
    layer_out = routed.astype(jnp.bfloat16)
    scaled = (routed * next_gain[None, :]).astype(jnp.bfloat16)
    weight_rows = qkv_flat
    if dense:
        mixed = permute_gather_dot(scaled, weight_rows)
    else:
        mixed = jnp.dot(
            lax.all_gather(scaled, "tp", axis=1, tiled=True),
            weight_rows,
            preferred_element_type=jnp.float32,
        )
    mixed = mixed.reshape(NEW, 3, local_width)
    squares_routed = jnp.sum(routed * routed, axis=1)
    routed_total, query_raw, key_raw = lax.psum(
        (
            squares_routed,
            jnp.sum(mixed[:, 0] * mixed[:, 0], axis=1),
            jnp.sum(mixed[:, 1] * mixed[:, 1], axis=1),
        ),
        "tp",
    )
    x_scale = lax.rsqrt(routed_total / D + epsilon)
    query_pre = mixed[:, 0] * x_scale[:, None]
    key_pre = mixed[:, 1] * x_scale[:, None]
    query_total = query_raw * x_scale * x_scale
    key_total = key_raw * x_scale * x_scale
    next_query = (
        query_pre * lax.rsqrt(query_total / D + epsilon)[:, None] * query_gain[None, :]
    ).astype(jnp.bfloat16)
    next_key = (key_pre * lax.rsqrt(key_total / D + epsilon)[:, None] * key_gain[None, :]).astype(
        jnp.bfloat16
    )
    next_value = (mixed[:, 2] * x_scale[:, None]).astype(jnp.bfloat16)
    return (layer_out, next_query, next_key, next_value)


def solution(mesh):
    return jax.shard_map(
        body,
        mesh=mesh,
        in_specs=(
            P("seq", "tp"),
            P("seq", "tp"),
            P("seq", "tp"),
            P("seq", "tp"),
            P("seq", None, "tp"),
            P("seq", None, "tp"),
            P(),
            P("tp", None),
            P("tp"),
            P("seq", None),
            P("seq", None),
            P("seq", None, None, "tp"),
            P("seq", "tp", None),
            P("tp"),
            P(None, None, "tp"),
            P("tp"),
            P("tp"),
        ),
        out_specs=(P("seq", "tp"), P("seq", "tp"), P("seq", "tp"), P("seq", "tp")),
        check_vma=False,
    )
```

```python
import functools
import math

import jax
import jax.numpy as jnp
from jax import lax
from jax.experimental import pallas as pl
from jax.experimental.pallas import tpu as pltpu
from jax.sharding import PartitionSpec as P

D = 2048
HEAD_DIM = 128
TOP = 8
NEW = 256


epsilon = 1e-05


def flash_kernel(len_ref, q_ref, k_ref, v_ref, nk_ref, nv_ref, o_ref, m_sc, l_sc, acc_sc, *, block, heads, steps):
    j = pl.program_id(0)
    length = len_ref[0]
    valid = (length + block - 1) // block
    tokens = q_ref.shape[0]
    scale = 1.0 / math.sqrt(HEAD_DIM)

    @pl.when(j == 0)
    def _():
        m_sc[...] = jnp.full(m_sc.shape, -1e30, jnp.float32)
        l_sc[...] = jnp.zeros(l_sc.shape, jnp.float32)
        acc_sc[...] = jnp.zeros(acc_sc.shape, jnp.float32)

    def update(keys_ref, values_ref, allowed):
        for h in range(heads):
            cols = slice(h * HEAD_DIM, (h + 1) * HEAD_DIM)
            q = q_ref[:, cols]
            k = keys_ref[:, cols]
            s = lax.dot_general(q, k, (((1,), (1,)), ((), ())), preferred_element_type=jnp.float32) * scale
            s = jnp.where(allowed, s, -1e30)
            m_old = m_sc[h]
            m_new = jnp.maximum(m_old, jnp.max(s, axis=1, keepdims=True))
            alpha = jnp.exp(m_old - m_new)
            p = jnp.where(allowed, jnp.exp(s - m_new), 0.0)
            l_sc[h] = alpha * l_sc[h] + jnp.sum(p, axis=1, keepdims=True)
            pv = jnp.dot(p.astype(jnp.bfloat16), values_ref[:, cols], preferred_element_type=jnp.float32)
            acc_sc[:, cols] = alpha * acc_sc[:, cols] + pv
            m_sc[h] = m_new

    @pl.when(j < valid)
    def _():
        pos = j * block + lax.broadcasted_iota(jnp.int32, (tokens, block), 1)
        update(k_ref, v_ref, pos < length)

    @pl.when(j == steps - 1)
    def _():
        row = lax.broadcasted_iota(jnp.int32, (tokens, tokens), 0)
        col = lax.broadcasted_iota(jnp.int32, (tokens, tokens), 1)
        update(nk_ref, nv_ref, col <= row)
        for h in range(heads):
            cols = slice(h * HEAD_DIM, (h + 1) * HEAD_DIM)
            o_ref[:, cols] = (acc_sc[:, cols] / l_sc[h]).astype(o_ref.dtype)


def flash_attention(length, queries, cache_k, cache_v, new_k, new_v, block=1024):
    tokens, width = queries.shape
    span = cache_k.shape[0]
    block = min(block, span)
    heads = width // HEAD_DIM
    steps = span // block + 1
    last = span // block - 1

    def cache_map(j, len_ref):
        valid = (len_ref[0] + block - 1) // block
        return (jnp.minimum(j, jnp.maximum(valid - 1, 0)), 0)

    grid_spec = pltpu.PrefetchScalarGridSpec(
        num_scalar_prefetch=1,
        grid=(steps,),
        in_specs=[
            pl.BlockSpec((tokens, width), lambda j, l: (0, 0)),
            pl.BlockSpec((block, width), cache_map),
            pl.BlockSpec((block, width), cache_map),
            pl.BlockSpec((tokens, width), lambda j, l: (0, 0)),
            pl.BlockSpec((tokens, width), lambda j, l: (0, 0)),
        ],
        out_specs=pl.BlockSpec((tokens, width), lambda j, l: (0, 0)),
        scratch_shapes=[
            pltpu.VMEM((heads, tokens, 1), jnp.float32),
            pltpu.VMEM((heads, tokens, 1), jnp.float32),
            pltpu.VMEM((tokens, width), jnp.float32),
        ],
    )
    kernel = functools.partial(flash_kernel, block=block, heads=heads, steps=steps)
    return pl.pallas_call(
        kernel,
        grid_spec=grid_spec,
        out_shape=jax.ShapeDtypeStruct((tokens, width), jnp.bfloat16),
        compiler_params=pltpu.CompilerParams(dimension_semantics=("arbitrary",)),
    )(length.reshape(1), queries, cache_k, cache_v, new_k, new_v)


def dense_experts(moe_in, expert_ids, route_weights, expert_gate_up, down_full, qkv_flat, here, experts_all):
    local_experts = expert_gate_up.shape[0]
    hidden_quarter = expert_gate_up.shape[-1] // 2
    tokens, quarter = moe_in.shape
    seq_count = experts_all // local_experts
    gate_w = jnp.sum(
        route_weights[:, :, None]
        * (expert_ids[:, :, None] == jnp.arange(experts_all, dtype=jnp.int32)[None, None, :]),
        axis=1,
    )
    gate_t = jnp.transpose(gate_w)
    gate_hi = gate_t.astype(jnp.bfloat16)
    gate_lo = (gate_t - gate_hi.astype(jnp.float32)).astype(jnp.bfloat16)
    info = jnp.concatenate([gate_hi, gate_lo], axis=0).reshape(-1, quarter)
    packed = jnp.concatenate([moe_in, info], axis=0)
    ring = ring_order(seq_count)
    offsets, blocks = ring_all_gather(packed, ring)
    cuts = sorted({0, min(3, len(blocks)), min(6, len(blocks)), len(blocks)})
    chunks = list(zip(cuts[:-1], cuts[1:]))
    outputs = []
    for begin, end in chunks:
        gathered = jnp.stack(blocks[begin:end])
        count = end - begin
        rows_q = gathered[:, :tokens].reshape(count * tokens, quarter)
        info_all = gathered[:, tokens:].reshape(count, 2, experts_all, tokens).astype(jnp.float32)
        gate_all = info_all[:, 0] + info_all[:, 1]
        gate_local = lax.dynamic_slice_in_dim(gate_all, here * local_experts, local_experts, axis=1)
        gate_local = jnp.transpose(gate_local, (1, 0, 2)).reshape(local_experts, count * tokens)
        rows = pair_gather(rows_q)
        if begin == 0:
            rows, expert_gate_up, qkv_flat = lax.optimization_barrier((rows, expert_gate_up, qkv_flat))
        gate_up_split = expert_gate_up.reshape(local_experts, rows.shape[0], quarter, -1)
        projected = jnp.einsum("qtd,eqdf->etf", rows, gate_up_split, preferred_element_type=jnp.float32)
        activated = jax.nn.silu(projected[..., :hidden_quarter]) * projected[..., hidden_quarter:]
        activated = activated.astype(jnp.bfloat16).astype(jnp.float32)
        weighted = (activated * gate_local[:, :, None]).astype(jnp.bfloat16)
        weighted = pair_gather(weighted)
        partial = jnp.einsum(
            "qetf,qefd->td", weighted, down_full, preferred_element_type=jnp.float32
        ).astype(jnp.bfloat16)
        outputs.append(partial.reshape(count, tokens, -1))
    by_offset = {}
    index = 0
    for part in outputs:
        for i in range(part.shape[0]):
            by_offset[offsets[index]] = part[i]
            index += 1
    return ring_reduce_scatter(by_offset, ring), qkv_flat


def permute_reduce_scatter(term, width):
    tp_count = lax.axis_size("tp")
    tp_here = lax.axis_index("tp")
    total = lax.dynamic_slice_in_dim(term, tp_here * width, width, axis=1)
    for shift in range(1, tp_count):
        target = (tp_here + shift) % tp_count
        piece = lax.dynamic_slice_in_dim(term, target * width, width, axis=1).astype(jnp.bfloat16)
        pairs = [(i, (i + shift) % tp_count) for i in range(tp_count)]
        total = total + lax.ppermute(piece, "tp", pairs).astype(jnp.float32)
    return total


def permute_gather_dot(rows, weight):
    tp_count = lax.axis_size("tp")
    tp_here = lax.axis_index("tp")
    width = rows.shape[1]
    total = jnp.dot(
        rows,
        lax.dynamic_slice_in_dim(weight, tp_here * width, width, axis=0),
        preferred_element_type=jnp.float32,
    )
    for shift in range(1, tp_count):
        source = (tp_here - shift) % tp_count
        pairs = [(i, (i + shift) % tp_count) for i in range(tp_count)]
        piece = lax.ppermute(rows, "tp", pairs)
        total = total + jnp.dot(
            piece,
            lax.dynamic_slice_in_dim(weight, source * width, width, axis=0),
            preferred_element_type=jnp.float32,
        )
    return total


def pair_gather(block):
    if lax.axis_size("tp") != 4:
        return lax.all_gather(block, "tp", axis=0, tiled=False)
    far = lax.ppermute(block, "tp", [(i, i ^ 2) for i in range(4)])
    near = lax.ppermute(jnp.stack([block, far]), "tp", [(i, i ^ 1) for i in range(4)])
    return jnp.stack([block, near[0], far, near[1]])


def ring_order(count):
    half = count // 2
    if count % 2 or count < 4:
        return list(range(count))
    return [2 * i for i in range(half)] + [2 * i + 1 for i in reversed(range(half))]


def ring_all_gather(block, cycle):
    count = len(cycle)
    forward = [(cycle[p], cycle[(p + 1) % count]) for p in range(count)]
    backward = [(cycle[p], cycle[(p - 1) % count]) for p in range(count)]
    offsets, blocks = [0], [block]
    ahead, behind = block, block
    for step in range(1, count // 2 + 1):
        ahead = lax.ppermute(ahead, "seq", forward)
        offsets.append((-step) % count)
        blocks.append(ahead)
        if step < count - count // 2:
            behind = lax.ppermute(behind, "seq", backward)
            offsets.append(step)
            blocks.append(behind)
    return offsets, blocks


def ring_reduce_scatter(by_offset, cycle):
    count = len(cycle)
    forward = [(cycle[p], cycle[(p + 1) % count]) for p in range(count)]
    backward = [(cycle[p], cycle[(p - 1) % count]) for p in range(count)]

    def block(offset):
        return by_offset[offset % count].astype(jnp.float32)

    total = block(0)
    for pairs, hops, sign in ((forward, count - 1 - count // 2, 1), (backward, count // 2, -1)):
        if hops == 0:
            continue
        acc = block(sign * hops)
        for step in range(1, hops + 1):
            received = lax.ppermute(acc.astype(jnp.bfloat16), "seq", pairs).astype(jnp.float32)
            if step < hops:
                acc = received + block(sign * (hops - step))
            else:
                total = total + received
    return total


def dispatch_experts(moe_in, expert_ids, route_weights, expert_gate_up, expert_down, experts_all, capacity):
    quarter = moe_in.shape[1]
    local_experts = expert_gate_up.shape[0]
    flat_ids = expert_ids.reshape(NEW * TOP)
    onehot = (flat_ids[:, None] == jnp.arange(experts_all, dtype=jnp.int32)[None, :]).astype(
        jnp.int32
    )
    ranks = jnp.sum((jnp.cumsum(onehot, axis=0) - onehot) * onehot, axis=1)
    target = (flat_ids * capacity + ranks).reshape(NEW, TOP)
    slot_ids = jnp.arange(experts_all * capacity, dtype=jnp.int32)
    selector = jnp.sum(
        (target[None, :, :] == slot_ids[:, None, None]).astype(jnp.int32), axis=2
    ).astype(jnp.bfloat16)
    send_rows = jnp.dot(selector, moe_in, preferred_element_type=jnp.float32).astype(jnp.bfloat16)
    send_rows = send_rows.reshape(experts_all, capacity, quarter)
    received = lax.all_to_all(send_rows, "seq", split_axis=0, concat_axis=1, tiled=True)
    hidden_quarter = expert_gate_up.shape[3]
    gate_up_local = expert_gate_up.reshape(local_experts, D, 2 * hidden_quarter)
    weight_rows = gate_up_local
    projected = jnp.einsum(
        "erd,edf->erf",
        lax.all_gather(received, "tp", axis=2, tiled=True),
        weight_rows,
        preferred_element_type=jnp.float32,
    )
    activated = (
        jax.nn.silu(projected[..., :hidden_quarter]) * projected[..., hidden_quarter:]
    ).astype(jnp.bfloat16)
    down_terms = jnp.einsum(
        "erf,efd->erd", activated, expert_down, preferred_element_type=jnp.float32
    )
    expert_result = lax.psum_scatter(
        down_terms.astype(jnp.bfloat16), "tp", scatter_dimension=2, tiled=True
    )
    returned = lax.all_to_all(
        expert_result, "seq", split_axis=1, concat_axis=0, tiled=True
    ).reshape(experts_all * capacity, quarter)
    picked = jnp.take(returned, target, axis=0)
    return jnp.sum(route_weights[:, :, None] * picked.astype(jnp.float32), axis=1)


def body(
    hidden,
    new_queries,
    new_keys,
    new_values,
    cache_keys,
    cache_values,
    cache_lengths,
    out_proj,
    moe_gain,
    expert_ids,
    route_weights,
    expert_gate_up,
    expert_down,
    next_gain,
    qkv_proj,
    query_gain,
    key_gain,
):
    seq_count = lax.axis_size("seq")
    here = lax.axis_index("seq")
    local_experts = expert_gate_up.shape[0]
    experts_all = local_experts * seq_count
    capacity = max(2, 3 * NEW * TOP // (2 * experts_all))
    dense = NEW <= 2 * capacity
    if dense:
        tp_here = lax.axis_index("tp")
        quarter_width = hidden.shape[1]
        tp_count = lax.axis_size("tp")
        pieces = [lax.dynamic_slice_in_dim(expert_down, tp_here * quarter_width, quarter_width, axis=2)]
        for shift in range(1, tp_count):
            target = (tp_here + shift) % tp_count
            piece = lax.dynamic_slice_in_dim(expert_down, target * quarter_width, quarter_width, axis=2)
            pairs = [(i, (i + shift) % tp_count) for i in range(tp_count)]
            pieces.append(lax.ppermute(piece, "tp", pairs))
        if tp_count == 4:
            order = (tp_here - (tp_here ^ jnp.arange(tp_count, dtype=jnp.int32))) % tp_count
        else:
            order = (tp_here - jnp.arange(tp_count, dtype=jnp.int32)) % tp_count
        down_full = jnp.take(jnp.stack(pieces), order, axis=0)
        gate_up_flat = expert_gate_up.reshape(local_experts, tp_count, quarter_width, -1)
        if tp_count == 4:
            source_order = tp_here ^ jnp.arange(tp_count, dtype=jnp.int32)
            gate_up_flat = jnp.take(gate_up_flat, source_order, axis=1)
        qkv_flat = qkv_proj.reshape(D, -1)
    local_width = new_queries.shape[1]
    local_heads = local_width // HEAD_DIM
    quarter = hidden.shape[1]
    span = cache_keys.shape[1]
    my_length = lax.dynamic_index_in_dim(cache_lengths, here, 0, keepdims=False)
    attended = flash_attention(
        my_length,
        new_queries,
        cache_keys.reshape(span, local_width),
        cache_values.reshape(span, local_width),
        new_keys,
        new_values,
    )
    if dense:
        attended, down_full = lax.optimization_barrier((attended, down_full))
    else:
        gate_up_flat = expert_gate_up
        qkv_flat = qkv_proj.reshape(D, -1)
    attn_term = jnp.dot(attended, out_proj, preferred_element_type=jnp.float32)
    if dense:
        residual = hidden.astype(jnp.float32) + permute_reduce_scatter(attn_term, local_width)
    else:
        residual = hidden.astype(jnp.float32) + lax.psum_scatter(
            attn_term.astype(jnp.bfloat16), "tp", scatter_dimension=1, tiled=True
        ).astype(jnp.float32)
    square_total = lax.psum(jnp.sum(residual * residual, axis=1), "tp")
    moe_in = (residual * lax.rsqrt(square_total / D + epsilon)[:, None] * moe_gain[None, :]).astype(
        jnp.bfloat16
    )
    if dense:
        moe_term, qkv_flat = dense_experts(
            moe_in, expert_ids, route_weights, gate_up_flat, down_full, qkv_flat, here, experts_all
        )
    else:
        moe_term = dispatch_experts(
            moe_in, expert_ids, route_weights, expert_gate_up, expert_down, experts_all, capacity
        )
    routed = residual + moe_term
    layer_out = routed.astype(jnp.bfloat16)
    scaled = (routed * next_gain[None, :]).astype(jnp.bfloat16)
    weight_rows = qkv_flat
    if dense:
        mixed = permute_gather_dot(scaled, weight_rows)
    else:
        mixed = jnp.dot(
            lax.all_gather(scaled, "tp", axis=1, tiled=True),
            weight_rows,
            preferred_element_type=jnp.float32,
        )
    mixed = mixed.reshape(NEW, 3, local_width)
    squares_routed = jnp.sum(routed * routed, axis=1)
    routed_total, query_raw, key_raw = lax.psum(
        (
            squares_routed,
            jnp.sum(mixed[:, 0] * mixed[:, 0], axis=1),
            jnp.sum(mixed[:, 1] * mixed[:, 1], axis=1),
        ),
        "tp",
    )
    x_scale = lax.rsqrt(routed_total / D + epsilon)
    query_pre = mixed[:, 0] * x_scale[:, None]
    key_pre = mixed[:, 1] * x_scale[:, None]
    query_total = query_raw * x_scale * x_scale
    key_total = key_raw * x_scale * x_scale
    next_query = (
        query_pre * lax.rsqrt(query_total / D + epsilon)[:, None] * query_gain[None, :]
    ).astype(jnp.bfloat16)
    next_key = (key_pre * lax.rsqrt(key_total / D + epsilon)[:, None] * key_gain[None, :]).astype(
        jnp.bfloat16
    )
    next_value = (mixed[:, 2] * x_scale[:, None]).astype(jnp.bfloat16)
    return (layer_out, next_query, next_key, next_value)


def solution(mesh):
    return jax.shard_map(
        body,
        mesh=mesh,
        in_specs=(
            P("seq", "tp"),
            P("seq", "tp"),
            P("seq", "tp"),
            P("seq", "tp"),
            P("seq", None, "tp"),
            P("seq", None, "tp"),
            P(),
            P("tp", None),
            P("tp"),
            P("seq", None),
            P("seq", None),
            P("seq", None, None, "tp"),
            P("seq", "tp", None),
            P("tp"),
            P(None, None, "tp"),
            P("tp"),
            P("tp"),
        ),
        out_specs=(P("seq", "tp"), P("seq", "tp"), P("seq", "tp"), P("seq", "tp")),
        check_vma=False,
    )
```

```python
import functools
import math

import jax
import jax.numpy as jnp
from jax import lax
from jax.experimental import pallas as pl
from jax.experimental.pallas import tpu as pltpu
from jax.sharding import PartitionSpec as P

D = 2048
HEAD_DIM = 128
TOP = 8
NEW = 256


epsilon = 1e-05


def flash_kernel(len_ref, q_ref, k_ref, v_ref, nk_ref, nv_ref, o_ref, m_sc, l_sc, acc_sc, *, block, heads, steps):
    j = pl.program_id(0)
    length = len_ref[0]
    valid = (length + block - 1) // block
    tokens = q_ref.shape[0]
    scale = 1.0 / math.sqrt(HEAD_DIM)

    @pl.when(j == 0)
    def _():
        m_sc[...] = jnp.full(m_sc.shape, -1e30, jnp.float32)
        l_sc[...] = jnp.zeros(l_sc.shape, jnp.float32)
        acc_sc[...] = jnp.zeros(acc_sc.shape, jnp.float32)

    def update(keys_ref, values_ref, allowed):
        for h in range(heads):
            cols = slice(h * HEAD_DIM, (h + 1) * HEAD_DIM)
            q = q_ref[:, cols]
            k = keys_ref[:, cols]
            s = lax.dot_general(q, k, (((1,), (1,)), ((), ())), preferred_element_type=jnp.float32) * scale
            s = jnp.where(allowed, s, -1e30)
            m_old = m_sc[h]
            m_new = jnp.maximum(m_old, jnp.max(s, axis=1, keepdims=True))
            alpha = jnp.exp(m_old - m_new)
            p = jnp.where(allowed, jnp.exp(s - m_new), 0.0)
            l_sc[h] = alpha * l_sc[h] + jnp.sum(p, axis=1, keepdims=True)
            pv = jnp.dot(p.astype(jnp.bfloat16), values_ref[:, cols], preferred_element_type=jnp.float32)
            acc_sc[:, cols] = alpha * acc_sc[:, cols] + pv
            m_sc[h] = m_new

    @pl.when(j < valid)
    def _():
        pos = j * block + lax.broadcasted_iota(jnp.int32, (tokens, block), 1)
        update(k_ref, v_ref, pos < length)

    @pl.when(j == steps - 1)
    def _():
        row = lax.broadcasted_iota(jnp.int32, (tokens, tokens), 0)
        col = lax.broadcasted_iota(jnp.int32, (tokens, tokens), 1)
        update(nk_ref, nv_ref, col <= row)
        for h in range(heads):
            cols = slice(h * HEAD_DIM, (h + 1) * HEAD_DIM)
            o_ref[:, cols] = (acc_sc[:, cols] / l_sc[h]).astype(o_ref.dtype)


def flash_attention(length, queries, cache_k, cache_v, new_k, new_v, block=1024):
    tokens, width = queries.shape
    span = cache_k.shape[0]
    block = min(block, span)
    heads = width // HEAD_DIM
    steps = span // block + 1
    last = span // block - 1

    def cache_map(j, len_ref):
        valid = (len_ref[0] + block - 1) // block
        return (jnp.minimum(j, jnp.maximum(valid - 1, 0)), 0)

    grid_spec = pltpu.PrefetchScalarGridSpec(
        num_scalar_prefetch=1,
        grid=(steps,),
        in_specs=[
            pl.BlockSpec((tokens, width), lambda j, l: (0, 0)),
            pl.BlockSpec((block, width), cache_map),
            pl.BlockSpec((block, width), cache_map),
            pl.BlockSpec((tokens, width), lambda j, l: (0, 0)),
            pl.BlockSpec((tokens, width), lambda j, l: (0, 0)),
        ],
        out_specs=pl.BlockSpec((tokens, width), lambda j, l: (0, 0)),
        scratch_shapes=[
            pltpu.VMEM((heads, tokens, 1), jnp.float32),
            pltpu.VMEM((heads, tokens, 1), jnp.float32),
            pltpu.VMEM((tokens, width), jnp.float32),
        ],
    )
    kernel = functools.partial(flash_kernel, block=block, heads=heads, steps=steps)
    return pl.pallas_call(
        kernel,
        grid_spec=grid_spec,
        out_shape=jax.ShapeDtypeStruct((tokens, width), jnp.bfloat16),
        compiler_params=pltpu.CompilerParams(dimension_semantics=("arbitrary",)),
    )(length.reshape(1), queries, cache_k, cache_v, new_k, new_v)


def dense_experts(moe_in, expert_ids, route_weights, expert_gate_up, down_full, qkv_flat, here, experts_all):
    local_experts = expert_gate_up.shape[0]
    hidden_quarter = expert_gate_up.shape[-1] // 2
    tokens, quarter = moe_in.shape
    seq_count = experts_all // local_experts
    gate_w = jnp.sum(
        route_weights[:, :, None]
        * (expert_ids[:, :, None] == jnp.arange(experts_all, dtype=jnp.int32)[None, None, :]),
        axis=1,
    )
    gate_t = jnp.transpose(gate_w)
    gate_hi = gate_t.astype(jnp.bfloat16)
    gate_lo = (gate_t - gate_hi.astype(jnp.float32)).astype(jnp.bfloat16)
    info = jnp.concatenate([gate_hi, gate_lo], axis=0).reshape(-1, quarter)
    packed = jnp.concatenate([moe_in, info], axis=0)
    ring = ring_order(seq_count)
    offsets, blocks = ring_all_gather(packed, ring)
    cuts = sorted({0, min(3, len(blocks)), min(6, len(blocks)), len(blocks)})
    chunks = list(zip(cuts[:-1], cuts[1:]))
    outputs = []
    for begin, end in chunks:
        gathered = jnp.stack(blocks[begin:end])
        count = end - begin
        rows_q = gathered[:, :tokens].reshape(count * tokens, quarter)
        info_all = gathered[:, tokens:].reshape(count, 2, experts_all, tokens).astype(jnp.float32)
        gate_all = info_all[:, 0] + info_all[:, 1]
        gate_local = lax.dynamic_slice_in_dim(gate_all, here * local_experts, local_experts, axis=1)
        gate_local = jnp.transpose(gate_local, (1, 0, 2)).reshape(local_experts, count * tokens)
        rows = pair_gather(rows_q)
        if lax.axis_size("tp") == 4:
            rows = jnp.take(rows, lax.axis_index("tp") ^ jnp.arange(4, dtype=jnp.int32), axis=0)
        if begin == 0:
            rows, expert_gate_up = lax.optimization_barrier((rows, expert_gate_up))
        if end == len(blocks):
            rows, qkv_flat = lax.optimization_barrier((rows, qkv_flat))
        gate_up_split = expert_gate_up.reshape(local_experts, rows.shape[0], quarter, -1)
        projected = jnp.einsum("qtd,eqdf->etf", rows, gate_up_split, preferred_element_type=jnp.float32)
        activated = jax.nn.silu(projected[..., :hidden_quarter]) * projected[..., hidden_quarter:]
        activated = activated.astype(jnp.bfloat16).astype(jnp.float32)
        weighted = (activated * gate_local[:, :, None]).astype(jnp.bfloat16)
        weighted = pair_gather(weighted)
        partial = jnp.einsum(
            "qetf,qefd->td", weighted, down_full, preferred_element_type=jnp.float32
        ).astype(jnp.bfloat16)
        outputs.append(partial.reshape(count, tokens, -1))
    by_offset = {}
    index = 0
    for part in outputs:
        for i in range(part.shape[0]):
            by_offset[offsets[index]] = part[i]
            index += 1
    return ring_reduce_scatter(by_offset, ring), qkv_flat


def permute_reduce_scatter(term, width):
    tp_count = lax.axis_size("tp")
    tp_here = lax.axis_index("tp")
    total = lax.dynamic_slice_in_dim(term, tp_here * width, width, axis=1)
    for shift in range(1, tp_count):
        target = (tp_here + shift) % tp_count
        piece = lax.dynamic_slice_in_dim(term, target * width, width, axis=1).astype(jnp.bfloat16)
        pairs = [(i, (i + shift) % tp_count) for i in range(tp_count)]
        total = total + lax.ppermute(piece, "tp", pairs).astype(jnp.float32)
    return total


def permute_gather_dot(rows, weight):
    tp_count = lax.axis_size("tp")
    tp_here = lax.axis_index("tp")
    width = rows.shape[1]
    total = jnp.dot(
        rows,
        lax.dynamic_slice_in_dim(weight, tp_here * width, width, axis=0),
        preferred_element_type=jnp.float32,
    )
    for shift in range(1, tp_count):
        source = (tp_here - shift) % tp_count
        pairs = [(i, (i + shift) % tp_count) for i in range(tp_count)]
        piece = lax.ppermute(rows, "tp", pairs)
        total = total + jnp.dot(
            piece,
            lax.dynamic_slice_in_dim(weight, source * width, width, axis=0),
            preferred_element_type=jnp.float32,
        )
    return total


def pair_gather(block):
    if lax.axis_size("tp") != 4:
        return lax.all_gather(block, "tp", axis=0, tiled=False)
    far = lax.ppermute(block, "tp", [(i, i ^ 2) for i in range(4)])
    near = lax.ppermute(jnp.stack([block, far]), "tp", [(i, i ^ 1) for i in range(4)])
    return jnp.stack([block, near[0], far, near[1]])


def ring_order(count):
    half = count // 2
    if count % 2 or count < 4:
        return list(range(count))
    return [2 * i for i in range(half)] + [2 * i + 1 for i in reversed(range(half))]


def ring_all_gather(block, cycle):
    count = len(cycle)
    forward = [(cycle[p], cycle[(p + 1) % count]) for p in range(count)]
    backward = [(cycle[p], cycle[(p - 1) % count]) for p in range(count)]
    offsets, blocks = [0], [block]
    ahead, behind = block, block
    for step in range(1, count // 2 + 1):
        ahead = lax.ppermute(ahead, "seq", forward)
        offsets.append((-step) % count)
        blocks.append(ahead)
        if step < count - count // 2:
            behind = lax.ppermute(behind, "seq", backward)
            offsets.append(step)
            blocks.append(behind)
    return offsets, blocks


def ring_reduce_scatter(by_offset, cycle):
    count = len(cycle)
    forward = [(cycle[p], cycle[(p + 1) % count]) for p in range(count)]
    backward = [(cycle[p], cycle[(p - 1) % count]) for p in range(count)]

    def block(offset):
        return by_offset[offset % count].astype(jnp.float32)

    total = block(0)
    for pairs, hops, sign in ((forward, count - 1 - count // 2, 1), (backward, count // 2, -1)):
        if hops == 0:
            continue
        acc = block(sign * hops)
        for step in range(1, hops + 1):
            received = lax.ppermute(acc.astype(jnp.bfloat16), "seq", pairs).astype(jnp.float32)
            if step < hops:
                acc = received + block(sign * (hops - step))
            else:
                total = total + received
    return total


def dispatch_experts(moe_in, expert_ids, route_weights, expert_gate_up, expert_down, experts_all, capacity):
    quarter = moe_in.shape[1]
    local_experts = expert_gate_up.shape[0]
    flat_ids = expert_ids.reshape(NEW * TOP)
    onehot = (flat_ids[:, None] == jnp.arange(experts_all, dtype=jnp.int32)[None, :]).astype(
        jnp.int32
    )
    ranks = jnp.sum((jnp.cumsum(onehot, axis=0) - onehot) * onehot, axis=1)
    target = (flat_ids * capacity + ranks).reshape(NEW, TOP)
    slot_ids = jnp.arange(experts_all * capacity, dtype=jnp.int32)
    selector = jnp.sum(
        (target[None, :, :] == slot_ids[:, None, None]).astype(jnp.int32), axis=2
    ).astype(jnp.bfloat16)
    send_rows = jnp.dot(selector, moe_in, preferred_element_type=jnp.float32).astype(jnp.bfloat16)
    send_rows = send_rows.reshape(experts_all, capacity, quarter)
    received = lax.all_to_all(send_rows, "seq", split_axis=0, concat_axis=1, tiled=True)
    hidden_quarter = expert_gate_up.shape[3]
    gate_up_local = expert_gate_up.reshape(local_experts, D, 2 * hidden_quarter)
    weight_rows = gate_up_local
    projected = jnp.einsum(
        "erd,edf->erf",
        lax.all_gather(received, "tp", axis=2, tiled=True),
        weight_rows,
        preferred_element_type=jnp.float32,
    )
    activated = (
        jax.nn.silu(projected[..., :hidden_quarter]) * projected[..., hidden_quarter:]
    ).astype(jnp.bfloat16)
    down_terms = jnp.einsum(
        "erf,efd->erd", activated, expert_down, preferred_element_type=jnp.float32
    )
    expert_result = lax.psum_scatter(
        down_terms.astype(jnp.bfloat16), "tp", scatter_dimension=2, tiled=True
    )
    returned = lax.all_to_all(
        expert_result, "seq", split_axis=1, concat_axis=0, tiled=True
    ).reshape(experts_all * capacity, quarter)
    picked = jnp.take(returned, target, axis=0)
    return jnp.sum(route_weights[:, :, None] * picked.astype(jnp.float32), axis=1)


def body(
    hidden,
    new_queries,
    new_keys,
    new_values,
    cache_keys,
    cache_values,
    cache_lengths,
    out_proj,
    moe_gain,
    expert_ids,
    route_weights,
    expert_gate_up,
    expert_down,
    next_gain,
    qkv_proj,
    query_gain,
    key_gain,
):
    seq_count = lax.axis_size("seq")
    here = lax.axis_index("seq")
    local_experts = expert_gate_up.shape[0]
    experts_all = local_experts * seq_count
    capacity = max(2, 3 * NEW * TOP // (2 * experts_all))
    dense = NEW <= 2 * capacity
    if dense:
        tp_here = lax.axis_index("tp")
        quarter_width = hidden.shape[1]
        tp_count = lax.axis_size("tp")
        pieces = [lax.dynamic_slice_in_dim(expert_down, tp_here * quarter_width, quarter_width, axis=2)]
        for shift in range(1, tp_count):
            target = (tp_here + shift) % tp_count
            piece = lax.dynamic_slice_in_dim(expert_down, target * quarter_width, quarter_width, axis=2)
            pairs = [(i, (i + shift) % tp_count) for i in range(tp_count)]
            pieces.append(lax.ppermute(piece, "tp", pairs))
        if tp_count == 4:
            order = (tp_here - (tp_here ^ jnp.arange(tp_count, dtype=jnp.int32))) % tp_count
        else:
            order = (tp_here - jnp.arange(tp_count, dtype=jnp.int32)) % tp_count
        down_full = jnp.take(jnp.stack(pieces), order, axis=0)
        gate_up_flat = expert_gate_up.reshape(local_experts, tp_count, quarter_width, -1)
        qkv_flat = qkv_proj.reshape(D, -1)
    local_width = new_queries.shape[1]
    local_heads = local_width // HEAD_DIM
    quarter = hidden.shape[1]
    span = cache_keys.shape[1]
    my_length = lax.dynamic_index_in_dim(cache_lengths, here, 0, keepdims=False)
    attended = flash_attention(
        my_length,
        new_queries,
        cache_keys.reshape(span, local_width),
        cache_values.reshape(span, local_width),
        new_keys,
        new_values,
    )
    if dense:
        attended, down_full = lax.optimization_barrier((attended, down_full))
    else:
        gate_up_flat = expert_gate_up
        qkv_flat = qkv_proj.reshape(D, -1)
    attn_term = jnp.dot(attended, out_proj, preferred_element_type=jnp.float32)
    if dense:
        residual = hidden.astype(jnp.float32) + permute_reduce_scatter(attn_term, local_width)
    else:
        residual = hidden.astype(jnp.float32) + lax.psum_scatter(
            attn_term.astype(jnp.bfloat16), "tp", scatter_dimension=1, tiled=True
        ).astype(jnp.float32)
    square_total = lax.psum(jnp.sum(residual * residual, axis=1), "tp")
    moe_in = (residual * lax.rsqrt(square_total / D + epsilon)[:, None] * moe_gain[None, :]).astype(
        jnp.bfloat16
    )
    if dense:
        moe_term, qkv_flat = dense_experts(
            moe_in, expert_ids, route_weights, gate_up_flat, down_full, qkv_flat, here, experts_all
        )
    else:
        moe_term = dispatch_experts(
            moe_in, expert_ids, route_weights, expert_gate_up, expert_down, experts_all, capacity
        )
    routed = residual + moe_term
    layer_out = routed.astype(jnp.bfloat16)
    scaled = (routed * next_gain[None, :]).astype(jnp.bfloat16)
    weight_rows = qkv_flat
    if dense:
        mixed = permute_gather_dot(scaled, weight_rows)
    else:
        mixed = jnp.dot(
            lax.all_gather(scaled, "tp", axis=1, tiled=True),
            weight_rows,
            preferred_element_type=jnp.float32,
        )
    mixed = mixed.reshape(NEW, 3, local_width)
    squares_routed = jnp.sum(routed * routed, axis=1)
    routed_total, query_raw, key_raw = lax.psum(
        (
            squares_routed,
            jnp.sum(mixed[:, 0] * mixed[:, 0], axis=1),
            jnp.sum(mixed[:, 1] * mixed[:, 1], axis=1),
        ),
        "tp",
    )
    x_scale = lax.rsqrt(routed_total / D + epsilon)
    query_pre = mixed[:, 0] * x_scale[:, None]
    key_pre = mixed[:, 1] * x_scale[:, None]
    query_total = query_raw * x_scale * x_scale
    key_total = key_raw * x_scale * x_scale
    next_query = (
        query_pre * lax.rsqrt(query_total / D + epsilon)[:, None] * query_gain[None, :]
    ).astype(jnp.bfloat16)
    next_key = (key_pre * lax.rsqrt(key_total / D + epsilon)[:, None] * key_gain[None, :]).astype(
        jnp.bfloat16
    )
    next_value = (mixed[:, 2] * x_scale[:, None]).astype(jnp.bfloat16)
    return (layer_out, next_query, next_key, next_value)


def solution(mesh):
    return jax.shard_map(
        body,
        mesh=mesh,
        in_specs=(
            P("seq", "tp"),
            P("seq", "tp"),
            P("seq", "tp"),
            P("seq", "tp"),
            P("seq", None, "tp"),
            P("seq", None, "tp"),
            P(),
            P("tp", None),
            P("tp"),
            P("seq", None),
            P("seq", None),
            P("seq", None, None, "tp"),
            P("seq", "tp", None),
            P("tp"),
            P(None, None, "tp"),
            P("tp"),
            P("tp"),
        ),
        out_specs=(P("seq", "tp"), P("seq", "tp"), P("seq", "tp"), P("seq", "tp")),
        check_vma=False,
    )
```

```python
import functools
import math

import jax
import jax.numpy as jnp
from jax import lax
from jax.experimental import pallas as pl
from jax.experimental.pallas import tpu as pltpu
from jax.sharding import PartitionSpec as P

D = 2048
HEAD_DIM = 128
TOP = 8
NEW = 256


epsilon = 1e-05


def flash_kernel(len_ref, q_ref, k_ref, v_ref, nk_ref, nv_ref, o_ref, m_sc, l_sc, acc_sc, *, block, heads, steps):
    j = pl.program_id(0)
    length = len_ref[0]
    valid = (length + block - 1) // block
    tokens = q_ref.shape[0]
    scale = 1.0 / math.sqrt(HEAD_DIM)

    @pl.when(j == 0)
    def _():
        m_sc[...] = jnp.full(m_sc.shape, -1e30, jnp.float32)
        l_sc[...] = jnp.zeros(l_sc.shape, jnp.float32)
        acc_sc[...] = jnp.zeros(acc_sc.shape, jnp.float32)

    def update(keys_ref, values_ref, allowed):
        for h in range(heads):
            cols = slice(h * HEAD_DIM, (h + 1) * HEAD_DIM)
            q = q_ref[:, cols]
            k = keys_ref[:, cols]
            s = lax.dot_general(q, k, (((1,), (1,)), ((), ())), preferred_element_type=jnp.float32) * scale
            s = jnp.where(allowed, s, -1e30)
            m_old = m_sc[h]
            m_new = jnp.maximum(m_old, jnp.max(s, axis=1, keepdims=True))
            alpha = jnp.exp(m_old - m_new)
            p = jnp.where(allowed, jnp.exp(s - m_new), 0.0)
            l_sc[h] = alpha * l_sc[h] + jnp.sum(p, axis=1, keepdims=True)
            pv = jnp.dot(p.astype(jnp.bfloat16), values_ref[:, cols], preferred_element_type=jnp.float32)
            acc_sc[:, cols] = alpha * acc_sc[:, cols] + pv
            m_sc[h] = m_new

    @pl.when(j < valid)
    def _():
        pos = j * block + lax.broadcasted_iota(jnp.int32, (tokens, block), 1)
        update(k_ref, v_ref, pos < length)

    @pl.when(j == steps - 1)
    def _():
        row = lax.broadcasted_iota(jnp.int32, (tokens, tokens), 0)
        col = lax.broadcasted_iota(jnp.int32, (tokens, tokens), 1)
        update(nk_ref, nv_ref, col <= row)
        for h in range(heads):
            cols = slice(h * HEAD_DIM, (h + 1) * HEAD_DIM)
            o_ref[:, cols] = (acc_sc[:, cols] / l_sc[h]).astype(o_ref.dtype)


def flash_attention(length, queries, cache_k, cache_v, new_k, new_v, block=1024):
    tokens, width = queries.shape
    span = cache_k.shape[0]
    block = min(block, span)
    heads = width // HEAD_DIM
    steps = span // block + 1
    last = span // block - 1

    def cache_map(j, len_ref):
        valid = (len_ref[0] + block - 1) // block
        return (jnp.minimum(j, jnp.maximum(valid - 1, 0)), 0)

    grid_spec = pltpu.PrefetchScalarGridSpec(
        num_scalar_prefetch=1,
        grid=(steps,),
        in_specs=[
            pl.BlockSpec((tokens, width), lambda j, l: (0, 0)),
            pl.BlockSpec((block, width), cache_map),
            pl.BlockSpec((block, width), cache_map),
            pl.BlockSpec((tokens, width), lambda j, l: (0, 0)),
            pl.BlockSpec((tokens, width), lambda j, l: (0, 0)),
        ],
        out_specs=pl.BlockSpec((tokens, width), lambda j, l: (0, 0)),
        scratch_shapes=[
            pltpu.VMEM((heads, tokens, 1), jnp.float32),
            pltpu.VMEM((heads, tokens, 1), jnp.float32),
            pltpu.VMEM((tokens, width), jnp.float32),
        ],
    )
    kernel = functools.partial(flash_kernel, block=block, heads=heads, steps=steps)
    return pl.pallas_call(
        kernel,
        grid_spec=grid_spec,
        out_shape=jax.ShapeDtypeStruct((tokens, width), jnp.bfloat16),
        compiler_params=pltpu.CompilerParams(dimension_semantics=("arbitrary",)),
    )(length.reshape(1), queries, cache_k, cache_v, new_k, new_v)


def dense_experts(moe_in, expert_ids, route_weights, expert_gate_up, down_full, qkv_flat, here, experts_all):
    local_experts = expert_gate_up.shape[0]
    hidden_quarter = expert_gate_up.shape[-1] // 2
    tokens, quarter = moe_in.shape
    seq_count = experts_all // local_experts
    gate_w = jnp.sum(
        route_weights[:, :, None]
        * (expert_ids[:, :, None] == jnp.arange(experts_all, dtype=jnp.int32)[None, None, :]),
        axis=1,
    )
    gate_t = jnp.transpose(gate_w)
    gate_hi = gate_t.astype(jnp.bfloat16)
    gate_lo = (gate_t - gate_hi.astype(jnp.float32)).astype(jnp.bfloat16)
    info = jnp.concatenate([gate_hi, gate_lo], axis=0).reshape(-1, quarter)
    packed = jnp.concatenate([moe_in, info], axis=0)
    ring = ring_order(seq_count)
    offsets, blocks = ring_all_gather(packed, ring)
    cuts = sorted({0, min(3, len(blocks)), min(6, len(blocks)), len(blocks)})
    chunks = list(zip(cuts[:-1], cuts[1:]))
    outputs = []
    for begin, end in chunks:
        gathered = jnp.stack(blocks[begin:end])
        count = end - begin
        rows_q = gathered[:, :tokens].reshape(count * tokens, quarter)
        info_all = gathered[:, tokens:].reshape(count, 2, experts_all, tokens).astype(jnp.float32)
        gate_all = info_all[:, 0] + info_all[:, 1]
        gate_local = lax.dynamic_slice_in_dim(gate_all, here * local_experts, local_experts, axis=1)
        gate_local = jnp.transpose(gate_local, (1, 0, 2)).reshape(local_experts, count * tokens)
        rows = pair_gather(rows_q)
        if lax.axis_size("tp") == 4:
            rows = jnp.take(rows, lax.axis_index("tp") ^ jnp.arange(4, dtype=jnp.int32), axis=0)
        if begin == 0:
            rows, expert_gate_up, qkv_flat = lax.optimization_barrier((rows, expert_gate_up, qkv_flat))
        gate_up_split = expert_gate_up.reshape(local_experts, rows.shape[0], quarter, -1)
        projected = jnp.einsum("qtd,eqdf->etf", rows, gate_up_split, preferred_element_type=jnp.float32)
        activated = jax.nn.silu(projected[..., :hidden_quarter]) * projected[..., hidden_quarter:]
        activated = activated.astype(jnp.bfloat16).astype(jnp.float32)
        weighted = (activated * gate_local[:, :, None]).astype(jnp.bfloat16)
        weighted = pair_gather(weighted)
        partial = jnp.einsum(
            "qetf,qefd->td", weighted, down_full, preferred_element_type=jnp.float32
        ).astype(jnp.bfloat16)
        outputs.append(partial.reshape(count, tokens, -1))
    by_offset = {}
    index = 0
    for part in outputs:
        for i in range(part.shape[0]):
            by_offset[offsets[index]] = part[i]
            index += 1
    return ring_reduce_scatter(by_offset, ring), qkv_flat


def permute_reduce_scatter(term, width):
    tp_count = lax.axis_size("tp")
    tp_here = lax.axis_index("tp")
    total = lax.dynamic_slice_in_dim(term, tp_here * width, width, axis=1)
    for shift in range(1, tp_count):
        target = (tp_here + shift) % tp_count
        piece = lax.dynamic_slice_in_dim(term, target * width, width, axis=1).astype(jnp.bfloat16)
        pairs = [(i, (i + shift) % tp_count) for i in range(tp_count)]
        total = total + lax.ppermute(piece, "tp", pairs).astype(jnp.float32)
    return total


def permute_gather_dot(rows, weight):
    tp_count = lax.axis_size("tp")
    tp_here = lax.axis_index("tp")
    width = rows.shape[1]
    total = jnp.dot(
        rows,
        lax.dynamic_slice_in_dim(weight, tp_here * width, width, axis=0),
        preferred_element_type=jnp.float32,
    )
    for shift in range(1, tp_count):
        source = (tp_here - shift) % tp_count
        pairs = [(i, (i + shift) % tp_count) for i in range(tp_count)]
        piece = lax.ppermute(rows, "tp", pairs)
        total = total + jnp.dot(
            piece,
            lax.dynamic_slice_in_dim(weight, source * width, width, axis=0),
            preferred_element_type=jnp.float32,
        )
    return total


def pair_gather(block):
    if lax.axis_size("tp") != 4:
        return lax.all_gather(block, "tp", axis=0, tiled=False)
    far = lax.ppermute(block, "tp", [(i, i ^ 2) for i in range(4)])
    near = lax.ppermute(jnp.stack([block, far]), "tp", [(i, i ^ 1) for i in range(4)])
    return jnp.stack([block, near[0], far, near[1]])


def ring_order(count):
    half = count // 2
    if count % 2 or count < 4:
        return list(range(count))
    return [2 * i for i in range(half)] + [2 * i + 1 for i in reversed(range(half))]


def ring_all_gather(block, cycle):
    count = len(cycle)
    forward = [(cycle[p], cycle[(p + 1) % count]) for p in range(count)]
    backward = [(cycle[p], cycle[(p - 1) % count]) for p in range(count)]
    offsets, blocks = [0], [block]
    ahead, behind = block, block
    for step in range(1, count // 2 + 1):
        ahead = lax.ppermute(ahead, "seq", forward)
        offsets.append((-step) % count)
        blocks.append(ahead)
        if step < count - count // 2:
            behind = lax.ppermute(behind, "seq", backward)
            offsets.append(step)
            blocks.append(behind)
    return offsets, blocks


def ring_reduce_scatter(by_offset, cycle):
    count = len(cycle)
    forward = [(cycle[p], cycle[(p + 1) % count]) for p in range(count)]
    backward = [(cycle[p], cycle[(p - 1) % count]) for p in range(count)]

    def block(offset):
        return by_offset[offset % count].astype(jnp.float32)

    total = block(0)
    for pairs, hops, sign in ((forward, count - 1 - count // 2, 1), (backward, count // 2, -1)):
        if hops == 0:
            continue
        acc = block(sign * hops)
        for step in range(1, hops + 1):
            received = lax.ppermute(acc.astype(jnp.bfloat16), "seq", pairs).astype(jnp.float32)
            if step < hops:
                acc = received + block(sign * (hops - step))
            else:
                total = total + received
    return total


def dispatch_experts(moe_in, expert_ids, route_weights, expert_gate_up, expert_down, experts_all, capacity):
    quarter = moe_in.shape[1]
    local_experts = expert_gate_up.shape[0]
    flat_ids = expert_ids.reshape(NEW * TOP)
    onehot = (flat_ids[:, None] == jnp.arange(experts_all, dtype=jnp.int32)[None, :]).astype(
        jnp.int32
    )
    ranks = jnp.sum((jnp.cumsum(onehot, axis=0) - onehot) * onehot, axis=1)
    target = (flat_ids * capacity + ranks).reshape(NEW, TOP)
    slot_ids = jnp.arange(experts_all * capacity, dtype=jnp.int32)
    selector = jnp.sum(
        (target[None, :, :] == slot_ids[:, None, None]).astype(jnp.int32), axis=2
    ).astype(jnp.bfloat16)
    send_rows = jnp.dot(selector, moe_in, preferred_element_type=jnp.float32).astype(jnp.bfloat16)
    send_rows = send_rows.reshape(experts_all, capacity, quarter)
    received = lax.all_to_all(send_rows, "seq", split_axis=0, concat_axis=1, tiled=True)
    hidden_quarter = expert_gate_up.shape[3]
    gate_up_local = expert_gate_up.reshape(local_experts, D, 2 * hidden_quarter)
    weight_rows = gate_up_local
    projected = jnp.einsum(
        "erd,edf->erf",
        lax.all_gather(received, "tp", axis=2, tiled=True),
        weight_rows,
        preferred_element_type=jnp.float32,
    )
    activated = (
        jax.nn.silu(projected[..., :hidden_quarter]) * projected[..., hidden_quarter:]
    ).astype(jnp.bfloat16)
    down_terms = jnp.einsum(
        "erf,efd->erd", activated, expert_down, preferred_element_type=jnp.float32
    )
    expert_result = lax.psum_scatter(
        down_terms.astype(jnp.bfloat16), "tp", scatter_dimension=2, tiled=True
    )
    returned = lax.all_to_all(
        expert_result, "seq", split_axis=1, concat_axis=0, tiled=True
    ).reshape(experts_all * capacity, quarter)
    picked = jnp.take(returned, target, axis=0)
    return jnp.sum(route_weights[:, :, None] * picked.astype(jnp.float32), axis=1)


def body(
    hidden,
    new_queries,
    new_keys,
    new_values,
    cache_keys,
    cache_values,
    cache_lengths,
    out_proj,
    moe_gain,
    expert_ids,
    route_weights,
    expert_gate_up,
    expert_down,
    next_gain,
    qkv_proj,
    query_gain,
    key_gain,
):
    seq_count = lax.axis_size("seq")
    here = lax.axis_index("seq")
    local_experts = expert_gate_up.shape[0]
    experts_all = local_experts * seq_count
    capacity = max(2, 3 * NEW * TOP // (2 * experts_all))
    dense = NEW <= 2 * capacity
    if dense:
        tp_here = lax.axis_index("tp")
        quarter_width = hidden.shape[1]
        tp_count = lax.axis_size("tp")
        pieces = [lax.dynamic_slice_in_dim(expert_down, tp_here * quarter_width, quarter_width, axis=2)]
        for shift in range(1, tp_count):
            target = (tp_here + shift) % tp_count
            piece = lax.dynamic_slice_in_dim(expert_down, target * quarter_width, quarter_width, axis=2)
            pairs = [(i, (i + shift) % tp_count) for i in range(tp_count)]
            pieces.append(lax.ppermute(piece, "tp", pairs))
        if tp_count == 4:
            order = (tp_here - (tp_here ^ jnp.arange(tp_count, dtype=jnp.int32))) % tp_count
        else:
            order = (tp_here - jnp.arange(tp_count, dtype=jnp.int32)) % tp_count
        down_full = jnp.take(jnp.stack(pieces), order, axis=0)
        gate_up_flat = expert_gate_up.reshape(local_experts, tp_count, quarter_width, -1)
        qkv_flat = qkv_proj.reshape(D, -1)
    local_width = new_queries.shape[1]
    local_heads = local_width // HEAD_DIM
    quarter = hidden.shape[1]
    span = cache_keys.shape[1]
    my_length = lax.dynamic_index_in_dim(cache_lengths, here, 0, keepdims=False)
    attended = flash_attention(
        my_length,
        new_queries,
        cache_keys.reshape(span, local_width),
        cache_values.reshape(span, local_width),
        new_keys,
        new_values,
    )
    if dense:
        attended, down_full = lax.optimization_barrier((attended, down_full))
    else:
        gate_up_flat = expert_gate_up
        qkv_flat = qkv_proj.reshape(D, -1)
    attn_term = jnp.dot(attended, out_proj, preferred_element_type=jnp.float32)
    if dense:
        residual = hidden.astype(jnp.float32) + permute_reduce_scatter(attn_term, local_width)
    else:
        residual = hidden.astype(jnp.float32) + lax.psum_scatter(
            attn_term.astype(jnp.bfloat16), "tp", scatter_dimension=1, tiled=True
        ).astype(jnp.float32)
    square_total = lax.psum(jnp.sum(residual * residual, axis=1), "tp")
    moe_in = (residual * lax.rsqrt(square_total / D + epsilon)[:, None] * moe_gain[None, :]).astype(
        jnp.bfloat16
    )
    if dense:
        moe_term, qkv_flat = dense_experts(
            moe_in, expert_ids, route_weights, gate_up_flat, down_full, qkv_flat, here, experts_all
        )
    else:
        moe_term = dispatch_experts(
            moe_in, expert_ids, route_weights, expert_gate_up, expert_down, experts_all, capacity
        )
    routed = residual + moe_term
    layer_out = routed.astype(jnp.bfloat16)
    scaled = (routed * next_gain[None, :]).astype(jnp.bfloat16)
    weight_rows = qkv_flat
    if dense:
        mixed = permute_gather_dot(scaled, weight_rows)
    else:
        mixed = jnp.dot(
            lax.all_gather(scaled, "tp", axis=1, tiled=True),
            weight_rows,
            preferred_element_type=jnp.float32,
        )
    mixed = mixed.reshape(NEW, 3, local_width)
    squares_routed = jnp.sum(routed * routed, axis=1)
    routed_total, query_raw, key_raw = lax.psum(
        (
            squares_routed,
            jnp.sum(mixed[:, 0] * mixed[:, 0], axis=1),
            jnp.sum(mixed[:, 1] * mixed[:, 1], axis=1),
        ),
        "tp",
    )
    x_scale = lax.rsqrt(routed_total / D + epsilon)
    query_pre = mixed[:, 0] * x_scale[:, None]
    key_pre = mixed[:, 1] * x_scale[:, None]
    query_total = query_raw * x_scale * x_scale
    key_total = key_raw * x_scale * x_scale
    next_query = (
        query_pre * lax.rsqrt(query_total / D + epsilon)[:, None] * query_gain[None, :]
    ).astype(jnp.bfloat16)
    next_key = (key_pre * lax.rsqrt(key_total / D + epsilon)[:, None] * key_gain[None, :]).astype(
        jnp.bfloat16
    )
    next_value = (mixed[:, 2] * x_scale[:, None]).astype(jnp.bfloat16)
    return (layer_out, next_query, next_key, next_value)


def solution(mesh):
    return jax.shard_map(
        body,
        mesh=mesh,
        in_specs=(
            P("seq", "tp"),
            P("seq", "tp"),
            P("seq", "tp"),
            P("seq", "tp"),
            P("seq", None, "tp"),
            P("seq", None, "tp"),
            P(),
            P("tp", None),
            P("tp"),
            P("seq", None),
            P("seq", None),
            P("seq", None, None, "tp"),
            P("seq", "tp", None),
            P("tp"),
            P(None, None, "tp"),
            P("tp"),
            P("tp"),
        ),
        out_specs=(P("seq", "tp"), P("seq", "tp"), P("seq", "tp"), P("seq", "tp")),
        check_vma=False,
    )
```

```python
import functools
import math

import jax
import jax.numpy as jnp
from jax import lax
from jax.experimental import pallas as pl
from jax.experimental.pallas import tpu as pltpu
from jax.sharding import PartitionSpec as P

D = 2048
HEAD_DIM = 128
TOP = 8
NEW = 256


epsilon = 1e-05


def flash_kernel(len_ref, q_ref, k_ref, v_ref, nk_ref, nv_ref, o_ref, m_sc, l_sc, acc_sc, *, block, heads, steps):
    j = pl.program_id(0)
    length = len_ref[0]
    valid = (length + block - 1) // block
    tokens = q_ref.shape[0]
    scale = 1.0 / math.sqrt(HEAD_DIM)

    @pl.when(j == 0)
    def _():
        m_sc[...] = jnp.full(m_sc.shape, -1e30, jnp.float32)
        l_sc[...] = jnp.zeros(l_sc.shape, jnp.float32)
        acc_sc[...] = jnp.zeros(acc_sc.shape, jnp.float32)

    def update(keys_ref, values_ref, allowed):
        for h in range(heads):
            cols = slice(h * HEAD_DIM, (h + 1) * HEAD_DIM)
            q = q_ref[:, cols]
            k = keys_ref[:, cols]
            s = lax.dot_general(q, k, (((1,), (1,)), ((), ())), preferred_element_type=jnp.float32) * scale
            s = jnp.where(allowed, s, -1e30)
            m_old = m_sc[h]
            m_new = jnp.maximum(m_old, jnp.max(s, axis=1, keepdims=True))
            alpha = jnp.exp(m_old - m_new)
            p = jnp.where(allowed, jnp.exp(s - m_new), 0.0)
            l_sc[h] = alpha * l_sc[h] + jnp.sum(p, axis=1, keepdims=True)
            pv = jnp.dot(p.astype(jnp.bfloat16), values_ref[:, cols], preferred_element_type=jnp.float32)
            acc_sc[:, cols] = alpha * acc_sc[:, cols] + pv
            m_sc[h] = m_new

    @pl.when(j < valid)
    def _():
        pos = j * block + lax.broadcasted_iota(jnp.int32, (tokens, block), 1)
        update(k_ref, v_ref, pos < length)

    @pl.when(j == steps - 1)
    def _():
        row = lax.broadcasted_iota(jnp.int32, (tokens, tokens), 0)
        col = lax.broadcasted_iota(jnp.int32, (tokens, tokens), 1)
        update(nk_ref, nv_ref, col <= row)
        for h in range(heads):
            cols = slice(h * HEAD_DIM, (h + 1) * HEAD_DIM)
            o_ref[:, cols] = (acc_sc[:, cols] / l_sc[h]).astype(o_ref.dtype)


def flash_attention(length, queries, cache_k, cache_v, new_k, new_v, block=1024):
    tokens, width = queries.shape
    span = cache_k.shape[0]
    block = min(block, span)
    heads = width // HEAD_DIM
    steps = span // block + 1
    last = span // block - 1

    def cache_map(j, len_ref):
        valid = (len_ref[0] + block - 1) // block
        return (jnp.minimum(j, jnp.maximum(valid - 1, 0)), 0)

    grid_spec = pltpu.PrefetchScalarGridSpec(
        num_scalar_prefetch=1,
        grid=(steps,),
        in_specs=[
            pl.BlockSpec((tokens, width), lambda j, l: (0, 0)),
            pl.BlockSpec((block, width), cache_map),
            pl.BlockSpec((block, width), cache_map),
            pl.BlockSpec((tokens, width), lambda j, l: (0, 0)),
            pl.BlockSpec((tokens, width), lambda j, l: (0, 0)),
        ],
        out_specs=pl.BlockSpec((tokens, width), lambda j, l: (0, 0)),
        scratch_shapes=[
            pltpu.VMEM((heads, tokens, 1), jnp.float32),
            pltpu.VMEM((heads, tokens, 1), jnp.float32),
            pltpu.VMEM((tokens, width), jnp.float32),
        ],
    )
    kernel = functools.partial(flash_kernel, block=block, heads=heads, steps=steps)
    return pl.pallas_call(
        kernel,
        grid_spec=grid_spec,
        out_shape=jax.ShapeDtypeStruct((tokens, width), jnp.bfloat16),
        compiler_params=pltpu.CompilerParams(dimension_semantics=("arbitrary",)),
    )(length.reshape(1), queries, cache_k, cache_v, new_k, new_v)


def dense_experts(moe_in, expert_ids, route_weights, expert_gate_up, down_full, qkv_flat, here, experts_all):
    local_experts = expert_gate_up.shape[0]
    hidden_quarter = expert_gate_up.shape[-1] // 2
    tokens, quarter = moe_in.shape
    seq_count = experts_all // local_experts
    gate_w = jnp.sum(
        route_weights[:, :, None]
        * (expert_ids[:, :, None] == jnp.arange(experts_all, dtype=jnp.int32)[None, None, :]),
        axis=1,
    )
    gate_t = jnp.transpose(gate_w)
    gate_hi = gate_t.astype(jnp.bfloat16)
    gate_lo = (gate_t - gate_hi.astype(jnp.float32)).astype(jnp.bfloat16)
    info = jnp.concatenate([gate_hi, gate_lo], axis=0).reshape(-1, quarter)
    packed = jnp.concatenate([moe_in, info], axis=0)
    ring = ring_order(seq_count)
    offsets, blocks = ring_all_gather(packed, ring)
    cuts = sorted({0, min(3, len(blocks)), min(6, len(blocks)), len(blocks)})
    chunks = list(zip(cuts[:-1], cuts[1:]))
    outputs = []
    for begin, end in chunks:
        gathered = jnp.stack(blocks[begin:end])
        count = end - begin
        rows_q = gathered[:, :tokens].reshape(count * tokens, quarter)
        info_all = gathered[:, tokens:].reshape(count, 2, experts_all, tokens).astype(jnp.float32)
        gate_all = info_all[:, 0] + info_all[:, 1]
        gate_local = lax.dynamic_slice_in_dim(gate_all, here * local_experts, local_experts, axis=1)
        gate_local = jnp.transpose(gate_local, (1, 0, 2)).reshape(local_experts, count * tokens)
        rows = pair_gather(rows_q)
        if begin == 0:
            rows, expert_gate_up, qkv_flat = lax.optimization_barrier((rows, expert_gate_up, qkv_flat))
        gate_up_split = expert_gate_up.reshape(local_experts, rows.shape[0], quarter, -1)
        projected = jnp.einsum("qtd,eqdf->etf", rows, gate_up_split, preferred_element_type=jnp.float32)
        activated = jax.nn.silu(projected[..., :hidden_quarter]) * projected[..., hidden_quarter:]
        activated = activated.astype(jnp.bfloat16).astype(jnp.float32)
        weighted = (activated * gate_local[:, :, None]).astype(jnp.bfloat16)
        weighted = pair_gather(weighted)
        partial = jnp.einsum(
            "qetf,qefd->td", weighted, down_full, preferred_element_type=jnp.float32
        ).astype(jnp.bfloat16)
        outputs.append(partial.reshape(count, tokens, -1))
    by_offset = {}
    index = 0
    for part in outputs:
        for i in range(part.shape[0]):
            by_offset[offsets[index]] = part[i]
            index += 1
    return ring_reduce_scatter(by_offset, ring), qkv_flat


def permute_reduce_scatter(term, width):
    tp_count = lax.axis_size("tp")
    tp_here = lax.axis_index("tp")
    total = lax.dynamic_slice_in_dim(term, tp_here * width, width, axis=1)
    for shift in range(1, tp_count):
        target = (tp_here + shift) % tp_count
        piece = lax.dynamic_slice_in_dim(term, target * width, width, axis=1).astype(jnp.bfloat16)
        pairs = [(i, (i + shift) % tp_count) for i in range(tp_count)]
        total = total + lax.ppermute(piece, "tp", pairs).astype(jnp.float32)
    return total


def permute_gather_dot(rows, weight):
    tp_count = lax.axis_size("tp")
    tp_here = lax.axis_index("tp")
    width = rows.shape[1]
    total = jnp.dot(
        rows,
        lax.dynamic_slice_in_dim(weight, tp_here * width, width, axis=0),
        preferred_element_type=jnp.float32,
    )
    if tp_count == 4:
        far = lax.ppermute(rows, "tp", [(i, i ^ 2) for i in range(4)])
        near = lax.ppermute(jnp.stack([rows, far]), "tp", [(i, i ^ 1) for i in range(4)])
        for piece, source in ((far, tp_here ^ 2), (near[0], tp_here ^ 1), (near[1], tp_here ^ 3)):
            total = total + jnp.dot(
                piece,
                lax.dynamic_slice_in_dim(weight, source * width, width, axis=0),
                preferred_element_type=jnp.float32,
            )
        return total
    for shift in range(1, tp_count):
        source = (tp_here - shift) % tp_count
        pairs = [(i, (i + shift) % tp_count) for i in range(tp_count)]
        piece = lax.ppermute(rows, "tp", pairs)
        total = total + jnp.dot(
            piece,
            lax.dynamic_slice_in_dim(weight, source * width, width, axis=0),
            preferred_element_type=jnp.float32,
        )
    return total


def pair_gather(block):
    if lax.axis_size("tp") != 4:
        return lax.all_gather(block, "tp", axis=0, tiled=False)
    far = lax.ppermute(block, "tp", [(i, i ^ 2) for i in range(4)])
    near = lax.ppermute(jnp.stack([block, far]), "tp", [(i, i ^ 1) for i in range(4)])
    return jnp.stack([block, near[0], far, near[1]])


def ring_order(count):
    half = count // 2
    if count % 2 or count < 4:
        return list(range(count))
    return [2 * i for i in range(half)] + [2 * i + 1 for i in reversed(range(half))]


def ring_all_gather(block, cycle):
    count = len(cycle)
    forward = [(cycle[p], cycle[(p + 1) % count]) for p in range(count)]
    backward = [(cycle[p], cycle[(p - 1) % count]) for p in range(count)]
    offsets, blocks = [0], [block]
    ahead, behind = block, block
    for step in range(1, count // 2 + 1):
        ahead = lax.ppermute(ahead, "seq", forward)
        offsets.append((-step) % count)
        blocks.append(ahead)
        if step < count - count // 2:
            behind = lax.ppermute(behind, "seq", backward)
            offsets.append(step)
            blocks.append(behind)
    return offsets, blocks


def ring_reduce_scatter(by_offset, cycle):
    count = len(cycle)
    forward = [(cycle[p], cycle[(p + 1) % count]) for p in range(count)]
    backward = [(cycle[p], cycle[(p - 1) % count]) for p in range(count)]

    def block(offset):
        return by_offset[offset % count].astype(jnp.float32)

    total = block(0)
    for pairs, hops, sign in ((forward, count - 1 - count // 2, 1), (backward, count // 2, -1)):
        if hops == 0:
            continue
        acc = block(sign * hops)
        for step in range(1, hops + 1):
            received = lax.ppermute(acc.astype(jnp.bfloat16), "seq", pairs).astype(jnp.float32)
            if step < hops:
                acc = received + block(sign * (hops - step))
            else:
                total = total + received
    return total


def dispatch_experts(moe_in, expert_ids, route_weights, expert_gate_up, expert_down, experts_all, capacity):
    quarter = moe_in.shape[1]
    local_experts = expert_gate_up.shape[0]
    flat_ids = expert_ids.reshape(NEW * TOP)
    onehot = (flat_ids[:, None] == jnp.arange(experts_all, dtype=jnp.int32)[None, :]).astype(
        jnp.int32
    )
    ranks = jnp.sum((jnp.cumsum(onehot, axis=0) - onehot) * onehot, axis=1)
    target = (flat_ids * capacity + ranks).reshape(NEW, TOP)
    slot_ids = jnp.arange(experts_all * capacity, dtype=jnp.int32)
    selector = jnp.sum(
        (target[None, :, :] == slot_ids[:, None, None]).astype(jnp.int32), axis=2
    ).astype(jnp.bfloat16)
    send_rows = jnp.dot(selector, moe_in, preferred_element_type=jnp.float32).astype(jnp.bfloat16)
    send_rows = send_rows.reshape(experts_all, capacity, quarter)
    received = lax.all_to_all(send_rows, "seq", split_axis=0, concat_axis=1, tiled=True)
    hidden_quarter = expert_gate_up.shape[3]
    gate_up_local = expert_gate_up.reshape(local_experts, D, 2 * hidden_quarter)
    weight_rows = gate_up_local
    projected = jnp.einsum(
        "erd,edf->erf",
        lax.all_gather(received, "tp", axis=2, tiled=True),
        weight_rows,
        preferred_element_type=jnp.float32,
    )
    activated = (
        jax.nn.silu(projected[..., :hidden_quarter]) * projected[..., hidden_quarter:]
    ).astype(jnp.bfloat16)
    down_terms = jnp.einsum(
        "erf,efd->erd", activated, expert_down, preferred_element_type=jnp.float32
    )
    expert_result = lax.psum_scatter(
        down_terms.astype(jnp.bfloat16), "tp", scatter_dimension=2, tiled=True
    )
    returned = lax.all_to_all(
        expert_result, "seq", split_axis=1, concat_axis=0, tiled=True
    ).reshape(experts_all * capacity, quarter)
    picked = jnp.take(returned, target, axis=0)
    return jnp.sum(route_weights[:, :, None] * picked.astype(jnp.float32), axis=1)


def body(
    hidden,
    new_queries,
    new_keys,
    new_values,
    cache_keys,
    cache_values,
    cache_lengths,
    out_proj,
    moe_gain,
    expert_ids,
    route_weights,
    expert_gate_up,
    expert_down,
    next_gain,
    qkv_proj,
    query_gain,
    key_gain,
):
    seq_count = lax.axis_size("seq")
    here = lax.axis_index("seq")
    local_experts = expert_gate_up.shape[0]
    experts_all = local_experts * seq_count
    capacity = max(2, 3 * NEW * TOP // (2 * experts_all))
    dense = NEW <= 2 * capacity
    if dense:
        tp_here = lax.axis_index("tp")
        quarter_width = hidden.shape[1]
        tp_count = lax.axis_size("tp")
        pieces = [lax.dynamic_slice_in_dim(expert_down, tp_here * quarter_width, quarter_width, axis=2)]
        for shift in range(1, tp_count):
            target = (tp_here + shift) % tp_count
            piece = lax.dynamic_slice_in_dim(expert_down, target * quarter_width, quarter_width, axis=2)
            pairs = [(i, (i + shift) % tp_count) for i in range(tp_count)]
            pieces.append(lax.ppermute(piece, "tp", pairs))
        if tp_count == 4:
            order = (tp_here - (tp_here ^ jnp.arange(tp_count, dtype=jnp.int32))) % tp_count
        else:
            order = (tp_here - jnp.arange(tp_count, dtype=jnp.int32)) % tp_count
        down_full = jnp.take(jnp.stack(pieces), order, axis=0)
        gate_up_flat = expert_gate_up.reshape(local_experts, tp_count, quarter_width, -1)
        if tp_count == 4:
            source_order = tp_here ^ jnp.arange(tp_count, dtype=jnp.int32)
            gate_up_flat = jnp.take(gate_up_flat, source_order, axis=1)
        qkv_flat = qkv_proj.reshape(D, -1)
    local_width = new_queries.shape[1]
    local_heads = local_width // HEAD_DIM
    quarter = hidden.shape[1]
    span = cache_keys.shape[1]
    my_length = lax.dynamic_index_in_dim(cache_lengths, here, 0, keepdims=False)
    attended = flash_attention(
        my_length,
        new_queries,
        cache_keys.reshape(span, local_width),
        cache_values.reshape(span, local_width),
        new_keys,
        new_values,
    )
    if dense:
        attended, down_full = lax.optimization_barrier((attended, down_full))
    else:
        gate_up_flat = expert_gate_up
        qkv_flat = qkv_proj.reshape(D, -1)
    attn_term = jnp.dot(attended, out_proj, preferred_element_type=jnp.float32)
    if dense:
        residual = hidden.astype(jnp.float32) + permute_reduce_scatter(attn_term, local_width)
    else:
        residual = hidden.astype(jnp.float32) + lax.psum_scatter(
            attn_term.astype(jnp.bfloat16), "tp", scatter_dimension=1, tiled=True
        ).astype(jnp.float32)
    square_total = lax.psum(jnp.sum(residual * residual, axis=1), "tp")
    moe_in = (residual * lax.rsqrt(square_total / D + epsilon)[:, None] * moe_gain[None, :]).astype(
        jnp.bfloat16
    )
    if dense:
        moe_term, qkv_flat = dense_experts(
            moe_in, expert_ids, route_weights, gate_up_flat, down_full, qkv_flat, here, experts_all
        )
    else:
        moe_term = dispatch_experts(
            moe_in, expert_ids, route_weights, expert_gate_up, expert_down, experts_all, capacity
        )
    routed = residual + moe_term
    layer_out = routed.astype(jnp.bfloat16)
    scaled = (routed * next_gain[None, :]).astype(jnp.bfloat16)
    weight_rows = qkv_flat
    if dense:
        mixed = permute_gather_dot(scaled, weight_rows)
    else:
        mixed = jnp.dot(
            lax.all_gather(scaled, "tp", axis=1, tiled=True),
            weight_rows,
            preferred_element_type=jnp.float32,
        )
    mixed = mixed.reshape(NEW, 3, local_width)
    squares_routed = jnp.sum(routed * routed, axis=1)
    routed_total, query_raw, key_raw = lax.psum(
        (
            squares_routed,
            jnp.sum(mixed[:, 0] * mixed[:, 0], axis=1),
            jnp.sum(mixed[:, 1] * mixed[:, 1], axis=1),
        ),
        "tp",
    )
    x_scale = lax.rsqrt(routed_total / D + epsilon)
    query_pre = mixed[:, 0] * x_scale[:, None]
    key_pre = mixed[:, 1] * x_scale[:, None]
    query_total = query_raw * x_scale * x_scale
    key_total = key_raw * x_scale * x_scale
    next_query = (
        query_pre * lax.rsqrt(query_total / D + epsilon)[:, None] * query_gain[None, :]
    ).astype(jnp.bfloat16)
    next_key = (key_pre * lax.rsqrt(key_total / D + epsilon)[:, None] * key_gain[None, :]).astype(
        jnp.bfloat16
    )
    next_value = (mixed[:, 2] * x_scale[:, None]).astype(jnp.bfloat16)
    return (layer_out, next_query, next_key, next_value)


def solution(mesh):
    return jax.shard_map(
        body,
        mesh=mesh,
        in_specs=(
            P("seq", "tp"),
            P("seq", "tp"),
            P("seq", "tp"),
            P("seq", "tp"),
            P("seq", None, "tp"),
            P("seq", None, "tp"),
            P(),
            P("tp", None),
            P("tp"),
            P("seq", None),
            P("seq", None),
            P("seq", None, None, "tp"),
            P("seq", "tp", None),
            P("tp"),
            P(None, None, "tp"),
            P("tp"),
            P("tp"),
        ),
        out_specs=(P("seq", "tp"), P("seq", "tp"), P("seq", "tp"), P("seq", "tp")),
        check_vma=False,
    )
```

```python
import functools
import math

import jax
import jax.numpy as jnp
from jax import lax
from jax.experimental import pallas as pl
from jax.experimental.pallas import tpu as pltpu
from jax.sharding import PartitionSpec as P

D = 2048
HEAD_DIM = 128
TOP = 8
NEW = 256


epsilon = 1e-05


def flash_kernel(len_ref, q_ref, k_ref, v_ref, nk_ref, nv_ref, o_ref, m_sc, l_sc, acc_sc, *, block, heads, steps):
    j = pl.program_id(0)
    length = len_ref[0]
    valid = (length + block - 1) // block
    tokens = q_ref.shape[0]
    scale = 1.0 / math.sqrt(HEAD_DIM)

    @pl.when(j == 0)
    def _():
        m_sc[...] = jnp.full(m_sc.shape, -1e30, jnp.float32)
        l_sc[...] = jnp.zeros(l_sc.shape, jnp.float32)
        acc_sc[...] = jnp.zeros(acc_sc.shape, jnp.float32)

    def update(keys_ref, values_ref, allowed):
        for h in range(heads):
            cols = slice(h * HEAD_DIM, (h + 1) * HEAD_DIM)
            q = q_ref[:, cols]
            k = keys_ref[:, cols]
            s = lax.dot_general(q, k, (((1,), (1,)), ((), ())), preferred_element_type=jnp.float32) * scale
            s = jnp.where(allowed, s, -1e30)
            m_old = m_sc[h]
            m_new = jnp.maximum(m_old, jnp.max(s, axis=1, keepdims=True))
            alpha = jnp.exp(m_old - m_new)
            p = jnp.where(allowed, jnp.exp(s - m_new), 0.0)
            l_sc[h] = alpha * l_sc[h] + jnp.sum(p, axis=1, keepdims=True)
            pv = jnp.dot(p.astype(jnp.bfloat16), values_ref[:, cols], preferred_element_type=jnp.float32)
            acc_sc[:, cols] = alpha * acc_sc[:, cols] + pv
            m_sc[h] = m_new

    @pl.when(j < valid)
    def _():
        pos = j * block + lax.broadcasted_iota(jnp.int32, (tokens, block), 1)
        update(k_ref, v_ref, pos < length)

    @pl.when(j == steps - 1)
    def _():
        row = lax.broadcasted_iota(jnp.int32, (tokens, tokens), 0)
        col = lax.broadcasted_iota(jnp.int32, (tokens, tokens), 1)
        update(nk_ref, nv_ref, col <= row)
        for h in range(heads):
            cols = slice(h * HEAD_DIM, (h + 1) * HEAD_DIM)
            o_ref[:, cols] = (acc_sc[:, cols] / l_sc[h]).astype(o_ref.dtype)


def flash_attention(length, queries, cache_k, cache_v, new_k, new_v, block=2048):
    tokens, width = queries.shape
    span = cache_k.shape[0]
    block = min(block, span)
    heads = width // HEAD_DIM
    steps = span // block + 1
    last = span // block - 1

    def cache_map(j, len_ref):
        valid = (len_ref[0] + block - 1) // block
        return (jnp.minimum(j, jnp.maximum(valid - 1, 0)), 0)

    grid_spec = pltpu.PrefetchScalarGridSpec(
        num_scalar_prefetch=1,
        grid=(steps,),
        in_specs=[
            pl.BlockSpec((tokens, width), lambda j, l: (0, 0)),
            pl.BlockSpec((block, width), cache_map),
            pl.BlockSpec((block, width), cache_map),
            pl.BlockSpec((tokens, width), lambda j, l: (0, 0)),
            pl.BlockSpec((tokens, width), lambda j, l: (0, 0)),
        ],
        out_specs=pl.BlockSpec((tokens, width), lambda j, l: (0, 0)),
        scratch_shapes=[
            pltpu.VMEM((heads, tokens, 1), jnp.float32),
            pltpu.VMEM((heads, tokens, 1), jnp.float32),
            pltpu.VMEM((tokens, width), jnp.float32),
        ],
    )
    kernel = functools.partial(flash_kernel, block=block, heads=heads, steps=steps)
    return pl.pallas_call(
        kernel,
        grid_spec=grid_spec,
        out_shape=jax.ShapeDtypeStruct((tokens, width), jnp.bfloat16),
        compiler_params=pltpu.CompilerParams(dimension_semantics=("arbitrary",)),
    )(length.reshape(1), queries, cache_k, cache_v, new_k, new_v)


def dense_experts(moe_in, expert_ids, route_weights, expert_gate_up, down_full, qkv_flat, here, experts_all):
    local_experts = expert_gate_up.shape[0]
    hidden_quarter = expert_gate_up.shape[-1] // 2
    tokens, quarter = moe_in.shape
    seq_count = experts_all // local_experts
    gate_w = jnp.sum(
        route_weights[:, :, None]
        * (expert_ids[:, :, None] == jnp.arange(experts_all, dtype=jnp.int32)[None, None, :]),
        axis=1,
    )
    gate_t = jnp.transpose(gate_w)
    gate_hi = gate_t.astype(jnp.bfloat16)
    gate_lo = (gate_t - gate_hi.astype(jnp.float32)).astype(jnp.bfloat16)
    info = jnp.concatenate([gate_hi, gate_lo], axis=0).reshape(-1, quarter)
    packed = jnp.concatenate([moe_in, info], axis=0)
    ring = ring_order(seq_count)
    offsets, blocks = ring_all_gather(packed, ring)
    cuts = sorted({0, min(3, len(blocks)), min(6, len(blocks)), len(blocks)})
    chunks = list(zip(cuts[:-1], cuts[1:]))
    outputs = []
    for begin, end in chunks:
        gathered = jnp.stack(blocks[begin:end])
        count = end - begin
        rows_q = gathered[:, :tokens].reshape(count * tokens, quarter)
        info_all = gathered[:, tokens:].reshape(count, 2, experts_all, tokens).astype(jnp.float32)
        gate_all = info_all[:, 0] + info_all[:, 1]
        gate_local = lax.dynamic_slice_in_dim(gate_all, here * local_experts, local_experts, axis=1)
        gate_local = jnp.transpose(gate_local, (1, 0, 2)).reshape(local_experts, count * tokens)
        rows = pair_gather(rows_q)
        if begin == 0:
            rows, expert_gate_up, qkv_flat = lax.optimization_barrier((rows, expert_gate_up, qkv_flat))
        gate_up_split = expert_gate_up.reshape(local_experts, rows.shape[0], quarter, -1)
        projected = jnp.einsum("qtd,eqdf->etf", rows, gate_up_split, preferred_element_type=jnp.float32)
        activated = jax.nn.silu(projected[..., :hidden_quarter]) * projected[..., hidden_quarter:]
        activated = activated.astype(jnp.bfloat16).astype(jnp.float32)
        weighted = (activated * gate_local[:, :, None]).astype(jnp.bfloat16)
        weighted = pair_gather(weighted)
        partial = jnp.einsum(
            "qetf,qefd->td", weighted, down_full, preferred_element_type=jnp.float32
        ).astype(jnp.bfloat16)
        outputs.append(partial.reshape(count, tokens, -1))
    by_offset = {}
    index = 0
    for part in outputs:
        for i in range(part.shape[0]):
            by_offset[offsets[index]] = part[i]
            index += 1
    return ring_reduce_scatter(by_offset, ring), qkv_flat


def permute_reduce_scatter(term, width):
    tp_count = lax.axis_size("tp")
    tp_here = lax.axis_index("tp")
    total = lax.dynamic_slice_in_dim(term, tp_here * width, width, axis=1)
    for shift in range(1, tp_count):
        target = (tp_here + shift) % tp_count
        piece = lax.dynamic_slice_in_dim(term, target * width, width, axis=1).astype(jnp.bfloat16)
        pairs = [(i, (i + shift) % tp_count) for i in range(tp_count)]
        total = total + lax.ppermute(piece, "tp", pairs).astype(jnp.float32)
    return total


def permute_gather_dot(rows, weight):
    tp_count = lax.axis_size("tp")
    tp_here = lax.axis_index("tp")
    width = rows.shape[1]
    total = jnp.dot(
        rows,
        lax.dynamic_slice_in_dim(weight, tp_here * width, width, axis=0),
        preferred_element_type=jnp.float32,
    )
    if tp_count == 4:
        far = lax.ppermute(rows, "tp", [(i, i ^ 2) for i in range(4)])
        near = lax.ppermute(jnp.stack([rows, far]), "tp", [(i, i ^ 1) for i in range(4)])
        for piece, source in ((far, tp_here ^ 2), (near[0], tp_here ^ 1), (near[1], tp_here ^ 3)):
            total = total + jnp.dot(
                piece,
                lax.dynamic_slice_in_dim(weight, source * width, width, axis=0),
                preferred_element_type=jnp.float32,
            )
        return total
    for shift in range(1, tp_count):
        source = (tp_here - shift) % tp_count
        pairs = [(i, (i + shift) % tp_count) for i in range(tp_count)]
        piece = lax.ppermute(rows, "tp", pairs)
        total = total + jnp.dot(
            piece,
            lax.dynamic_slice_in_dim(weight, source * width, width, axis=0),
            preferred_element_type=jnp.float32,
        )
    return total


def pair_gather(block):
    if lax.axis_size("tp") != 4:
        return lax.all_gather(block, "tp", axis=0, tiled=False)
    far = lax.ppermute(block, "tp", [(i, i ^ 2) for i in range(4)])
    near = lax.ppermute(jnp.stack([block, far]), "tp", [(i, i ^ 1) for i in range(4)])
    return jnp.stack([block, near[0], far, near[1]])


def ring_order(count):
    half = count // 2
    if count % 2 or count < 4:
        return list(range(count))
    return [2 * i for i in range(half)] + [2 * i + 1 for i in reversed(range(half))]


def ring_all_gather(block, cycle):
    count = len(cycle)
    forward = [(cycle[p], cycle[(p + 1) % count]) for p in range(count)]
    backward = [(cycle[p], cycle[(p - 1) % count]) for p in range(count)]
    offsets, blocks = [0], [block]
    ahead, behind = block, block
    for step in range(1, count // 2 + 1):
        ahead = lax.ppermute(ahead, "seq", forward)
        offsets.append((-step) % count)
        blocks.append(ahead)
        if step < count - count // 2:
            behind = lax.ppermute(behind, "seq", backward)
            offsets.append(step)
            blocks.append(behind)
    return offsets, blocks


def ring_reduce_scatter(by_offset, cycle):
    count = len(cycle)
    forward = [(cycle[p], cycle[(p + 1) % count]) for p in range(count)]
    backward = [(cycle[p], cycle[(p - 1) % count]) for p in range(count)]

    def block(offset):
        return by_offset[offset % count].astype(jnp.float32)

    total = block(0)
    for pairs, hops, sign in ((forward, count - 1 - count // 2, 1), (backward, count // 2, -1)):
        if hops == 0:
            continue
        acc = block(sign * hops)
        for step in range(1, hops + 1):
            received = lax.ppermute(acc.astype(jnp.bfloat16), "seq", pairs).astype(jnp.float32)
            if step < hops:
                acc = received + block(sign * (hops - step))
            else:
                total = total + received
    return total


def dispatch_experts(moe_in, expert_ids, route_weights, expert_gate_up, expert_down, experts_all, capacity):
    quarter = moe_in.shape[1]
    local_experts = expert_gate_up.shape[0]
    flat_ids = expert_ids.reshape(NEW * TOP)
    onehot = (flat_ids[:, None] == jnp.arange(experts_all, dtype=jnp.int32)[None, :]).astype(
        jnp.int32
    )
    ranks = jnp.sum((jnp.cumsum(onehot, axis=0) - onehot) * onehot, axis=1)
    target = (flat_ids * capacity + ranks).reshape(NEW, TOP)
    slot_ids = jnp.arange(experts_all * capacity, dtype=jnp.int32)
    selector = jnp.sum(
        (target[None, :, :] == slot_ids[:, None, None]).astype(jnp.int32), axis=2
    ).astype(jnp.bfloat16)
    send_rows = jnp.dot(selector, moe_in, preferred_element_type=jnp.float32).astype(jnp.bfloat16)
    send_rows = send_rows.reshape(experts_all, capacity, quarter)
    received = lax.all_to_all(send_rows, "seq", split_axis=0, concat_axis=1, tiled=True)
    hidden_quarter = expert_gate_up.shape[3]
    gate_up_local = expert_gate_up.reshape(local_experts, D, 2 * hidden_quarter)
    weight_rows = gate_up_local
    projected = jnp.einsum(
        "erd,edf->erf",
        lax.all_gather(received, "tp", axis=2, tiled=True),
        weight_rows,
        preferred_element_type=jnp.float32,
    )
    activated = (
        jax.nn.silu(projected[..., :hidden_quarter]) * projected[..., hidden_quarter:]
    ).astype(jnp.bfloat16)
    down_terms = jnp.einsum(
        "erf,efd->erd", activated, expert_down, preferred_element_type=jnp.float32
    )
    expert_result = lax.psum_scatter(
        down_terms.astype(jnp.bfloat16), "tp", scatter_dimension=2, tiled=True
    )
    returned = lax.all_to_all(
        expert_result, "seq", split_axis=1, concat_axis=0, tiled=True
    ).reshape(experts_all * capacity, quarter)
    picked = jnp.take(returned, target, axis=0)
    return jnp.sum(route_weights[:, :, None] * picked.astype(jnp.float32), axis=1)


def body(
    hidden,
    new_queries,
    new_keys,
    new_values,
    cache_keys,
    cache_values,
    cache_lengths,
    out_proj,
    moe_gain,
    expert_ids,
    route_weights,
    expert_gate_up,
    expert_down,
    next_gain,
    qkv_proj,
    query_gain,
    key_gain,
):
    seq_count = lax.axis_size("seq")
    here = lax.axis_index("seq")
    local_experts = expert_gate_up.shape[0]
    experts_all = local_experts * seq_count
    capacity = max(2, 3 * NEW * TOP // (2 * experts_all))
    dense = NEW <= 2 * capacity
    if dense:
        tp_here = lax.axis_index("tp")
        quarter_width = hidden.shape[1]
        tp_count = lax.axis_size("tp")
        pieces = [lax.dynamic_slice_in_dim(expert_down, tp_here * quarter_width, quarter_width, axis=2)]
        for shift in range(1, tp_count):
            target = (tp_here + shift) % tp_count
            piece = lax.dynamic_slice_in_dim(expert_down, target * quarter_width, quarter_width, axis=2)
            pairs = [(i, (i + shift) % tp_count) for i in range(tp_count)]
            pieces.append(lax.ppermute(piece, "tp", pairs))
        if tp_count == 4:
            order = (tp_here - (tp_here ^ jnp.arange(tp_count, dtype=jnp.int32))) % tp_count
        else:
            order = (tp_here - jnp.arange(tp_count, dtype=jnp.int32)) % tp_count
        down_full = jnp.take(jnp.stack(pieces), order, axis=0)
        gate_up_flat = expert_gate_up.reshape(local_experts, tp_count, quarter_width, -1)
        if tp_count == 4:
            source_order = tp_here ^ jnp.arange(tp_count, dtype=jnp.int32)
            gate_up_flat = jnp.take(gate_up_flat, source_order, axis=1)
        qkv_flat = qkv_proj.reshape(D, -1)
    local_width = new_queries.shape[1]
    local_heads = local_width // HEAD_DIM
    quarter = hidden.shape[1]
    span = cache_keys.shape[1]
    my_length = lax.dynamic_index_in_dim(cache_lengths, here, 0, keepdims=False)
    attended = flash_attention(
        my_length,
        new_queries,
        cache_keys.reshape(span, local_width),
        cache_values.reshape(span, local_width),
        new_keys,
        new_values,
    )
    if dense:
        attended, down_full = lax.optimization_barrier((attended, down_full))
    else:
        gate_up_flat = expert_gate_up
        qkv_flat = qkv_proj.reshape(D, -1)
    attn_term = jnp.dot(attended, out_proj, preferred_element_type=jnp.float32)
    if dense:
        residual = hidden.astype(jnp.float32) + permute_reduce_scatter(attn_term, local_width)
    else:
        residual = hidden.astype(jnp.float32) + lax.psum_scatter(
            attn_term.astype(jnp.bfloat16), "tp", scatter_dimension=1, tiled=True
        ).astype(jnp.float32)
    square_total = lax.psum(jnp.sum(residual * residual, axis=1), "tp")
    moe_in = (residual * lax.rsqrt(square_total / D + epsilon)[:, None] * moe_gain[None, :]).astype(
        jnp.bfloat16
    )
    if dense:
        moe_term, qkv_flat = dense_experts(
            moe_in, expert_ids, route_weights, gate_up_flat, down_full, qkv_flat, here, experts_all
        )
    else:
        moe_term = dispatch_experts(
            moe_in, expert_ids, route_weights, expert_gate_up, expert_down, experts_all, capacity
        )
    routed = residual + moe_term
    layer_out = routed.astype(jnp.bfloat16)
    scaled = (routed * next_gain[None, :]).astype(jnp.bfloat16)
    weight_rows = qkv_flat
    if dense:
        mixed = permute_gather_dot(scaled, weight_rows)
    else:
        mixed = jnp.dot(
            lax.all_gather(scaled, "tp", axis=1, tiled=True),
            weight_rows,
            preferred_element_type=jnp.float32,
        )
    mixed = mixed.reshape(NEW, 3, local_width)
    squares_routed = jnp.sum(routed * routed, axis=1)
    routed_total, query_raw, key_raw = lax.psum(
        (
            squares_routed,
            jnp.sum(mixed[:, 0] * mixed[:, 0], axis=1),
            jnp.sum(mixed[:, 1] * mixed[:, 1], axis=1),
        ),
        "tp",
    )
    x_scale = lax.rsqrt(routed_total / D + epsilon)
    query_pre = mixed[:, 0] * x_scale[:, None]
    key_pre = mixed[:, 1] * x_scale[:, None]
    query_total = query_raw * x_scale * x_scale
    key_total = key_raw * x_scale * x_scale
    next_query = (
        query_pre * lax.rsqrt(query_total / D + epsilon)[:, None] * query_gain[None, :]
    ).astype(jnp.bfloat16)
    next_key = (key_pre * lax.rsqrt(key_total / D + epsilon)[:, None] * key_gain[None, :]).astype(
        jnp.bfloat16
    )
    next_value = (mixed[:, 2] * x_scale[:, None]).astype(jnp.bfloat16)
    return (layer_out, next_query, next_key, next_value)


def solution(mesh):
    return jax.shard_map(
        body,
        mesh=mesh,
        in_specs=(
            P("seq", "tp"),
            P("seq", "tp"),
            P("seq", "tp"),
            P("seq", "tp"),
            P("seq", None, "tp"),
            P("seq", None, "tp"),
            P(),
            P("tp", None),
            P("tp"),
            P("seq", None),
            P("seq", None),
            P("seq", None, None, "tp"),
            P("seq", "tp", None),
            P("tp"),
            P(None, None, "tp"),
            P("tp"),
            P("tp"),
        ),
        out_specs=(P("seq", "tp"), P("seq", "tp"), P("seq", "tp"), P("seq", "tp")),
        check_vma=False,
    )
```
